256 devices in a mesh: dp: 8 (over x, core), ctx: 32 (over y, z).
Axes of the slice: x: 4, y: 4, z: 8, core: 2. Of those that a mesh axis runs over, the one named last changes fastest.
Arguments:
- tokens: bfloat16 [8, 8192, 1024], P('dp', 'ctx'), may hold values from -6 to 6
- log_decay: float32 [8, 8, 8192], P('dp', None, 'ctx'), may hold values from -2.2 to 0
- lengths: int32 [8, 2], P('dp'), may hold values from 1 to 5120, 8192 in all within a row
- label_ids: int32 [8, 8192], P('dp', 'ctx'), may hold values from 0 to 511
- w_query: bfloat16 [1024, 1024], replicated, may hold values from -0.1875 to 0.1875
- w_key: bfloat16 [1024, 1024], replicated, may hold values from -0.1875 to 0.1875
- w_value: bfloat16 [1024, 1024], replicated, may hold values from -0.1875 to 0.1875
- norm_gain: float32 [1024], replicated, may hold values from 0.1 to 1.9
- label_query: bfloat16 [512, 1024], replicated, may hold values from -24 to 24
- label_weight: bfloat16 [512, 1024], replicated, may hold values from -0.75 to 0.75
Outputs:
- retention_out: bfloat16 [8, 8192, 1024], P('dp', 'ctx')
- logits: float32 [8, 2, 512], P('dp')
- recording_loss: float32 [8, 2], P('dp')
- mean_loss: float32 [], replicated
The draws below stay inside these ranges and needn't reach their ends.
Inputs may be any that keep to these rules, and one draw needn't show every extreme that they name: Row g lists the lengths of the 2 recordings packed in order into the 8192 tokens of group g; they sum to 8192.
All inputs are finite; a program needn't handle non-finite values.
Results may differ from the reference program's by a relative error of at most 0.0058.
The reference program's roundings to bfloat16 on the way count: a program that leaves them out, or rounds other values in their place, can miss the bound.
Values sent between devices are 32-bit elements; how exact they have to be, the bound alone decides.
No kernel may reach another device: no remote copies, remote signals or barrier semaphores. Data moves between devices by JAX's collectives and lax.ppermute only.
A program may use at most 128 MiB of HBM per device.

```python
import math
import jax
import jax.numpy as jnp
import numpy as np
from jax import lax

D = 1024
H = 8
DH = 128
LABELS = 512
RECS = 2
TOK = 256
PACKED_GROUPS = 8
GROUP_TOKENS = 8192


def alignment_plan(key):
    pick_key = jax.random.fold_in(key, 701)
    sign_key = jax.random.fold_in(key, 702)
    label_key = jax.random.fold_in(key, 703)
    spot_rows = jax.random.randint(pick_key, (4,), 0, PACKED_GROUPS * GROUP_TOKENS - 1)
    sign_rows = (jax.random.randint(sign_key, (4, D), 0, 2) * 2 - 1).astype(jnp.float32)
    chosen = jax.random.permutation(label_key, LABELS)[:4]
    target_score = jnp.array([120.0, 160.0, 200.0, 250.0], jnp.float32)
    return (spot_rows, sign_rows, chosen, target_score)


def draw_tokens(key, part):
    base_key = jax.random.fold_in(key, 11)
    values = jnp.clip(jax.random.normal(base_key, (PACKED_GROUPS, GROUP_TOKENS, D), jnp.float32), -6.0, 6.0)
    spot_rows, sign_rows, chosen, target_score = alignment_plan(key)
    second_level = (4.0 - 8.0 / target_score)[:, None]
    flat_rows = values.reshape(PACKED_GROUPS * GROUP_TOKENS, D)
    flat_rows = flat_rows.at[spot_rows].set(4.0 * sign_rows)
    flat_rows = flat_rows.at[spot_rows + 1].set(second_level * sign_rows)
    values = flat_rows.reshape(PACKED_GROUPS, GROUP_TOKENS, D)
    return values.astype(jnp.bfloat16)


def draw_label_query(key, part):
    base_key = jax.random.fold_in(key, 21)
    values = jnp.clip(jax.random.normal(base_key, (LABELS, D), jnp.float32), -4.0, 4.0)
    spot_rows, sign_rows, chosen, target_score = alignment_plan(key)
    strength = target_score / (4.0 * jnp.sqrt(jnp.float32(DH)))
    values = values.at[chosen].set(strength[:, None] * sign_rows)
    return values.astype(jnp.bfloat16)


def draw_log_decay(key, part):
    power_key = jax.random.fold_in(key, 31)
    device_key = jax.random.fold_in(key, 32)
    token_key = jax.random.fold_in(key, 33)
    position_seed_key = jax.random.fold_in(key, 34)
    length_seed_key = jax.random.fold_in(key, 35)
    low_power = 5.3
    exponent = jax.random.uniform(power_key, (PACKED_GROUPS, H, 1, 1), jnp.float32, low_power, 13.0)
    rate_base = jnp.exp2(-exponent)
    device_factor = jnp.exp(jax.random.uniform(device_key, (PACKED_GROUPS, H, GROUP_TOKENS // TOK, 1), jnp.float32, jnp.log(0.6), jnp.log(1.5)))
    token_factor = jax.random.uniform(token_key, (PACKED_GROUPS, H, GROUP_TOKENS // TOK, TOK), jnp.float32, 0.5, 1.5)
    heart_rates = jnp.maximum(rate_base * device_factor * token_factor, 2.0 ** (-13))
    heart_rates = heart_rates.reshape(PACKED_GROUPS, H, GROUP_TOKENS)
    spike_position = jax.random.randint(position_seed_key, (PACKED_GROUPS, 3), 0, GROUP_TOKENS)
    spike_length = jax.random.uniform(length_seed_key, (PACKED_GROUPS, 3), jnp.float32, 0.2, 0.5)
    placed_value = jnp.arange(GROUP_TOKENS)[None, None, :] == spike_position[:, :, None]
    spike_addition = jnp.sum(jnp.where(placed_value, jnp.log1p(-spike_length)[:, :, None], 0.0), axis=1)
    return -heart_rates + spike_addition[:, None, :]


def set_ends(drawn, own_key, least, high):
    dims = drawn.shape
    spot = [jax.random.randint(jax.random.fold_in(own_key, axis), (), 0, dims[axis]) for axis in range(len(dims))]
    drawn = drawn.at[tuple(spot)].set(least)
    longest = dims.index(max(dims))
    spot[longest] = (spot[longest] + 1) % dims[longest]
    return drawn.at[tuple(spot)].set(high)


def rank_table(amount, skew):
    weights = [(1 << 20) // math.isqrt(grade ** skew) + 1 for grade in range(1, amount + 1)]
    spread = 1 + sum(weights) // (1 << 30)
    return np.cumsum(np.array([max(1, weight // spread) for weight in weights]))


def skewed_ids(stream_key, extent, number_of, slope):
    listing = rank_table(number_of, slope)
    pick = jax.random.randint(jax.random.fold_in(stream_key, 1), extent, 0, int(listing[number_of - 1]))
    standing = jnp.searchsorted(jnp.asarray(listing, jnp.int32), pick, side="right")
    return jax.random.permutation(jax.random.fold_in(stream_key, 2), number_of)[standing].astype(jnp.int32)


def length_profile(amount, total, most, lean):
    loads = [(1 << 20) // math.isqrt(rank ** lean) + 1 for rank in range(2, amount + 1)]
    spare, given = total - most - (amount - 1), [1] * (amount - 1)
    while spare > 0:
        movable = [i for i in range(amount - 1) if given[i] < most]
        pool, left = sum([loads[i] for i in movable]), spare
        for i in movable:
            addition = min(most - given[i], max(1, left * loads[i] // pool), spare)
            given[i] = given[i] + addition
            spare = spare - addition
    return np.array([most] + given)


def ragged(own_key, count, total, limit, slope):
    if count == 2:
        one = jax.random.randint(own_key, (), max(1, total - limit), min(limit, total - 1) + 1)
        return jnp.stack([one, total - one])
    sizes = jnp.asarray(length_profile(count, total, limit, slope), jnp.int32)
    twos = (count - 1) // 2
    source_of, taker = sizes[1:1 + 2 * twos:2], sizes[2:2 + 2 * twos:2]
    margin = jnp.minimum(source_of - 1, limit - taker)
    moved = jax.random.randint(jax.random.fold_in(own_key, 1), (twos,), 0, 1 << 20) % (margin + 1)
    sizes = sizes.at[1:1 + 2 * twos:2].set(source_of - moved).at[2:2 + 2 * twos:2].set(taker + moved)
    return sizes[jax.random.permutation(jax.random.fold_in(own_key, 2), count)]


def scatter_about(key, dims, spread, most, kind=jnp.bfloat16):
    return jnp.clip(spread * jax.random.normal(key, dims, jnp.float32), -most, most).astype(kind)


def setup_inputs(seed: int = 0) -> dict:
    seeds = jax.random.split(jax.random.key(seed), 11)
    tokens = draw_tokens(jax.random.fold_in(seeds[10], 71), 0)
    log_decay = draw_log_decay(jax.random.fold_in(seeds[10], 71), 0)
    lengths = jax.vmap(lambda own: ragged(own, RECS, GROUP_TOKENS, GROUP_TOKENS * 5 // 8, 2))(jax.random.split(seeds[2], PACKED_GROUPS)).reshape((PACKED_GROUPS, RECS)).astype(jnp.int32)
    label_ids = set_ends(skewed_ids(seeds[3], (PACKED_GROUPS, GROUP_TOKENS), LABELS, 2), jax.random.fold_in(seeds[3], 3), 0, LABELS - 1).astype(jnp.int32)
    w_query = scatter_about(seeds[4], (D, D), D ** -0.5, 0.1875)
    w_key = scatter_about(seeds[5], (D, D), D ** -0.5, 0.1875)
    w_value = scatter_about(seeds[6], (D, D), D ** -0.5, 0.1875)
    norm_gain = jnp.clip(1.0 + 0.18 * jax.random.normal(seeds[7], (D,), jnp.float32), 0.1, 1.9)
    label_query = draw_label_query(jax.random.fold_in(seeds[10], 71), 0)
    label_weight = scatter_about(seeds[9], (LABELS, D), (D // 16) ** -0.5, 0.75)
    return {"tokens": tokens, "log_decay": log_decay, "lengths": lengths, "label_ids": label_ids, "w_query": w_query, "w_key": w_key, "w_value": w_value, "norm_gain": norm_gain, "label_query": label_query, "label_weight": label_weight}


NEG_FILL = -1e+30

def record_ids(length_row, positions):
    starts = (jnp.cumsum(length_row) - length_row).astype(jnp.int32)
    return (lax.optimization_barrier(jnp.sum((starts[:, None] <= positions[None, :]).astype(jnp.int32), axis=0)) - 1).astype(jnp.int32)

def retention_block(state_all, block, w_query, w_key, w_value, norm_gain):
    features, decays, record, before_rec = block
    qk_scale = DH ** (-0.5)
    queries = jnp.dot(features, w_query, preferred_element_type=jnp.float32).astype(jnp.bfloat16)
    key_rows = jnp.dot(features, w_key, preferred_element_type=jnp.float32).astype(jnp.bfloat16)
    value_rows = jnp.dot(features, w_value, preferred_element_type=jnp.float32).astype(jnp.bfloat16)
    decay_cum = jnp.cumsum(decays, axis=1)
    local_pos = jnp.arange(TOK, dtype=jnp.int32)
    pair_mask = (local_pos[:, None] >= local_pos[None, :]) & (record[:, None] == record[None, :])
    linked = record == before_rec
    tail_rec = record == record[TOK - 1]

    def one_head(inputs):
        head_idx, state_head = inputs
        q_head = lax.dynamic_slice_in_dim(queries, head_idx * DH, DH, 1)
        k_head = lax.dynamic_slice_in_dim(key_rows, head_idx * DH, DH, 1)
        v_head = lax.dynamic_slice_in_dim(value_rows, head_idx * DH, DH, 1)
        cum_head = lax.dynamic_index_in_dim(decay_cum, head_idx, 0, keepdims=False)
        scores = jnp.dot(q_head, k_head.T, preferred_element_type=jnp.float32) * qk_scale
        decay_pair = jnp.exp(jnp.minimum(cum_head[:, None] - cum_head[None, :], 0.0))
        weights = jnp.where(pair_mask, scores * decay_pair, 0.0).astype(jnp.bfloat16)
        intra_sum = jnp.dot(weights, v_head, preferred_element_type=jnp.float32)
        k_decayed = (k_head.astype(jnp.float32) * jnp.where(tail_rec, jnp.exp(cum_head[TOK - 1] - cum_head), 0.0)[:, None]).astype(jnp.bfloat16)
        local_state = jnp.dot(k_decayed.T, v_head, preferred_element_type=jnp.float32)
        carry_factor = jnp.where(linked[TOK - 1], jnp.exp(cum_head[TOK - 1]), 0.0)
        q_decayed = q_head.astype(jnp.float32) * jnp.where(linked, jnp.exp(cum_head), 0.0)[:, None]
        total_out = intra_sum + jnp.dot(q_decayed, state_head, precision=lax.Precision.HIGH) * qk_scale
        centred = total_out - lax.optimization_barrier(jnp.mean(total_out, axis=1, keepdims=True))
        variance = lax.optimization_barrier(jnp.mean(centred * centred, axis=1, keepdims=True))
        gain_head = lax.dynamic_slice_in_dim(norm_gain, head_idx * DH, DH, 0)
        normed = centred * lax.rsqrt(variance + 1e-05) * gain_head[None, :]
        return (normed, carry_factor * state_head + local_state)
    normed, new_state = lax.map(one_head, (jnp.arange(H, dtype=jnp.int32), state_all))
    out_rows = jnp.transpose(normed, (1, 0, 2)).reshape(TOK, D).astype(jnp.bfloat16)
    return (new_state, out_rows)

def pool_group(features, out_rows, record, label_query, label_weight):
    qk_scale = DH ** (-0.5)

    def one_head(head_idx):
        k_head = lax.dynamic_slice_in_dim(features, head_idx * DH, DH, 1)
        q_label = lax.dynamic_slice_in_dim(label_query, head_idx * DH, DH, 1)
        y_head = lax.dynamic_slice_in_dim(out_rows, head_idx * DH, DH, 1)
        w_head = lax.dynamic_slice_in_dim(label_weight, head_idx * DH, DH, 1)
        scores = jnp.dot(q_label, k_head.T, preferred_element_type=jnp.float32) * qk_scale

        def record_max(rec_idx):
            return lax.optimization_barrier(jnp.max(jnp.where(record[None, :] == rec_idx, scores, NEG_FILL), axis=1))
        maxima = lax.map(record_max, jnp.arange(RECS, dtype=jnp.int32))
        pool_weight = jnp.exp(scores - maxima[record].T)
        label_value = jnp.dot(w_head, y_head.T, preferred_element_type=jnp.float32)
        mass_part = jax.ops.segment_sum(pool_weight.T, record, num_segments=RECS)
        weighted = jax.ops.segment_sum((pool_weight * label_value).T, record, num_segments=RECS)
        return weighted / mass_part
    return lax.optimization_barrier(jnp.sum(lax.map(one_head, jnp.arange(H, dtype=jnp.int32)), axis=0))

def reference(tokens, log_decay, lengths, label_ids, w_query, w_key, w_value, norm_gain, label_query, label_weight):
    blocks = GROUP_TOKENS // TOK
    positions = jnp.arange(GROUP_TOKENS, dtype=jnp.int32)
    out_list = []
    logit_list = []
    loss_list = []
    for group in range(PACKED_GROUPS):
        record = record_ids(lengths[group], positions)
        before_rec = jnp.concatenate([jnp.full((1,), -1, jnp.int32), record[TOK - 1::TOK][:blocks - 1].astype(jnp.int32)]).astype(jnp.int32)
        block_inputs = (tokens[group].reshape(blocks, TOK, D), jnp.transpose(log_decay[group].reshape(H, blocks, TOK), (1, 0, 2)), record.reshape(blocks, TOK), before_rec)

        def step_fn(state_all, block):
            return retention_block(state_all, block, w_query, w_key, w_value, norm_gain)
        final_state, out_blocks = lax.scan(step_fn, jnp.zeros((H, DH, DH), jnp.float32), block_inputs)
        out_rows = out_blocks.reshape(GROUP_TOKENS, D)
        logits = pool_group(tokens[group], out_rows, record, label_query, label_weight)
        counts = jnp.zeros((RECS, LABELS), jnp.float32).at[record, label_ids[group]].add(1.0)
        target = (counts + 0.5) / (lengths[group].astype(jnp.float32)[:, None] + 1.0)
        rec_loss = lax.optimization_barrier(jnp.mean(jax.nn.softplus(logits) - target * logits, axis=1))
        out_list.append(out_rows)
        logit_list.append(logits)
        loss_list.append(rec_loss)
    loss_all = jnp.stack(loss_list)
    mean_loss = jnp.sum(loss_all) / (PACKED_GROUPS * RECS)
    return (jnp.stack(out_list), jnp.stack(logit_list), loss_all, mean_loss)
```

```python
import jax
import jax.numpy as jnp
from jax import lax
from jax.sharding import PartitionSpec as P

NEG_FILL = -1e30


def shifted(x, axis, by):
    count = lax.axis_size(axis)
    pairs = [(i, i + by) for i in range(count) if 0 <= i + by < count]
    return lax.ppermute(x, axis, pairs)


def swapped(x, axis, bit):
    count = lax.axis_size(axis)
    return lax.ppermute(x, axis, [(i, i ^ bit) for i in range(count)])


def butterfly_bits(axis):
    count = lax.axis_size(axis)
    assert count & (count - 1) == 0
    bits = []
    bit = 1
    while bit < count:
        bits.append(bit)
        bit *= 2
    return bits


def record_ids(length_row, positions):
    starts = jnp.cumsum(length_row) - length_row
    return jnp.sum((starts[:, None] <= positions[None, :]).astype(jnp.int32), axis=0) - 1


def exclusive_state_scan(local_state, carry, axis):
    head_count, head_dim, _ = local_state.shape
    count = lax.axis_size(axis)

    def pack(state, factor):
        rows = jnp.broadcast_to(factor[:, None, None], (head_count, 8, head_dim))
        return jnp.concatenate([state, rows], axis=1)

    state, factor = local_state, carry
    span = 1
    while 2 * span < count:
        got = shifted(pack(state, factor), axis, span)
        state = state + factor[:, None, None] * got[:, :head_dim, :]
        factor = factor * got[:, head_dim, 0]
        span *= 2
    near = shifted(pack(state, factor), axis, 1)
    far = shifted(state, axis, span + 1)
    near_state = near[:, :head_dim, :]
    near_factor = near[:, head_dim, 0]
    return near_state + near_factor[:, None, None] * far


def local(
    tokens,
    log_decay,
    lengths,
    label_ids,
    w_query,
    w_key,
    w_value,
    norm_gain,
    label_query,
    label_weight,
):
    tok_rows = tokens.shape[1]
    model_width = tokens.shape[2]
    head_count = log_decay.shape[1]
    head_dim = model_width // head_count
    qk_scale = head_dim ** (-0.5)
    record_count = lengths.shape[1]
    label_count = label_query.shape[0]
    shard_start = lax.axis_index("ctx") * tok_rows
    local_pos = jnp.arange(tok_rows, dtype=jnp.int32)
    record = record_ids(lengths[0], shard_start + local_pos)
    before_rec = record_ids(lengths[0], jnp.reshape(shard_start - 1, (1,)))[0]
    features = tokens[0]
    queries = jnp.dot(features, w_query, preferred_element_type=jnp.float32).astype(jnp.bfloat16)
    key_rows = jnp.dot(features, w_key, preferred_element_type=jnp.float32).astype(jnp.bfloat16)
    value_rows = jnp.dot(features, w_value, preferred_element_type=jnp.float32).astype(jnp.bfloat16)
    q3 = queries.reshape(tok_rows, head_count, head_dim)
    k3 = key_rows.reshape(tok_rows, head_count, head_dim)
    v3 = value_rows.reshape(tok_rows, head_count, head_dim)
    decay_cum = jnp.cumsum(log_decay[0], axis=1)
    pair_mask = (local_pos[:, None] >= local_pos[None, :]) & (record[:, None] == record[None, :])
    linked = record == before_rec
    tail_rec = record == record[tok_rows - 1]

    last_cum = decay_cum[:, tok_rows - 1]
    k_factor = jnp.where(tail_rec[None, :], jnp.exp(last_cum[:, None] - decay_cum), 0.0)
    k_decayed = (k3.astype(jnp.float32) * k_factor.T[:, :, None]).astype(jnp.bfloat16)
    local_state = jnp.einsum("thd,the->hde", k_decayed, v3, preferred_element_type=jnp.float32)
    carry = jnp.where(linked[tok_rows - 1], jnp.exp(last_cum), 0.0)
    incoming = exclusive_state_scan(local_state, carry, "ctx")

    scores = jnp.einsum("thd,shd->hts", q3, k3, preferred_element_type=jnp.float32) * qk_scale
    decay_pair = jnp.exp(jnp.minimum(decay_cum[:, :, None] - decay_cum[:, None, :], 0.0))
    weights = jnp.where(pair_mask[None], scores * decay_pair, 0.0).astype(jnp.bfloat16)
    intra = jnp.einsum("hts,shd->thd", weights, v3, preferred_element_type=jnp.float32)

    member = record[None, :] == jnp.arange(record_count, dtype=jnp.int32)[:, None]
    kf3 = features.reshape(tok_rows, head_count, head_dim)
    lq3 = label_query.reshape(label_count, head_count, head_dim)
    lw3 = label_weight.reshape(label_count, head_count, head_dim)
    pscore = jnp.einsum("lhd,thd->hlt", lq3, kf3, preferred_element_type=jnp.float32) * qk_scale
    maxima = jnp.max(
        jnp.where(member[None, :, None, :], pscore[:, None, :, :], NEG_FILL), axis=3
    )
    maxima_tok = jnp.sum(
        jnp.where(member[None, :, None, :], maxima[:, :, :, None], 0.0), axis=1
    )
    pool_weight = jnp.exp(pscore - maxima_tok)
    mass = jnp.sum(jnp.where(member[None, :, None, :], pool_weight[:, None], 0.0), axis=3)
    label_hot = (label_ids[0][:, None] == jnp.arange(label_count, dtype=jnp.int32)[None, :]).astype(
        jnp.bfloat16
    )
    counts = jnp.dot(member.astype(jnp.bfloat16), label_hot, preferred_element_type=jnp.float32)

    top, total_mass, total_counts = maxima, mass, counts
    for bit in butterfly_bits("ctx"):
        packed = jnp.concatenate([top, total_mass, total_counts[None]], axis=0)
        other = swapped(packed, "ctx", bit)
        o_top = other[:head_count]
        o_mass = other[head_count:2 * head_count]
        o_counts = other[2 * head_count]
        new_top = jnp.maximum(top, o_top)
        total_mass = total_mass * jnp.exp(top - new_top) + o_mass * jnp.exp(o_top - new_top)
        total_counts = total_counts + o_counts
        top = new_top
    rescale = jnp.exp(maxima - top) / total_mass

    q_decayed = q3.astype(jnp.float32) * jnp.where(linked[None, :], jnp.exp(decay_cum), 0.0).T[:, :, None]
    inter = jnp.einsum(
        "thd,hde->the", q_decayed, incoming, precision=lax.Precision.HIGH,
        preferred_element_type=jnp.float32,
    )
    total_out = intra + inter * qk_scale
    centred = total_out - jnp.mean(total_out, axis=2, keepdims=True)
    variance = jnp.mean(centred * centred, axis=2, keepdims=True)
    gain3 = norm_gain.reshape(head_count, head_dim)
    normed = centred * lax.rsqrt(variance + 1e-05) * gain3[None]
    out_rows = normed.reshape(tok_rows, model_width).astype(jnp.bfloat16)

    y3 = out_rows.reshape(tok_rows, head_count, head_dim)
    label_value = jnp.einsum("lhd,thd->hlt", lw3, y3, preferred_element_type=jnp.float32)
    weighted = jnp.sum(
        jnp.where(member[None, :, None, :], (pool_weight * label_value)[:, None], 0.0), axis=3
    )
    part = jnp.sum(weighted * rescale, axis=0)
    for bit in butterfly_bits("ctx"):
        part = part + swapped(part, "ctx", bit)
    logits = part
    target = (total_counts + 0.5) / (lengths[0].astype(jnp.float32)[:, None] + 1.0)
    rec_loss = jnp.mean(jax.nn.softplus(logits) - target * logits, axis=1)
    mean_loss = lax.psum(jnp.sum(rec_loss), "dp") / (lax.axis_size("dp") * record_count)
    return (out_rows[None], logits[None], rec_loss[None], mean_loss)


def solution(mesh):
    return jax.shard_map(
        local,
        mesh=mesh,
        in_specs=(
            P("dp", "ctx", None),
            P("dp", None, "ctx"),
            P("dp", None),
            P("dp", "ctx"),
            P(),
            P(),
            P(),
            P(),
            P(),
            P(),
        ),
        out_specs=(P("dp", "ctx", None), P("dp", None, None), P("dp", None), P()),
        check_vma=False,
    )
```

```python
import jax
import jax.numpy as jnp
from jax import lax
from jax.sharding import PartitionSpec as P

NEG_FILL = -1e30


def shifted(x, axis, by):
    count = lax.axis_size(axis)
    pairs = [(i, i + by) for i in range(count) if 0 <= i + by < count]
    return lax.ppermute(x, axis, pairs)


def swapped(x, axis, bit):
    count = lax.axis_size(axis)
    return lax.ppermute(x, axis, [(i, i ^ bit) for i in range(count)])


def butterfly_bits(axis):
    count = lax.axis_size(axis)
    assert count & (count - 1) == 0
    bits = []
    bit = 1
    while bit < count:
        bits.append(bit)
        bit *= 2
    return bits


def record_ids(length_row, positions):
    starts = jnp.cumsum(length_row) - length_row
    return jnp.sum((starts[:, None] <= positions[None, :]).astype(jnp.int32), axis=0) - 1


def exclusive_state_scan(local_state, carry, axis):
    head_count, head_dim, _ = local_state.shape
    count = lax.axis_size(axis)
    rows = head_count * head_dim // count
    assert rows * count == head_count * head_dim and head_dim % rows == 0
    owner_head = (jnp.arange(count) * rows) // head_dim
    slices = local_state.reshape(count, rows, head_dim)
    factor_rows = jnp.broadcast_to(carry[owner_head][:, None, None], (count, 8, head_dim))
    sent = jnp.concatenate([slices, factor_rows], axis=1)
    got = lax.all_to_all(sent, axis, 0, 0)
    factors = got[:, rows, 0]
    block = jnp.arange(count)
    inside = (block[None, None, :] > block[None, :, None]) & (block[None, None, :] < block[:, None, None])
    spans = jnp.prod(jnp.where(inside, factors[None, None, :], 1.0), axis=2)
    mix = jnp.where(block[None, :] < block[:, None], spans, 0.0)
    scanned = jnp.dot(
        mix, got[:, :rows, :].reshape(count, rows * head_dim), precision=lax.Precision.HIGHEST
    )
    back = lax.all_to_all(scanned.reshape(count, rows, head_dim), axis, 0, 0)
    return back.reshape(head_count, head_dim, head_dim)


def local(
    tokens,
    log_decay,
    lengths,
    label_ids,
    w_query,
    w_key,
    w_value,
    norm_gain,
    label_query,
    label_weight,
):
    tok_rows = tokens.shape[1]
    model_width = tokens.shape[2]
    head_count = log_decay.shape[1]
    head_dim = model_width // head_count
    qk_scale = head_dim ** (-0.5)
    record_count = lengths.shape[1]
    label_count = label_query.shape[0]
    shard_start = lax.axis_index("ctx") * tok_rows
    local_pos = jnp.arange(tok_rows, dtype=jnp.int32)
    record = record_ids(lengths[0], shard_start + local_pos)
    before_rec = record_ids(lengths[0], jnp.reshape(shard_start - 1, (1,)))[0]
    features = tokens[0]
    queries = jnp.dot(features, w_query, preferred_element_type=jnp.float32).astype(jnp.bfloat16)
    key_rows = jnp.dot(features, w_key, preferred_element_type=jnp.float32).astype(jnp.bfloat16)
    value_rows = jnp.dot(features, w_value, preferred_element_type=jnp.float32).astype(jnp.bfloat16)
    q3 = queries.reshape(tok_rows, head_count, head_dim)
    k3 = key_rows.reshape(tok_rows, head_count, head_dim)
    v3 = value_rows.reshape(tok_rows, head_count, head_dim)
    decay_cum = jnp.cumsum(log_decay[0], axis=1)
    pair_mask = (local_pos[:, None] >= local_pos[None, :]) & (record[:, None] == record[None, :])
    linked = record == before_rec
    tail_rec = record == record[tok_rows - 1]

    last_cum = decay_cum[:, tok_rows - 1]
    k_factor = jnp.where(tail_rec[None, :], jnp.exp(last_cum[:, None] - decay_cum), 0.0)
    k_decayed = (k3.astype(jnp.float32) * k_factor.T[:, :, None]).astype(jnp.bfloat16)
    local_state = jnp.einsum("thd,the->hde", k_decayed, v3, preferred_element_type=jnp.float32)
    carry = jnp.where(linked[tok_rows - 1], jnp.exp(last_cum), 0.0)
    incoming = exclusive_state_scan(local_state, carry, "ctx")

    scores = jnp.einsum("thd,shd->hts", q3, k3, preferred_element_type=jnp.float32) * qk_scale
    decay_pair = jnp.exp(jnp.minimum(decay_cum[:, :, None] - decay_cum[:, None, :], 0.0))
    weights = jnp.where(pair_mask[None], scores * decay_pair, 0.0).astype(jnp.bfloat16)
    intra = jnp.einsum("hts,shd->thd", weights, v3, preferred_element_type=jnp.float32)

    member = record[None, :] == jnp.arange(record_count, dtype=jnp.int32)[:, None]
    kf3 = features.reshape(tok_rows, head_count, head_dim)
    lq3 = label_query.reshape(label_count, head_count, head_dim)
    lw3 = label_weight.reshape(label_count, head_count, head_dim)
    pscore = jnp.einsum("lhd,thd->hlt", lq3, kf3, preferred_element_type=jnp.float32) * qk_scale
    maxima = jnp.max(
        jnp.where(member[None, :, None, :], pscore[:, None, :, :], NEG_FILL), axis=3
    )
    maxima_tok = jnp.sum(
        jnp.where(member[None, :, None, :], maxima[:, :, :, None], 0.0), axis=1
    )
    pool_weight = jnp.exp(pscore - maxima_tok)
    mass = jnp.sum(jnp.where(member[None, :, None, :], pool_weight[:, None], 0.0), axis=3)
    label_hot = (label_ids[0][:, None] == jnp.arange(label_count, dtype=jnp.int32)[None, :]).astype(
        jnp.bfloat16
    )
    counts = jnp.dot(member.astype(jnp.bfloat16), label_hot, preferred_element_type=jnp.float32)

    top, total_mass, total_counts = maxima, mass, counts
    for bit in butterfly_bits("ctx"):
        packed = jnp.concatenate([top, total_mass, total_counts[None]], axis=0)
        other = swapped(packed, "ctx", bit)
        o_top = other[:head_count]
        o_mass = other[head_count:2 * head_count]
        o_counts = other[2 * head_count]
        new_top = jnp.maximum(top, o_top)
        total_mass = total_mass * jnp.exp(top - new_top) + o_mass * jnp.exp(o_top - new_top)
        total_counts = total_counts + o_counts
        top = new_top
    rescale = jnp.exp(maxima - top) / total_mass

    q_decayed = q3.astype(jnp.float32) * jnp.where(linked[None, :], jnp.exp(decay_cum), 0.0).T[:, :, None]
    inter = jnp.einsum(
        "thd,hde->the", q_decayed, incoming, precision=lax.Precision.HIGH,
        preferred_element_type=jnp.float32,
    )
    total_out = intra + inter * qk_scale
    centred = total_out - jnp.mean(total_out, axis=2, keepdims=True)
    variance = jnp.mean(centred * centred, axis=2, keepdims=True)
    gain3 = norm_gain.reshape(head_count, head_dim)
    normed = centred * lax.rsqrt(variance + 1e-05) * gain3[None]
    out_rows = normed.reshape(tok_rows, model_width).astype(jnp.bfloat16)

    y3 = out_rows.reshape(tok_rows, head_count, head_dim)
    label_value = jnp.einsum("lhd,thd->hlt", lw3, y3, preferred_element_type=jnp.float32)
    weighted = jnp.sum(
        jnp.where(member[None, :, None, :], (pool_weight * label_value)[:, None], 0.0), axis=3
    )
    part = jnp.sum(weighted * rescale, axis=0)
    for bit in butterfly_bits("ctx"):
        part = part + swapped(part, "ctx", bit)
    logits = part
    target = (total_counts + 0.5) / (lengths[0].astype(jnp.float32)[:, None] + 1.0)
    rec_loss = jnp.mean(jax.nn.softplus(logits) - target * logits, axis=1)
    mean_loss = lax.psum(jnp.sum(rec_loss), "dp") / (lax.axis_size("dp") * record_count)
    return (out_rows[None], logits[None], rec_loss[None], mean_loss)


def solution(mesh):
    return jax.shard_map(
        local,
        mesh=mesh,
        in_specs=(
            P("dp", "ctx", None),
            P("dp", None, "ctx"),
            P("dp", None),
            P("dp", "ctx"),
            P(),
            P(),
            P(),
            P(),
            P(),
            P(),
        ),
        out_specs=(P("dp", "ctx", None), P("dp", None, None), P("dp", None), P()),
        check_vma=False,
    )
```

```python
import jax
import jax.numpy as jnp
from jax import lax
from jax.sharding import PartitionSpec as P

NEG_FILL = -1e30


def shifted(x, axis, by):
    count = lax.axis_size(axis)
    pairs = [(i, i + by) for i in range(count) if 0 <= i + by < count]
    return lax.ppermute(x, axis, pairs)


def swapped(x, axis, bit):
    count = lax.axis_size(axis)
    return lax.ppermute(x, axis, [(i, i ^ bit) for i in range(count)])


def butterfly_bits(axis):
    count = lax.axis_size(axis)
    assert count & (count - 1) == 0
    bits = []
    bit = 1
    while bit < count:
        bits.append(bit)
        bit *= 2
    return bits


def record_ids(length_row, positions):
    starts = jnp.cumsum(length_row) - length_row
    return jnp.sum((starts[:, None] <= positions[None, :]).astype(jnp.int32), axis=0) - 1


def exclusive_state_scan(local_state, carry, stats, axis):
    head_count, head_dim, _ = local_state.shape
    count = lax.axis_size(axis)
    rows = head_count * head_dim // count
    assert rows * count == head_count * head_dim and head_dim % rows == 0
    pair_count, fields = stats.shape
    per_owner = pair_count // count
    assert per_owner * count == pair_count and per_owner * fields < 8 * head_dim
    pad = 8 * head_dim - per_owner * fields - 1
    owner_head = (jnp.arange(count) * rows) // head_dim
    slices = local_state.reshape(count, rows, head_dim)
    extra = jnp.concatenate(
        [
            stats.reshape(count, per_owner * fields),
            carry[owner_head][:, None],
            jnp.zeros((count, pad), jnp.float32),
        ],
        axis=1,
    ).reshape(count, 8, head_dim)
    got = lax.all_to_all(jnp.concatenate([slices, extra], axis=1), axis, 0, 0)
    got_extra = got[:, rows:, :].reshape(count, 8 * head_dim)
    factors = got_extra[:, per_owner * fields]
    part = got_extra[:, : per_owner * fields].reshape(count, per_owner, fields)
    part_top = part[:, :, :head_count]
    top = jnp.max(part_top, axis=0)
    mass = jnp.sum(part[:, :, head_count:2 * head_count] * jnp.exp(part_top - top[None]), axis=0)
    tally = jnp.sum(part[:, :, 2 * head_count:], axis=0)
    combined = jnp.concatenate([top, mass, tally], axis=1).reshape(1, per_owner * fields)
    block = jnp.arange(count)
    inside = (block[None, None, :] > block[None, :, None]) & (block[None, None, :] < block[:, None, None])
    spans = jnp.prod(jnp.where(inside, factors[None, None, :], 1.0), axis=2)
    mix = jnp.where(block[None, :] < block[:, None], spans, 0.0)
    scanned = jnp.dot(
        mix, got[:, :rows, :].reshape(count, rows * head_dim), precision=lax.Precision.HIGHEST
    )
    back_extra = jnp.broadcast_to(
        jnp.concatenate([combined, jnp.zeros((1, pad + 1), jnp.float32)], axis=1),
        (count, 8 * head_dim),
    ).reshape(count, 8, head_dim)
    sent_back = jnp.concatenate([scanned.reshape(count, rows, head_dim), back_extra], axis=1)
    back = lax.all_to_all(sent_back, axis, 0, 0)
    state = back[:, :rows, :].reshape(head_count, head_dim, head_dim)
    totals = back[:, rows:, :].reshape(count, 8 * head_dim)[:, : per_owner * fields]
    return state, totals.reshape(pair_count, fields)


def local(
    tokens,
    log_decay,
    lengths,
    label_ids,
    w_query,
    w_key,
    w_value,
    norm_gain,
    label_query,
    label_weight,
):
    tok_rows = tokens.shape[1]
    model_width = tokens.shape[2]
    head_count = log_decay.shape[1]
    head_dim = model_width // head_count
    qk_scale = head_dim ** (-0.5)
    record_count = lengths.shape[1]
    label_count = label_query.shape[0]
    shard_start = lax.axis_index("ctx") * tok_rows
    local_pos = jnp.arange(tok_rows, dtype=jnp.int32)
    record = record_ids(lengths[0], shard_start + local_pos)
    before_rec = record_ids(lengths[0], jnp.reshape(shard_start - 1, (1,)))[0]
    features = tokens[0]
    queries = jnp.dot(features, w_query, preferred_element_type=jnp.float32).astype(jnp.bfloat16)
    key_rows = jnp.dot(features, w_key, preferred_element_type=jnp.float32).astype(jnp.bfloat16)
    value_rows = jnp.dot(features, w_value, preferred_element_type=jnp.float32).astype(jnp.bfloat16)
    q3 = queries.reshape(tok_rows, head_count, head_dim)
    k3 = key_rows.reshape(tok_rows, head_count, head_dim)
    v3 = value_rows.reshape(tok_rows, head_count, head_dim)
    decay_cum = jnp.cumsum(log_decay[0], axis=1)
    pair_mask = (local_pos[:, None] >= local_pos[None, :]) & (record[:, None] == record[None, :])
    linked = record == before_rec
    tail_rec = record == record[tok_rows - 1]

    last_cum = decay_cum[:, tok_rows - 1]
    k_factor = jnp.where(tail_rec[None, :], jnp.exp(last_cum[:, None] - decay_cum), 0.0)
    k_decayed = (k3.astype(jnp.float32) * k_factor.T[:, :, None]).astype(jnp.bfloat16)
    local_state = jnp.einsum("thd,the->hde", k_decayed, v3, preferred_element_type=jnp.float32)
    carry = jnp.where(linked[tok_rows - 1], jnp.exp(last_cum), 0.0)

    scores = jnp.einsum("thd,shd->hts", q3, k3, preferred_element_type=jnp.float32) * qk_scale
    decay_pair = jnp.exp(jnp.minimum(decay_cum[:, :, None] - decay_cum[:, None, :], 0.0))
    weights = jnp.where(pair_mask[None], scores * decay_pair, 0.0).astype(jnp.bfloat16)
    intra = jnp.einsum("hts,shd->thd", weights, v3, preferred_element_type=jnp.float32)

    member = record[None, :] == jnp.arange(record_count, dtype=jnp.int32)[:, None]
    kf3 = features.reshape(tok_rows, head_count, head_dim)
    lq3 = label_query.reshape(label_count, head_count, head_dim)
    lw3 = label_weight.reshape(label_count, head_count, head_dim)
    pscore = jnp.einsum("lhd,thd->hlt", lq3, kf3, preferred_element_type=jnp.float32) * qk_scale
    maxima = jnp.max(
        jnp.where(member[None, :, None, :], pscore[:, None, :, :], NEG_FILL), axis=3
    )
    maxima_tok = jnp.sum(
        jnp.where(member[None, :, None, :], maxima[:, :, :, None], 0.0), axis=1
    )
    pool_weight = jnp.exp(pscore - maxima_tok)
    mass = jnp.sum(jnp.where(member[None, :, None, :], pool_weight[:, None], 0.0), axis=3)
    label_hot = (label_ids[0][:, None] == jnp.arange(label_count, dtype=jnp.int32)[None, :]).astype(
        jnp.bfloat16
    )
    counts = jnp.dot(member.astype(jnp.bfloat16), label_hot, preferred_element_type=jnp.float32)

    stats = jnp.concatenate(
        [
            jnp.transpose(maxima, (1, 2, 0)),
            jnp.transpose(mass, (1, 2, 0)),
            counts[:, :, None],
        ],
        axis=2,
    ).reshape(record_count * label_count, 2 * head_count + 1)
    incoming, totals = exclusive_state_scan(local_state, carry, stats, "ctx")
    totals = totals.reshape(record_count, label_count, 2 * head_count + 1)
    top = jnp.transpose(totals[:, :, :head_count], (2, 0, 1))
    total_mass = jnp.transpose(totals[:, :, head_count:2 * head_count], (2, 0, 1))
    total_counts = totals[:, :, 2 * head_count]
    rescale = jnp.exp(maxima - top) / total_mass

    q_decayed = q3.astype(jnp.float32) * jnp.where(linked[None, :], jnp.exp(decay_cum), 0.0).T[:, :, None]
    inter = jnp.einsum(
        "thd,hde->the", q_decayed, incoming, precision=lax.Precision.HIGH,
        preferred_element_type=jnp.float32,
    )
    total_out = intra + inter * qk_scale
    centred = total_out - jnp.mean(total_out, axis=2, keepdims=True)
    variance = jnp.mean(centred * centred, axis=2, keepdims=True)
    gain3 = norm_gain.reshape(head_count, head_dim)
    normed = centred * lax.rsqrt(variance + 1e-05) * gain3[None]
    out_rows = normed.reshape(tok_rows, model_width).astype(jnp.bfloat16)

    y3 = out_rows.reshape(tok_rows, head_count, head_dim)
    label_value = jnp.einsum("lhd,thd->hlt", lw3, y3, preferred_element_type=jnp.float32)
    weighted = jnp.sum(
        jnp.where(member[None, :, None, :], (pool_weight * label_value)[:, None], 0.0), axis=3
    )
    part = jnp.sum(weighted * rescale, axis=0)
    for bit in butterfly_bits("ctx"):
        part = part + swapped(part, "ctx", bit)
    logits = part
    target = (total_counts + 0.5) / (lengths[0].astype(jnp.float32)[:, None] + 1.0)
    rec_loss = jnp.mean(jax.nn.softplus(logits) - target * logits, axis=1)
    mean_loss = lax.psum(jnp.sum(rec_loss), "dp") / (lax.axis_size("dp") * record_count)
    return (out_rows[None], logits[None], rec_loss[None], mean_loss)


def solution(mesh):
    return jax.shard_map(
        local,
        mesh=mesh,
        in_specs=(
            P("dp", "ctx", None),
            P("dp", None, "ctx"),
            P("dp", None),
            P("dp", "ctx"),
            P(),
            P(),
            P(),
            P(),
            P(),
            P(),
        ),
        out_specs=(P("dp", "ctx", None), P("dp", None, None), P("dp", None), P()),
        check_vma=False,
    )
```

```python
import jax
import jax.numpy as jnp
from jax import lax
from jax.sharding import PartitionSpec as P

NEG_FILL = -1e30


def shifted(x, axis, by):
    count = lax.axis_size(axis)
    pairs = [(i, i + by) for i in range(count) if 0 <= i + by < count]
    return lax.ppermute(x, axis, pairs)


def swapped(x, axis, bit):
    count = lax.axis_size(axis)
    return lax.ppermute(x, axis, [(i, i ^ bit) for i in range(count)])


def group_sum(x, axis, stride, size):
    values = [x] + [swapped(x, axis, stride * d) for d in range(1, size)]
    while len(values) > 1:
        values = [values[i] + values[i + 1] for i in range(0, len(values), 2)]
    return values[0]


def butterfly_bits(axis):
    count = lax.axis_size(axis)
    assert count & (count - 1) == 0
    bits = []
    bit = 1
    while bit < count:
        bits.append(bit)
        bit *= 2
    return bits


def record_ids(length_row, positions):
    starts = jnp.cumsum(length_row) - length_row
    return jnp.sum((starts[:, None] <= positions[None, :]).astype(jnp.int32), axis=0) - 1


def exclusive_state_scan(local_state, carry, stats, axis):
    head_count, head_dim, _ = local_state.shape
    count = lax.axis_size(axis)
    rows = head_count * head_dim // count
    assert rows * count == head_count * head_dim and head_dim % rows == 0
    pair_count, fields = stats.shape
    per_owner = pair_count // count
    assert per_owner * count == pair_count and per_owner * fields < 8 * head_dim
    pad = 8 * head_dim - per_owner * fields - 1
    owner_head = (jnp.arange(count) * rows) // head_dim
    slices = local_state.reshape(count, rows, head_dim)
    extra = jnp.concatenate(
        [
            stats.reshape(count, per_owner * fields),
            carry[owner_head][:, None],
            jnp.zeros((count, pad), jnp.float32),
        ],
        axis=1,
    ).reshape(count, 8, head_dim)
    got = lax.all_to_all(jnp.concatenate([slices, extra], axis=1), axis, 0, 0)
    got_extra = got[:, rows:, :].reshape(count, 8 * head_dim)
    factors = got_extra[:, per_owner * fields]
    part = got_extra[:, : per_owner * fields].reshape(count, per_owner, fields)
    part_top = part[:, :, :head_count]
    top = jnp.max(part_top, axis=0)
    mass = jnp.sum(part[:, :, head_count:2 * head_count] * jnp.exp(part_top - top[None]), axis=0)
    tally = jnp.sum(part[:, :, 2 * head_count:], axis=0)
    combined = jnp.concatenate([top, mass, tally], axis=1).reshape(1, per_owner * fields)
    block = jnp.arange(count)
    inside = (block[None, None, :] > block[None, :, None]) & (block[None, None, :] < block[:, None, None])
    spans = jnp.prod(jnp.where(inside, factors[None, None, :], 1.0), axis=2)
    mix = jnp.where(block[None, :] < block[:, None], spans, 0.0)
    scanned = jnp.dot(
        mix, got[:, :rows, :].reshape(count, rows * head_dim), precision=lax.Precision.HIGHEST
    )
    back_extra = jnp.broadcast_to(
        jnp.concatenate([combined, jnp.zeros((1, pad + 1), jnp.float32)], axis=1),
        (count, 8 * head_dim),
    ).reshape(count, 8, head_dim)
    sent_back = jnp.concatenate([scanned.reshape(count, rows, head_dim), back_extra], axis=1)
    back = lax.all_to_all(sent_back, axis, 0, 0)
    state = back[:, :rows, :].reshape(head_count, head_dim, head_dim)
    totals = back[:, rows:, :].reshape(count, 8 * head_dim)[:, : per_owner * fields]
    return state, totals.reshape(pair_count, fields)


def local(
    tokens,
    log_decay,
    lengths,
    label_ids,
    w_query,
    w_key,
    w_value,
    norm_gain,
    label_query,
    label_weight,
):
    tok_rows = tokens.shape[1]
    model_width = tokens.shape[2]
    head_count = log_decay.shape[1]
    head_dim = model_width // head_count
    qk_scale = head_dim ** (-0.5)
    record_count = lengths.shape[1]
    label_count = label_query.shape[0]
    shard_start = lax.axis_index("ctx") * tok_rows
    local_pos = jnp.arange(tok_rows, dtype=jnp.int32)
    record = record_ids(lengths[0], shard_start + local_pos)
    before_rec = record_ids(lengths[0], jnp.reshape(shard_start - 1, (1,)))[0]
    features = tokens[0]
    queries = jnp.dot(features, w_query, preferred_element_type=jnp.float32).astype(jnp.bfloat16)
    key_rows = jnp.dot(features, w_key, preferred_element_type=jnp.float32).astype(jnp.bfloat16)
    value_rows = jnp.dot(features, w_value, preferred_element_type=jnp.float32).astype(jnp.bfloat16)
    q3 = queries.reshape(tok_rows, head_count, head_dim)
    k3 = key_rows.reshape(tok_rows, head_count, head_dim)
    v3 = value_rows.reshape(tok_rows, head_count, head_dim)
    decay_cum = jnp.cumsum(log_decay[0], axis=1)
    pair_mask = (local_pos[:, None] >= local_pos[None, :]) & (record[:, None] == record[None, :])
    linked = record == before_rec
    tail_rec = record == record[tok_rows - 1]

    last_cum = decay_cum[:, tok_rows - 1]
    k_factor = jnp.where(tail_rec[None, :], jnp.exp(last_cum[:, None] - decay_cum), 0.0)
    k_decayed = (k3.astype(jnp.float32) * k_factor.T[:, :, None]).astype(jnp.bfloat16)
    local_state = jnp.einsum("thd,the->hde", k_decayed, v3, preferred_element_type=jnp.float32)
    carry = jnp.where(linked[tok_rows - 1], jnp.exp(last_cum), 0.0)

    scores = jnp.einsum("thd,shd->hts", q3, k3, preferred_element_type=jnp.float32) * qk_scale
    decay_pair = jnp.exp(jnp.minimum(decay_cum[:, :, None] - decay_cum[:, None, :], 0.0))
    weights = jnp.where(pair_mask[None], scores * decay_pair, 0.0).astype(jnp.bfloat16)
    intra = jnp.einsum("hts,shd->thd", weights, v3, preferred_element_type=jnp.float32)

    member = record[None, :] == jnp.arange(record_count, dtype=jnp.int32)[:, None]
    kf3 = features.reshape(tok_rows, head_count, head_dim)
    lq3 = label_query.reshape(label_count, head_count, head_dim)
    lw3 = label_weight.reshape(label_count, head_count, head_dim)
    pscore = jnp.einsum("lhd,thd->hlt", lq3, kf3, preferred_element_type=jnp.float32) * qk_scale
    maxima = jnp.max(
        jnp.where(member[None, :, None, :], pscore[:, None, :, :], NEG_FILL), axis=3
    )
    maxima_tok = jnp.sum(
        jnp.where(member[None, :, None, :], maxima[:, :, :, None], 0.0), axis=1
    )
    pool_weight = jnp.exp(pscore - maxima_tok)
    mass = jnp.sum(jnp.where(member[None, :, None, :], pool_weight[:, None], 0.0), axis=3)
    label_hot = (label_ids[0][:, None] == jnp.arange(label_count, dtype=jnp.int32)[None, :]).astype(
        jnp.bfloat16
    )
    counts = jnp.dot(member.astype(jnp.bfloat16), label_hot, preferred_element_type=jnp.float32)

    stats = jnp.concatenate(
        [
            jnp.transpose(maxima, (1, 2, 0)),
            jnp.transpose(mass, (1, 2, 0)),
            counts[:, :, None],
        ],
        axis=2,
    ).reshape(record_count * label_count, 2 * head_count + 1)
    incoming, totals = exclusive_state_scan(local_state, carry, stats, "ctx")
    totals = totals.reshape(record_count, label_count, 2 * head_count + 1)
    top = jnp.transpose(totals[:, :, :head_count], (2, 0, 1))
    total_mass = jnp.transpose(totals[:, :, head_count:2 * head_count], (2, 0, 1))
    total_counts = totals[:, :, 2 * head_count]
    rescale = jnp.exp(maxima - top) / total_mass

    q_decayed = q3.astype(jnp.float32) * jnp.where(linked[None, :], jnp.exp(decay_cum), 0.0).T[:, :, None]
    inter = jnp.einsum(
        "thd,hde->the", q_decayed, incoming, precision=lax.Precision.HIGH,
        preferred_element_type=jnp.float32,
    )
    total_out = intra + inter * qk_scale
    centred = total_out - jnp.mean(total_out, axis=2, keepdims=True)
    variance = jnp.mean(centred * centred, axis=2, keepdims=True)
    gain3 = norm_gain.reshape(head_count, head_dim)
    normed = centred * lax.rsqrt(variance + 1e-05) * gain3[None]
    out_rows = normed.reshape(tok_rows, model_width).astype(jnp.bfloat16)

    y3 = out_rows.reshape(tok_rows, head_count, head_dim)
    label_value = jnp.einsum("lhd,thd->hlt", lw3, y3, preferred_element_type=jnp.float32)
    weighted = jnp.sum(
        jnp.where(member[None, :, None, :], (pool_weight * label_value)[:, None], 0.0), axis=3
    )
    part = jnp.sum(weighted * rescale, axis=0)
    count = lax.axis_size("ctx")
    inner = min(count, 8)
    assert count % inner == 0 and inner & (inner - 1) == 0
    part = group_sum(part, "ctx", 1, inner)
    if count > inner:
        part = group_sum(part, "ctx", inner, count // inner)
    logits = part
    target = (total_counts + 0.5) / (lengths[0].astype(jnp.float32)[:, None] + 1.0)
    rec_loss = jnp.mean(jax.nn.softplus(logits) - target * logits, axis=1)
    mean_loss = group_sum(jnp.sum(rec_loss), "dp", 1, lax.axis_size("dp")) / (
        lax.axis_size("dp") * record_count
    )
    return (out_rows[None], logits[None], rec_loss[None], mean_loss)


def solution(mesh):
    return jax.shard_map(
        local,
        mesh=mesh,
        in_specs=(
            P("dp", "ctx", None),
            P("dp", None, "ctx"),
            P("dp", None),
            P("dp", "ctx"),
            P(),
            P(),
            P(),
            P(),
            P(),
            P(),
        ),
        out_specs=(P("dp", "ctx", None), P("dp", None, None), P("dp", None), P()),
        check_vma=False,
    )
```

```python
import functools

import jax
import jax.numpy as jnp
from jax import lax
from jax.experimental import pallas as pl
from jax.sharding import PartitionSpec as P

NEG_FILL = -1e30


def shifted(x, axis, by):
    count = lax.axis_size(axis)
    pairs = [(i, i + by) for i in range(count) if 0 <= i + by < count]
    return lax.ppermute(x, axis, pairs)


def swapped(x, axis, bit):
    count = lax.axis_size(axis)
    return lax.ppermute(x, axis, [(i, i ^ bit) for i in range(count)])


def group_sum(x, axis, stride, size):
    values = [x] + [swapped(x, axis, stride * d) for d in range(1, size)]
    while len(values) > 1:
        values = [values[i] + values[i + 1] for i in range(0, len(values), 2)]
    return values[0]


def butterfly_bits(axis):
    count = lax.axis_size(axis)
    assert count & (count - 1) == 0
    bits = []
    bit = 1
    while bit < count:
        bits.append(bit)
        bit *= 2
    return bits


def split_dot(a, b):
    a_hi = a.astype(jnp.bfloat16)
    a_lo = (a - a_hi.astype(jnp.float32)).astype(jnp.bfloat16)
    b_hi = b.astype(jnp.bfloat16)
    b_lo = (b - b_hi.astype(jnp.float32)).astype(jnp.bfloat16)
    out = jnp.dot(a_hi, b_hi, preferred_element_type=jnp.float32)
    out = out + jnp.dot(a_hi, b_lo, preferred_element_type=jnp.float32)
    return out + jnp.dot(a_lo, b_hi, preferred_element_type=jnp.float32)


def finish_kernel(qd_ref, state_ref, intra_ref, gain_ref, lw_ref, pw_ref, member_ref, rescale_ref,
                  out_ref, part_ref, *, qk_scale):
    inter = split_dot(qd_ref[...], state_ref[0])
    total = intra_ref[...] + inter * qk_scale
    centred = total - jnp.mean(total, axis=1, keepdims=True)
    variance = jnp.mean(centred * centred, axis=1, keepdims=True)
    normed = centred * lax.rsqrt(variance + 1e-05) * gain_ref[...]
    y = normed.astype(jnp.bfloat16)
    out_ref[...] = y
    label_value = lax.dot_general(
        lw_ref[...], y, (((1,), (1,)), ((), ())), preferred_element_type=jnp.float32
    )
    prod = pw_ref[0] * label_value
    weighted = lax.dot_general(
        member_ref[...], prod, (((1,), (1,)), ((), ())),
        precision=lax.Precision.HIGHEST, preferred_element_type=jnp.float32,
    )
    part_ref[0] = weighted * rescale_ref[0]


def finish_call(q_decayed, incoming, intra, norm_gain, label_weight, pool_weight, member, rescale,
                qk_scale):
    tok_rows, model_width = q_decayed.shape
    head_count, head_dim, _ = incoming.shape
    label_count = label_weight.shape[0]
    record_count = member.shape[0]
    return pl.pallas_call(
        functools.partial(finish_kernel, qk_scale=qk_scale),
        grid=(head_count,),
        in_specs=[
            pl.BlockSpec((tok_rows, head_dim), lambda h: (0, h)),
            pl.BlockSpec((1, head_dim, head_dim), lambda h: (h, 0, 0)),
            pl.BlockSpec((tok_rows, head_dim), lambda h: (0, h)),
            pl.BlockSpec((1, head_dim), lambda h: (0, h)),
            pl.BlockSpec((label_count, head_dim), lambda h: (0, h)),
            pl.BlockSpec((1, label_count, tok_rows), lambda h: (h, 0, 0)),
            pl.BlockSpec((record_count, tok_rows), lambda h: (0, 0)),
            pl.BlockSpec((1, record_count, label_count), lambda h: (h, 0, 0)),
        ],
        out_specs=[
            pl.BlockSpec((tok_rows, head_dim), lambda h: (0, h)),
            pl.BlockSpec((1, record_count, label_count), lambda h: (h, 0, 0)),
        ],
        out_shape=[
            jax.ShapeDtypeStruct((tok_rows, model_width), jnp.bfloat16),
            jax.ShapeDtypeStruct((head_count, record_count, label_count), jnp.float32),
        ],
    )(q_decayed, incoming, intra, norm_gain.reshape(1, model_width), label_weight, pool_weight,
      member, rescale)


def record_ids(length_row, positions):
    starts = jnp.cumsum(length_row) - length_row
    return jnp.sum((starts[:, None] <= positions[None, :]).astype(jnp.int32), axis=0) - 1


def exclusive_state_scan(local_state, carry, stats, axis):
    head_count, head_dim, _ = local_state.shape
    count = lax.axis_size(axis)
    rows = head_count * head_dim // count
    assert rows * count == head_count * head_dim and head_dim % rows == 0
    pair_count, fields = stats.shape
    per_owner = pair_count // count
    assert per_owner * count == pair_count and per_owner * fields < 8 * head_dim
    pad = 8 * head_dim - per_owner * fields - 1
    owner_head = (jnp.arange(count) * rows) // head_dim
    slices = local_state.reshape(count, rows, head_dim)
    extra = jnp.concatenate(
        [
            stats.reshape(count, per_owner * fields),
            carry[owner_head][:, None],
            jnp.zeros((count, pad), jnp.float32),
        ],
        axis=1,
    ).reshape(count, 8, head_dim)
    got = lax.all_to_all(jnp.concatenate([slices, extra], axis=1), axis, 0, 0)
    got_extra = got[:, rows:, :].reshape(count, 8 * head_dim)
    factors = got_extra[:, per_owner * fields]
    part = got_extra[:, : per_owner * fields].reshape(count, per_owner, fields)
    part_top = part[:, :, :head_count]
    top = jnp.max(part_top, axis=0)
    mass = jnp.sum(part[:, :, head_count:2 * head_count] * jnp.exp(part_top - top[None]), axis=0)
    tally = jnp.sum(part[:, :, 2 * head_count:], axis=0)
    combined = jnp.concatenate([top, mass, tally], axis=1).reshape(1, per_owner * fields)
    block = jnp.arange(count)
    inside = (block[None, None, :] > block[None, :, None]) & (block[None, None, :] < block[:, None, None])
    spans = jnp.prod(jnp.where(inside, factors[None, None, :], 1.0), axis=2)
    mix = jnp.where(block[None, :] < block[:, None], spans, 0.0)
    scanned = jnp.dot(
        mix, got[:, :rows, :].reshape(count, rows * head_dim), precision=lax.Precision.HIGHEST
    )
    back_extra = jnp.broadcast_to(
        jnp.concatenate([combined, jnp.zeros((1, pad + 1), jnp.float32)], axis=1),
        (count, 8 * head_dim),
    ).reshape(count, 8, head_dim)
    sent_back = jnp.concatenate([scanned.reshape(count, rows, head_dim), back_extra], axis=1)
    back = lax.all_to_all(sent_back, axis, 0, 0)
    state = back[:, :rows, :].reshape(head_count, head_dim, head_dim)
    totals = back[:, rows:, :].reshape(count, 8 * head_dim)[:, : per_owner * fields]
    return state, totals.reshape(pair_count, fields)


def local(
    tokens,
    log_decay,
    lengths,
    label_ids,
    w_query,
    w_key,
    w_value,
    norm_gain,
    label_query,
    label_weight,
):
    tok_rows = tokens.shape[1]
    model_width = tokens.shape[2]
    head_count = log_decay.shape[1]
    head_dim = model_width // head_count
    qk_scale = head_dim ** (-0.5)
    record_count = lengths.shape[1]
    label_count = label_query.shape[0]
    shard_start = lax.axis_index("ctx") * tok_rows
    local_pos = jnp.arange(tok_rows, dtype=jnp.int32)
    record = record_ids(lengths[0], shard_start + local_pos)
    before_rec = record_ids(lengths[0], jnp.reshape(shard_start - 1, (1,)))[0]
    features = tokens[0]
    queries = jnp.dot(features, w_query, preferred_element_type=jnp.float32).astype(jnp.bfloat16)
    key_rows = jnp.dot(features, w_key, preferred_element_type=jnp.float32).astype(jnp.bfloat16)
    value_rows = jnp.dot(features, w_value, preferred_element_type=jnp.float32).astype(jnp.bfloat16)
    q3 = queries.reshape(tok_rows, head_count, head_dim)
    k3 = key_rows.reshape(tok_rows, head_count, head_dim)
    v3 = value_rows.reshape(tok_rows, head_count, head_dim)
    decay_cum = jnp.cumsum(log_decay[0], axis=1)
    pair_mask = (local_pos[:, None] >= local_pos[None, :]) & (record[:, None] == record[None, :])
    linked = record == before_rec
    tail_rec = record == record[tok_rows - 1]

    last_cum = decay_cum[:, tok_rows - 1]
    k_factor = jnp.where(tail_rec[None, :], jnp.exp(last_cum[:, None] - decay_cum), 0.0)
    k_decayed = (k3.astype(jnp.float32) * k_factor.T[:, :, None]).astype(jnp.bfloat16)
    local_state = jnp.einsum("thd,the->hde", k_decayed, v3, preferred_element_type=jnp.float32)
    carry = jnp.where(linked[tok_rows - 1], jnp.exp(last_cum), 0.0)

    scores = jnp.einsum("thd,shd->hts", q3, k3, preferred_element_type=jnp.float32) * qk_scale
    decay_pair = jnp.exp(jnp.minimum(decay_cum[:, :, None] - decay_cum[:, None, :], 0.0))
    weights = jnp.where(pair_mask[None], scores * decay_pair, 0.0).astype(jnp.bfloat16)
    intra = jnp.einsum("hts,shd->thd", weights, v3, preferred_element_type=jnp.float32)

    member = record[None, :] == jnp.arange(record_count, dtype=jnp.int32)[:, None]
    kf3 = features.reshape(tok_rows, head_count, head_dim)
    lq3 = label_query.reshape(label_count, head_count, head_dim)
    lw3 = label_weight.reshape(label_count, head_count, head_dim)
    pscore = jnp.einsum("lhd,thd->hlt", lq3, kf3, preferred_element_type=jnp.float32) * qk_scale
    maxima = jnp.max(
        jnp.where(member[None, :, None, :], pscore[:, None, :, :], NEG_FILL), axis=3
    )
    maxima_tok = jnp.sum(
        jnp.where(member[None, :, None, :], maxima[:, :, :, None], 0.0), axis=1
    )
    pool_weight = jnp.exp(pscore - maxima_tok)
    mass = jnp.sum(jnp.where(member[None, :, None, :], pool_weight[:, None], 0.0), axis=3)
    label_hot = (label_ids[0][:, None] == jnp.arange(label_count, dtype=jnp.int32)[None, :]).astype(
        jnp.bfloat16
    )
    counts = jnp.dot(member.astype(jnp.bfloat16), label_hot, preferred_element_type=jnp.float32)

    stats = jnp.concatenate(
        [
            jnp.transpose(maxima, (1, 2, 0)),
            jnp.transpose(mass, (1, 2, 0)),
            counts[:, :, None],
        ],
        axis=2,
    ).reshape(record_count * label_count, 2 * head_count + 1)
    incoming, totals = exclusive_state_scan(local_state, carry, stats, "ctx")
    totals = totals.reshape(record_count, label_count, 2 * head_count + 1)
    top = jnp.transpose(totals[:, :, :head_count], (2, 0, 1))
    total_mass = jnp.transpose(totals[:, :, head_count:2 * head_count], (2, 0, 1))
    total_counts = totals[:, :, 2 * head_count]
    rescale = jnp.exp(maxima - top) / total_mass

    q_decayed = (
        q3.astype(jnp.float32) * jnp.where(linked[None, :], jnp.exp(decay_cum), 0.0).T[:, :, None]
    ).reshape(tok_rows, model_width)
    out_rows, head_parts = finish_call(
        q_decayed, incoming, intra.reshape(tok_rows, model_width), norm_gain, label_weight,
        pool_weight, member.astype(jnp.float32), rescale, qk_scale,
    )
    part = jnp.sum(head_parts, axis=0)
    count = lax.axis_size("ctx")
    inner = min(count, 8)
    assert count % inner == 0 and inner & (inner - 1) == 0
    part = group_sum(part, "ctx", 1, inner)
    if count > inner:
        part = group_sum(part, "ctx", inner, count // inner)
    logits = part
    target = (total_counts + 0.5) / (lengths[0].astype(jnp.float32)[:, None] + 1.0)
    rec_loss = jnp.mean(jax.nn.softplus(logits) - target * logits, axis=1)
    mean_loss = group_sum(jnp.sum(rec_loss), "dp", 1, lax.axis_size("dp")) / (
        lax.axis_size("dp") * record_count
    )
    return (out_rows[None], logits[None], rec_loss[None], mean_loss)


def solution(mesh):
    return jax.shard_map(
        local,
        mesh=mesh,
        in_specs=(
            P("dp", "ctx", None),
            P("dp", None, "ctx"),
            P("dp", None),
            P("dp", "ctx"),
            P(),
            P(),
            P(),
            P(),
            P(),
            P(),
        ),
        out_specs=(P("dp", "ctx", None), P("dp", None, None), P("dp", None), P()),
        check_vma=False,
    )
```

```python
import functools

import jax
import jax.numpy as jnp
from jax import lax
from jax.experimental import pallas as pl
from jax.sharding import PartitionSpec as P

NEG_FILL = -1e30


def shifted(x, axis, by):
    count = lax.axis_size(axis)
    pairs = [(i, i + by) for i in range(count) if 0 <= i + by < count]
    return lax.ppermute(x, axis, pairs)


def swapped(x, axis, bit):
    count = lax.axis_size(axis)
    return lax.ppermute(x, axis, [(i, i ^ bit) for i in range(count)])


def group_sum(x, axis, stride, size):
    values = [x] + [swapped(x, axis, stride * d) for d in range(1, size)]
    while len(values) > 1:
        values = [values[i] + values[i + 1] for i in range(0, len(values), 2)]
    return values[0]


def butterfly_bits(axis):
    count = lax.axis_size(axis)
    assert count & (count - 1) == 0
    bits = []
    bit = 1
    while bit < count:
        bits.append(bit)
        bit *= 2
    return bits


def split_dot(a, b):
    a_hi = a.astype(jnp.bfloat16)
    a_lo = (a - a_hi.astype(jnp.float32)).astype(jnp.bfloat16)
    b_hi = b.astype(jnp.bfloat16)
    b_lo = (b - b_hi.astype(jnp.float32)).astype(jnp.bfloat16)
    out = jnp.dot(a_hi, b_hi, preferred_element_type=jnp.float32)
    out = out + jnp.dot(a_hi, b_lo, preferred_element_type=jnp.float32)
    return out + jnp.dot(a_lo, b_hi, preferred_element_type=jnp.float32)


def finish_kernel(qd_ref, back_ref, intra_ref, gain_ref, lw_ref, pw_ref, member_ref,
                  out_ref, part_ref, *, qk_scale):
    block = back_ref[...]
    state = block.reshape(block.shape[0] * block.shape[1], block.shape[2])
    inter = split_dot(qd_ref[...], state)
    total = intra_ref[...] + inter * qk_scale
    centred = total - jnp.mean(total, axis=1, keepdims=True)
    variance = jnp.mean(centred * centred, axis=1, keepdims=True)
    normed = centred * lax.rsqrt(variance + 1e-05) * gain_ref[...]
    y = normed.astype(jnp.bfloat16)
    out_ref[...] = y
    label_value = lax.dot_general(
        lw_ref[...], y, (((1,), (1,)), ((), ())), preferred_element_type=jnp.float32
    )
    prod = pw_ref[0] * label_value
    member = member_ref[...]
    hi = prod.astype(jnp.bfloat16)
    rest = prod - hi.astype(jnp.float32)
    mid = rest.astype(jnp.bfloat16)
    lo = (rest - mid.astype(jnp.float32)).astype(jnp.bfloat16)
    weighted = jnp.dot(hi, member, preferred_element_type=jnp.float32)
    weighted = weighted + jnp.dot(mid, member, preferred_element_type=jnp.float32)
    part_ref[0] = weighted + jnp.dot(lo, member, preferred_element_type=jnp.float32)


def finish_call(q_decayed, back, intra, norm_gain, label_weight, pool_weight, member_cols,
                head_count, qk_scale):
    tok_rows, model_width = q_decayed.shape
    head_dim = model_width // head_count
    owners, _, lanes = back.shape
    per_head = owners // head_count
    rows = head_dim // per_head
    label_count = label_weight.shape[0]
    width = member_cols.shape[1]
    return pl.pallas_call(
        functools.partial(finish_kernel, qk_scale=qk_scale),
        grid=(head_count,),
        in_specs=[
            pl.BlockSpec((tok_rows, head_dim), lambda h: (0, h)),
            pl.BlockSpec((per_head, rows, lanes), lambda h: (h, 0, 0)),
            pl.BlockSpec((tok_rows, head_dim), lambda h: (0, h)),
            pl.BlockSpec((1, head_dim), lambda h: (0, h)),
            pl.BlockSpec((label_count, head_dim), lambda h: (0, h)),
            pl.BlockSpec((1, label_count, tok_rows), lambda h: (h, 0, 0)),
            pl.BlockSpec((tok_rows, width), lambda h: (0, 0)),
        ],
        out_specs=[
            pl.BlockSpec((tok_rows, head_dim), lambda h: (0, h)),
            pl.BlockSpec((1, label_count, width), lambda h: (h, 0, 0)),
        ],
        out_shape=[
            jax.ShapeDtypeStruct((tok_rows, model_width), jnp.bfloat16),
            jax.ShapeDtypeStruct((head_count, label_count, width), jnp.float32),
        ],
    )(q_decayed, back, intra, norm_gain.reshape(1, model_width), label_weight, pool_weight,
      member_cols)


def record_ids(length_row, positions):
    starts = jnp.cumsum(length_row) - length_row
    return jnp.sum((starts[:, None] <= positions[None, :]).astype(jnp.int32), axis=0) - 1


def exclusive_state_scan(local_state, carry, stats, axis):
    head_count, head_dim, _ = local_state.shape
    count = lax.axis_size(axis)
    rows = head_count * head_dim // count
    assert rows * count == head_count * head_dim and head_dim % rows == 0
    pair_count, fields = stats.shape
    per_owner = pair_count // count
    assert per_owner * count == pair_count and per_owner * fields < 8 * head_dim
    pad = 8 * head_dim - per_owner * fields - 1
    owner_head = (jnp.arange(count) * rows) // head_dim
    slices = local_state.reshape(count, rows, head_dim)
    extra = jnp.concatenate(
        [
            stats.reshape(count, per_owner * fields),
            carry[owner_head][:, None],
            jnp.zeros((count, pad), jnp.float32),
        ],
        axis=1,
    ).reshape(count, 8, head_dim)
    got = lax.all_to_all(jnp.concatenate([slices, extra], axis=1), axis, 0, 0)
    got_extra = got[:, rows:, :].reshape(count, 8 * head_dim)
    factors = got_extra[:, per_owner * fields]
    part = got_extra[:, : per_owner * fields].reshape(count, per_owner, fields)
    part_top = part[:, :, :head_count]
    top = jnp.max(part_top, axis=0)
    mass = jnp.sum(part[:, :, head_count:2 * head_count] * jnp.exp(part_top - top[None]), axis=0)
    tally = jnp.sum(part[:, :, 2 * head_count:], axis=0)
    combined = jnp.concatenate([top, mass, tally], axis=1).reshape(1, per_owner * fields)
    block = jnp.arange(count)
    inside = (block[None, None, :] > block[None, :, None]) & (block[None, None, :] < block[:, None, None])
    spans = jnp.prod(jnp.where(inside, factors[None, None, :], 1.0), axis=2)
    mix = jnp.where(block[None, :] < block[:, None], spans, 0.0)
    scanned = jnp.dot(
        mix, got[:, :rows, :].reshape(count, rows * head_dim), precision=lax.Precision.HIGHEST
    )
    back_extra = jnp.broadcast_to(
        jnp.concatenate([combined, jnp.zeros((1, pad + 1), jnp.float32)], axis=1),
        (count, 8 * head_dim),
    ).reshape(count, 8, head_dim)
    sent_back = jnp.concatenate([scanned.reshape(count, rows, head_dim), back_extra], axis=1)
    back = lax.all_to_all(sent_back, axis, 0, 0)
    totals = back[:, rows:, :].reshape(count, 8 * head_dim)[:, : per_owner * fields]
    return back, totals.reshape(pair_count, fields)


def local(
    tokens,
    log_decay,
    lengths,
    label_ids,
    w_query,
    w_key,
    w_value,
    norm_gain,
    label_query,
    label_weight,
):
    tok_rows = tokens.shape[1]
    model_width = tokens.shape[2]
    head_count = log_decay.shape[1]
    head_dim = model_width // head_count
    qk_scale = head_dim ** (-0.5)
    record_count = lengths.shape[1]
    label_count = label_query.shape[0]
    shard_start = lax.axis_index("ctx") * tok_rows
    local_pos = jnp.arange(tok_rows, dtype=jnp.int32)
    record = record_ids(lengths[0], shard_start + local_pos)
    before_rec = record_ids(lengths[0], jnp.reshape(shard_start - 1, (1,)))[0]
    features = tokens[0]
    queries = jnp.dot(features, w_query, preferred_element_type=jnp.float32).astype(jnp.bfloat16)
    key_rows = jnp.dot(features, w_key, preferred_element_type=jnp.float32).astype(jnp.bfloat16)
    value_rows = jnp.dot(features, w_value, preferred_element_type=jnp.float32).astype(jnp.bfloat16)
    q3 = queries.reshape(tok_rows, head_count, head_dim)
    k3 = key_rows.reshape(tok_rows, head_count, head_dim)
    v3 = value_rows.reshape(tok_rows, head_count, head_dim)
    decay_cum = jnp.cumsum(log_decay[0], axis=1)
    pair_mask = (local_pos[:, None] >= local_pos[None, :]) & (record[:, None] == record[None, :])
    linked = record == before_rec
    tail_rec = record == record[tok_rows - 1]

    last_cum = decay_cum[:, tok_rows - 1]
    k_factor = jnp.where(tail_rec[None, :], jnp.exp(last_cum[:, None] - decay_cum), 0.0)
    k_decayed = (k3.astype(jnp.float32) * k_factor.T[:, :, None]).astype(jnp.bfloat16)
    local_state = jnp.einsum("thd,the->hde", k_decayed, v3, preferred_element_type=jnp.float32)
    carry = jnp.where(linked[tok_rows - 1], jnp.exp(last_cum), 0.0)

    scores = jnp.einsum("thd,shd->hts", q3, k3, preferred_element_type=jnp.float32) * qk_scale
    decay_pair = jnp.exp(jnp.minimum(decay_cum[:, :, None] - decay_cum[:, None, :], 0.0))
    weights = jnp.where(pair_mask[None], scores * decay_pair, 0.0).astype(jnp.bfloat16)
    intra = jnp.einsum("hts,shd->thd", weights, v3, preferred_element_type=jnp.float32)

    member = record[None, :] == jnp.arange(record_count, dtype=jnp.int32)[:, None]
    kf3 = features.reshape(tok_rows, head_count, head_dim)
    lq3 = label_query.reshape(label_count, head_count, head_dim)
    lw3 = label_weight.reshape(label_count, head_count, head_dim)
    pscore = jnp.einsum("lhd,thd->hlt", lq3, kf3, preferred_element_type=jnp.float32) * qk_scale
    maxima = jnp.max(
        jnp.where(member[None, :, None, :], pscore[:, None, :, :], NEG_FILL), axis=3
    )
    maxima_tok = jnp.sum(
        jnp.where(member[None, :, None, :], maxima[:, :, :, None], 0.0), axis=1
    )
    pool_weight = jnp.exp(pscore - maxima_tok)
    mass = jnp.sum(jnp.where(member[None, :, None, :], pool_weight[:, None], 0.0), axis=3)
    label_hot = (label_ids[0][:, None] == jnp.arange(label_count, dtype=jnp.int32)[None, :]).astype(
        jnp.bfloat16
    )
    counts = jnp.dot(member.astype(jnp.bfloat16), label_hot, preferred_element_type=jnp.float32)

    stats = jnp.concatenate(
        [
            jnp.transpose(maxima, (1, 2, 0)),
            jnp.transpose(mass, (1, 2, 0)),
            counts[:, :, None],
        ],
        axis=2,
    ).reshape(record_count * label_count, 2 * head_count + 1)
    incoming, totals = exclusive_state_scan(local_state, carry, stats, "ctx")
    totals = totals.reshape(record_count, label_count, 2 * head_count + 1)
    top = jnp.transpose(totals[:, :, :head_count], (2, 0, 1))
    total_mass = jnp.transpose(totals[:, :, head_count:2 * head_count], (2, 0, 1))
    total_counts = totals[:, :, 2 * head_count]
    rescale = jnp.exp(maxima - top) / total_mass

    q_decayed = (
        q3.astype(jnp.float32) * jnp.where(linked[None, :], jnp.exp(decay_cum), 0.0).T[:, :, None]
    ).reshape(tok_rows, model_width)
    member_cols = jnp.zeros((tok_rows, 128), jnp.bfloat16).at[:, :record_count].set(
        member.T.astype(jnp.bfloat16)
    )
    out_rows, head_parts = finish_call(
        q_decayed, incoming, intra.reshape(tok_rows, model_width), norm_gain, label_weight,
        pool_weight, member_cols, head_count, qk_scale,
    )
    part = jnp.sum(jnp.transpose(head_parts[:, :, :record_count], (0, 2, 1)) * rescale, axis=0)
    count = lax.axis_size("ctx")
    inner = min(count, 8)
    assert count % inner == 0 and inner & (inner - 1) == 0
    part = group_sum(part, "ctx", 1, inner)
    if count > inner:
        part = group_sum(part, "ctx", inner, count // inner)
    logits = part
    target = (total_counts + 0.5) / (lengths[0].astype(jnp.float32)[:, None] + 1.0)
    rec_loss = jnp.mean(jax.nn.softplus(logits) - target * logits, axis=1)
    mean_loss = group_sum(jnp.sum(rec_loss), "dp", 1, lax.axis_size("dp")) / (
        lax.axis_size("dp") * record_count
    )
    return (out_rows[None], logits[None], rec_loss[None], mean_loss)


def solution(mesh):
    return jax.shard_map(
        local,
        mesh=mesh,
        in_specs=(
            P("dp", "ctx", None),
            P("dp", None, "ctx"),
            P("dp", None),
            P("dp", "ctx"),
            P(),
            P(),
            P(),
            P(),
            P(),
            P(),
        ),
        out_specs=(P("dp", "ctx", None), P("dp", None, None), P("dp", None), P()),
        check_vma=False,
    )
```

```python
import jax
import jax.numpy as jnp
from jax import lax
from jax.sharding import PartitionSpec as P

NEG_FILL = -1e30


def shifted(x, axis, by):
    count = lax.axis_size(axis)
    pairs = [(i, i + by) for i in range(count) if 0 <= i + by < count]
    return lax.ppermute(x, axis, pairs)


def swapped(x, axis, bit):
    count = lax.axis_size(axis)
    return lax.ppermute(x, axis, [(i, i ^ bit) for i in range(count)])


def group_sum(x, axis, stride, size):
    values = [x] + [swapped(x, axis, stride * d) for d in range(1, size)]
    while len(values) > 1:
        values = [values[i] + values[i + 1] for i in range(0, len(values), 2)]
    return values[0]


def butterfly_bits(axis):
    count = lax.axis_size(axis)
    assert count & (count - 1) == 0
    bits = []
    bit = 1
    while bit < count:
        bits.append(bit)
        bit *= 2
    return bits


def record_ids(length_row, positions):
    starts = jnp.cumsum(length_row) - length_row
    return jnp.sum((starts[:, None] <= positions[None, :]).astype(jnp.int32), axis=0) - 1


def exclusive_state_scan(local_state, carry, stats, axis):
    head_count, head_dim, _ = local_state.shape
    count = lax.axis_size(axis)
    rows = head_count * head_dim // count
    assert rows * count == head_count * head_dim and head_dim % rows == 0
    pair_count, fields = stats.shape
    per_owner = pair_count // count
    assert per_owner * count == pair_count and per_owner * fields < 8 * head_dim
    pad = 8 * head_dim - per_owner * fields - 1
    owner_head = (jnp.arange(count) * rows) // head_dim
    slices = local_state.reshape(count, rows, head_dim)
    extra = jnp.concatenate(
        [
            stats.reshape(count, per_owner * fields),
            carry[owner_head][:, None],
            jnp.zeros((count, pad), jnp.float32),
        ],
        axis=1,
    ).reshape(count, 8, head_dim)
    got = lax.all_to_all(jnp.concatenate([slices, extra], axis=1), axis, 0, 0)
    got_extra = got[:, rows:, :].reshape(count, 8 * head_dim)
    factors = got_extra[:, per_owner * fields]
    part = got_extra[:, : per_owner * fields].reshape(count, per_owner, fields)
    part_top = part[:, :, :head_count]
    top = jnp.max(part_top, axis=0)
    mass = jnp.sum(part[:, :, head_count:2 * head_count] * jnp.exp(part_top - top[None]), axis=0)
    tally = jnp.sum(part[:, :, 2 * head_count:], axis=0)
    combined = jnp.concatenate([top, mass, tally], axis=1).reshape(1, per_owner * fields)
    block = jnp.arange(count)
    inside = (block[None, None, :] > block[None, :, None]) & (block[None, None, :] < block[:, None, None])
    spans = jnp.prod(jnp.where(inside, factors[None, None, :], 1.0), axis=2)
    mix = jnp.where(block[None, :] < block[:, None], spans, 0.0)
    scanned = jnp.dot(
        mix, got[:, :rows, :].reshape(count, rows * head_dim), precision=lax.Precision.HIGHEST
    )
    back_extra = jnp.broadcast_to(
        jnp.concatenate([combined, jnp.zeros((1, pad + 1), jnp.float32)], axis=1),
        (count, 8 * head_dim),
    ).reshape(count, 8, head_dim)
    sent_back = jnp.concatenate([scanned.reshape(count, rows, head_dim), back_extra], axis=1)
    back = lax.all_to_all(sent_back, axis, 0, 0)
    state = back[:, :rows, :].reshape(head_count, head_dim, head_dim)
    totals = back[:, rows:, :].reshape(count, 8 * head_dim)[:, : per_owner * fields]
    return state, totals.reshape(pair_count, fields)


def local(
    tokens,
    log_decay,
    lengths,
    label_ids,
    w_query,
    w_key,
    w_value,
    norm_gain,
    label_query,
    label_weight,
):
    tok_rows = tokens.shape[1]
    model_width = tokens.shape[2]
    head_count = log_decay.shape[1]
    head_dim = model_width // head_count
    qk_scale = head_dim ** (-0.5)
    record_count = lengths.shape[1]
    label_count = label_query.shape[0]
    shard_start = lax.axis_index("ctx") * tok_rows
    local_pos = jnp.arange(tok_rows, dtype=jnp.int32)
    record = record_ids(lengths[0], shard_start + local_pos)
    before_rec = record_ids(lengths[0], jnp.reshape(shard_start - 1, (1,)))[0]
    features = tokens[0]
    queries = jnp.dot(features, w_query, preferred_element_type=jnp.float32).astype(jnp.bfloat16)
    key_rows = jnp.dot(features, w_key, preferred_element_type=jnp.float32).astype(jnp.bfloat16)
    value_rows = jnp.dot(features, w_value, preferred_element_type=jnp.float32).astype(jnp.bfloat16)
    q3 = queries.reshape(tok_rows, head_count, head_dim)
    k3 = key_rows.reshape(tok_rows, head_count, head_dim)
    v3 = value_rows.reshape(tok_rows, head_count, head_dim)
    decay_cum = jnp.cumsum(log_decay[0], axis=1)
    pair_mask = (local_pos[:, None] >= local_pos[None, :]) & (record[:, None] == record[None, :])
    linked = record == before_rec
    tail_rec = record == record[tok_rows - 1]

    last_cum = decay_cum[:, tok_rows - 1]
    k_factor = jnp.where(tail_rec[None, :], jnp.exp(last_cum[:, None] - decay_cum), 0.0)
    k_decayed = (k3.astype(jnp.float32) * k_factor.T[:, :, None]).astype(jnp.bfloat16)
    local_state = jnp.einsum("thd,the->hde", k_decayed, v3, preferred_element_type=jnp.float32)
    carry = jnp.where(linked[tok_rows - 1], jnp.exp(last_cum), 0.0)

    scores = jnp.einsum("thd,shd->hts", q3, k3, preferred_element_type=jnp.float32) * qk_scale
    decay_pair = jnp.exp(jnp.minimum(decay_cum[:, :, None] - decay_cum[:, None, :], 0.0))
    weights = jnp.where(pair_mask[None], scores * decay_pair, 0.0).astype(jnp.bfloat16)
    intra = jnp.einsum("hts,shd->thd", weights, v3, preferred_element_type=jnp.float32)

    member = record[None, :] == jnp.arange(record_count, dtype=jnp.int32)[:, None]
    kf3 = features.reshape(tok_rows, head_count, head_dim)
    lq3 = label_query.reshape(label_count, head_count, head_dim)
    lw3 = label_weight.reshape(label_count, head_count, head_dim)
    pscore = jnp.einsum("lhd,thd->hlt", lq3, kf3, preferred_element_type=jnp.float32) * qk_scale
    maxima = jnp.max(
        jnp.where(member[None, :, None, :], pscore[:, None, :, :], NEG_FILL), axis=3
    )
    maxima_tok = jnp.sum(
        jnp.where(member[None, :, None, :], maxima[:, :, :, None], 0.0), axis=1
    )
    pool_weight = jnp.exp(pscore - maxima_tok)
    mass = jnp.sum(jnp.where(member[None, :, None, :], pool_weight[:, None], 0.0), axis=3)
    label_hot = (label_ids[0][:, None] == jnp.arange(label_count, dtype=jnp.int32)[None, :]).astype(
        jnp.bfloat16
    )
    counts = jnp.dot(member.astype(jnp.bfloat16), label_hot, preferred_element_type=jnp.float32)

    stats = jnp.concatenate(
        [
            jnp.transpose(maxima, (1, 2, 0)),
            jnp.transpose(mass, (1, 2, 0)),
            counts[:, :, None],
        ],
        axis=2,
    ).reshape(record_count * label_count, 2 * head_count + 1)
    incoming, totals = exclusive_state_scan(local_state, carry, stats, "ctx")
    totals = totals.reshape(record_count, label_count, 2 * head_count + 1)
    top = jnp.transpose(totals[:, :, :head_count], (2, 0, 1))
    total_mass = jnp.transpose(totals[:, :, head_count:2 * head_count], (2, 0, 1))
    total_counts = totals[:, :, 2 * head_count]
    rescale = jnp.exp(maxima - top) / total_mass

    q_decayed = q3.astype(jnp.float32) * jnp.where(linked[None, :], jnp.exp(decay_cum), 0.0).T[:, :, None]
    inter = jnp.einsum(
        "thd,hde->the", q_decayed, incoming, precision=lax.Precision.HIGH,
        preferred_element_type=jnp.float32,
    )
    total_out = intra + inter * qk_scale
    centred = total_out - jnp.mean(total_out, axis=2, keepdims=True)
    variance = jnp.mean(centred * centred, axis=2, keepdims=True)
    gain3 = norm_gain.reshape(head_count, head_dim)
    normed = centred * lax.rsqrt(variance + 1e-05) * gain3[None]
    out_rows = normed.reshape(tok_rows, model_width).astype(jnp.bfloat16)

    y3 = out_rows.reshape(tok_rows, head_count, head_dim)
    label_value = jnp.einsum("lhd,thd->hlt", lw3, y3, preferred_element_type=jnp.float32)
    weighted = jnp.sum(
        jnp.where(member[None, :, None, :], (pool_weight * label_value)[:, None], 0.0), axis=3
    )
    part = jnp.sum(weighted * rescale, axis=0)
    count = lax.axis_size("ctx")
    inner = min(count, 8)
    assert count % inner == 0 and inner & (inner - 1) == 0
    part = group_sum(part, "ctx", 1, inner)
    if count > inner:
        part = group_sum(part, "ctx", inner, count // inner)
    logits = part
    target = (total_counts + 0.5) / (lengths[0].astype(jnp.float32)[:, None] + 1.0)
    rec_loss = jnp.mean(jax.nn.softplus(logits) - target * logits, axis=1)
    loss_sum = jnp.sum(rec_loss)
    for bit in butterfly_bits("dp"):
        loss_sum = loss_sum + swapped(loss_sum, "dp", bit)
    mean_loss = loss_sum / (lax.axis_size("dp") * record_count)
    return (out_rows[None], logits[None], rec_loss[None], mean_loss)


def solution(mesh):
    return jax.shard_map(
        local,
        mesh=mesh,
        in_specs=(
            P("dp", "ctx", None),
            P("dp", None, "ctx"),
            P("dp", None),
            P("dp", "ctx"),
            P(),
            P(),
            P(),
            P(),
            P(),
            P(),
        ),
        out_specs=(P("dp", "ctx", None), P("dp", None, None), P("dp", None), P()),
        check_vma=False,
    )
```

```python
import functools

import jax
import jax.numpy as jnp
from jax import lax
from jax.experimental import pallas as pl
from jax.sharding import PartitionSpec as P

NEG_FILL = -1e30


def shifted(x, axis, by):
    count = lax.axis_size(axis)
    pairs = [(i, i + by) for i in range(count) if 0 <= i + by < count]
    return lax.ppermute(x, axis, pairs)


def swapped(x, axis, bit):
    count = lax.axis_size(axis)
    return lax.ppermute(x, axis, [(i, i ^ bit) for i in range(count)])


def group_sum(x, axis, stride, size):
    values = [x] + [swapped(x, axis, stride * d) for d in range(1, size)]
    while len(values) > 1:
        values = [values[i] + values[i + 1] for i in range(0, len(values), 2)]
    return values[0]


def butterfly_bits(axis):
    count = lax.axis_size(axis)
    assert count & (count - 1) == 0
    bits = []
    bit = 1
    while bit < count:
        bits.append(bit)
        bit *= 2
    return bits


def pool_stats_kernel(lq_ref, kf_ref, member_ref, weight_ref, stats_ref, *, qk_scale, record_count):
    score = lax.dot_general(
        lq_ref[...], kf_ref[...], (((1,), (1,)), ((), ())), preferred_element_type=jnp.float32
    ) * qk_scale
    member = member_ref[...]
    masks = [member[r:r + 1, :] > 0.5 for r in range(record_count)]
    tops = [jnp.max(jnp.where(m, score, NEG_FILL), axis=1, keepdims=True) for m in masks]
    top_tok = jnp.zeros_like(score)
    for m, t in zip(masks, tops):
        top_tok = top_tok + jnp.where(m, t, 0.0)
    weight = jnp.exp(score - top_tok)
    weight_ref[0] = weight
    masses = [jnp.sum(jnp.where(m, weight, 0.0), axis=1, keepdims=True) for m in masks]
    stats_ref[0] = jnp.concatenate(tops + masses, axis=1)


def pool_stats_call(label_query, features, member_rows, head_count, qk_scale):
    label_count, model_width = label_query.shape
    tok_rows = features.shape[0]
    head_dim = model_width // head_count
    record_count = member_rows.shape[0]
    return pl.pallas_call(
        functools.partial(pool_stats_kernel, qk_scale=qk_scale, record_count=record_count),
        grid=(head_count,),
        in_specs=[
            pl.BlockSpec((label_count, head_dim), lambda h: (0, h)),
            pl.BlockSpec((tok_rows, head_dim), lambda h: (0, h)),
            pl.BlockSpec((record_count, tok_rows), lambda h: (0, 0)),
        ],
        out_specs=[
            pl.BlockSpec((1, label_count, tok_rows), lambda h: (h, 0, 0)),
            pl.BlockSpec((1, label_count, 2 * record_count), lambda h: (h, 0, 0)),
        ],
        out_shape=[
            jax.ShapeDtypeStruct((head_count, label_count, tok_rows), jnp.float32),
            jax.ShapeDtypeStruct((head_count, label_count, 2 * record_count), jnp.float32),
        ],
    )(label_query, features, member_rows)


def record_ids(length_row, positions):
    starts = jnp.cumsum(length_row) - length_row
    return jnp.sum((starts[:, None] <= positions[None, :]).astype(jnp.int32), axis=0) - 1


def exclusive_state_scan(local_state, carry, stats, passenger, axis):
    head_count, head_dim, _ = local_state.shape
    count = lax.axis_size(axis)
    rows = head_count * head_dim // count
    assert rows * count == head_count * head_dim and head_dim % rows == 0
    pair_count, fields = stats.shape
    per_owner = pair_count // count
    assert per_owner * count == pair_count and per_owner * fields < 8 * head_dim
    pad = 8 * head_dim - per_owner * fields - 1
    owner_head = (jnp.arange(count) * rows) // head_dim
    slices = local_state.reshape(count, rows, head_dim)
    extra = jnp.concatenate(
        [
            stats.reshape(count, per_owner * fields),
            carry[owner_head][:, None],
            jnp.zeros((count, pad), jnp.float32),
        ],
        axis=1,
    ).reshape(count, 8, head_dim)
    got = lax.all_to_all(jnp.concatenate([slices, extra], axis=1), axis, 0, 0)
    got, passenger = lax.optimization_barrier((got, passenger))
    got_extra = got[:, rows:, :].reshape(count, 8 * head_dim)
    factors = got_extra[:, per_owner * fields]
    part = got_extra[:, : per_owner * fields].reshape(count, per_owner, fields)
    part_top = part[:, :, :head_count]
    top = jnp.max(part_top, axis=0)
    mass = jnp.sum(part[:, :, head_count:2 * head_count] * jnp.exp(part_top - top[None]), axis=0)
    tally = jnp.sum(part[:, :, 2 * head_count:], axis=0)
    combined = jnp.concatenate([top, mass, tally], axis=1).reshape(1, per_owner * fields)
    block = jnp.arange(count)
    inside = (block[None, None, :] > block[None, :, None]) & (block[None, None, :] < block[:, None, None])
    spans = jnp.prod(jnp.where(inside, factors[None, None, :], 1.0), axis=2)
    mix = jnp.where(block[None, :] < block[:, None], spans, 0.0)
    scanned = jnp.dot(
        mix, got[:, :rows, :].reshape(count, rows * head_dim), precision=lax.Precision.HIGHEST
    )
    back_extra = jnp.broadcast_to(
        jnp.concatenate([combined, jnp.zeros((1, pad + 1), jnp.float32)], axis=1),
        (count, 8 * head_dim),
    ).reshape(count, 8, head_dim)
    sent_back = jnp.concatenate([scanned.reshape(count, rows, head_dim), back_extra], axis=1)
    back = lax.all_to_all(sent_back, axis, 0, 0)
    state = back[:, :rows, :].reshape(head_count, head_dim, head_dim)
    totals = back[:, rows:, :].reshape(count, 8 * head_dim)[:, : per_owner * fields]
    return state, totals.reshape(pair_count, fields), passenger


def local(
    tokens,
    log_decay,
    lengths,
    label_ids,
    w_query,
    w_key,
    w_value,
    norm_gain,
    label_query,
    label_weight,
):
    tok_rows = tokens.shape[1]
    model_width = tokens.shape[2]
    head_count = log_decay.shape[1]
    head_dim = model_width // head_count
    qk_scale = head_dim ** (-0.5)
    record_count = lengths.shape[1]
    label_count = label_query.shape[0]
    shard_start = lax.axis_index("ctx") * tok_rows
    local_pos = jnp.arange(tok_rows, dtype=jnp.int32)
    record = record_ids(lengths[0], shard_start + local_pos)
    before_rec = record_ids(lengths[0], jnp.reshape(shard_start - 1, (1,)))[0]
    features = tokens[0]
    queries = jnp.dot(features, w_query, preferred_element_type=jnp.float32).astype(jnp.bfloat16)
    key_rows = jnp.dot(features, w_key, preferred_element_type=jnp.float32).astype(jnp.bfloat16)
    value_rows = jnp.dot(features, w_value, preferred_element_type=jnp.float32).astype(jnp.bfloat16)
    q3 = queries.reshape(tok_rows, head_count, head_dim)
    k3 = key_rows.reshape(tok_rows, head_count, head_dim)
    v3 = value_rows.reshape(tok_rows, head_count, head_dim)
    decay_cum = jnp.cumsum(log_decay[0], axis=1)
    pair_mask = (local_pos[:, None] >= local_pos[None, :]) & (record[:, None] == record[None, :])
    linked = record == before_rec
    tail_rec = record == record[tok_rows - 1]

    last_cum = decay_cum[:, tok_rows - 1]
    k_factor = jnp.where(tail_rec[None, :], jnp.exp(last_cum[:, None] - decay_cum), 0.0)
    k_decayed = (k3.astype(jnp.float32) * k_factor.T[:, :, None]).astype(jnp.bfloat16)
    local_state = jnp.einsum("thd,the->hde", k_decayed, v3, preferred_element_type=jnp.float32)
    carry = jnp.where(linked[tok_rows - 1], jnp.exp(last_cum), 0.0)

    scores = jnp.einsum("thd,shd->hts", q3, k3, preferred_element_type=jnp.float32) * qk_scale
    decay_pair = jnp.exp(jnp.minimum(decay_cum[:, :, None] - decay_cum[:, None, :], 0.0))
    weights = jnp.where(pair_mask[None], scores * decay_pair, 0.0).astype(jnp.bfloat16)
    intra = jnp.einsum("hts,shd->thd", weights, v3, preferred_element_type=jnp.float32)

    member = record[None, :] == jnp.arange(record_count, dtype=jnp.int32)[:, None]
    kf3 = features.reshape(tok_rows, head_count, head_dim)
    lq3 = label_query.reshape(label_count, head_count, head_dim)
    lw3 = label_weight.reshape(label_count, head_count, head_dim)
    pool_weight, head_stats = pool_stats_call(
        label_query, features, member.astype(jnp.float32), head_count, qk_scale
    )
    maxima = jnp.transpose(head_stats[:, :, :record_count], (0, 2, 1))
    mass = jnp.transpose(head_stats[:, :, record_count:], (0, 2, 1))
    label_hot = (label_ids[0][:, None] == jnp.arange(label_count, dtype=jnp.int32)[None, :]).astype(
        jnp.bfloat16
    )
    counts = jnp.dot(member.astype(jnp.bfloat16), label_hot, preferred_element_type=jnp.float32)

    stats = jnp.concatenate(
        [
            jnp.transpose(maxima, (1, 2, 0)),
            jnp.transpose(mass, (1, 2, 0)),
            counts[:, :, None],
        ],
        axis=2,
    ).reshape(record_count * label_count, 2 * head_count + 1)
    incoming, totals, intra = exclusive_state_scan(local_state, carry, stats, intra, "ctx")
    totals = totals.reshape(record_count, label_count, 2 * head_count + 1)
    top = jnp.transpose(totals[:, :, :head_count], (2, 0, 1))
    total_mass = jnp.transpose(totals[:, :, head_count:2 * head_count], (2, 0, 1))
    total_counts = totals[:, :, 2 * head_count]
    rescale = jnp.exp(maxima - top) / total_mass

    q_decayed = q3.astype(jnp.float32) * jnp.where(linked[None, :], jnp.exp(decay_cum), 0.0).T[:, :, None]
    inter = jnp.einsum(
        "thd,hde->the", q_decayed, incoming, precision=lax.Precision.HIGH,
        preferred_element_type=jnp.float32,
    )
    total_out = intra + inter * qk_scale
    centred = total_out - jnp.mean(total_out, axis=2, keepdims=True)
    variance = jnp.mean(centred * centred, axis=2, keepdims=True)
    gain3 = norm_gain.reshape(head_count, head_dim)
    normed = centred * lax.rsqrt(variance + 1e-05) * gain3[None]
    out_rows = normed.reshape(tok_rows, model_width).astype(jnp.bfloat16)

    y3 = out_rows.reshape(tok_rows, head_count, head_dim)
    label_value = jnp.einsum("lhd,thd->hlt", lw3, y3, preferred_element_type=jnp.float32)
    weighted = jnp.sum(
        jnp.where(member[None, :, None, :], (pool_weight * label_value)[:, None], 0.0), axis=3
    )
    part = jnp.sum(weighted * rescale, axis=0)
    count = lax.axis_size("ctx")
    inner = min(count, 8)
    assert count % inner == 0 and inner & (inner - 1) == 0
    part = group_sum(part, "ctx", 1, inner)
    if count > inner:
        part = group_sum(part, "ctx", inner, count // inner)
    logits = part
    target = (total_counts + 0.5) / (lengths[0].astype(jnp.float32)[:, None] + 1.0)
    rec_loss = jnp.mean(jax.nn.softplus(logits) - target * logits, axis=1)
    loss_sum = jnp.sum(rec_loss)
    for bit in butterfly_bits("dp"):
        loss_sum = loss_sum + swapped(loss_sum, "dp", bit)
    mean_loss = loss_sum / (lax.axis_size("dp") * record_count)
    return (out_rows[None], logits[None], rec_loss[None], mean_loss)


def solution(mesh):
    return jax.shard_map(
        local,
        mesh=mesh,
        in_specs=(
            P("dp", "ctx", None),
            P("dp", None, "ctx"),
            P("dp", None),
            P("dp", "ctx"),
            P(),
            P(),
            P(),
            P(),
            P(),
            P(),
        ),
        out_specs=(P("dp", "ctx", None), P("dp", None, None), P("dp", None), P()),
        check_vma=False,
    )
```

```python
import jax
import jax.numpy as jnp
from jax import lax
from jax.sharding import PartitionSpec as P

NEG_FILL = -1e30


def shifted(x, axis, by):
    count = lax.axis_size(axis)
    pairs = [(i, i + by) for i in range(count) if 0 <= i + by < count]
    return lax.ppermute(x, axis, pairs)


def swapped(x, axis, bit):
    count = lax.axis_size(axis)
    return lax.ppermute(x, axis, [(i, i ^ bit) for i in range(count)])


def group_sum(x, axis, stride, size):
    values = [x] + [swapped(x, axis, stride * d) for d in range(1, size)]
    while len(values) > 1:
        values = [values[i] + values[i + 1] for i in range(0, len(values), 2)]
    return values[0]


def butterfly_bits(axis):
    count = lax.axis_size(axis)
    assert count & (count - 1) == 0
    bits = []
    bit = 1
    while bit < count:
        bits.append(bit)
        bit *= 2
    return bits


def record_ids(length_row, positions):
    starts = jnp.cumsum(length_row) - length_row
    return jnp.sum((starts[:, None] <= positions[None, :]).astype(jnp.int32), axis=0) - 1


def exclusive_state_scan(local_state, carry, stats, passenger, axis):
    head_count, head_dim, _ = local_state.shape
    count = lax.axis_size(axis)
    rows = head_count * head_dim // count
    assert rows * count == head_count * head_dim and head_dim % rows == 0
    pair_count, fields = stats.shape
    per_owner = pair_count // count
    assert per_owner * count == pair_count and per_owner * fields < 8 * head_dim
    pad = 8 * head_dim - per_owner * fields - 1
    owner_head = (jnp.arange(count) * rows) // head_dim
    slices = local_state.reshape(count, rows, head_dim)
    extra = jnp.concatenate(
        [
            stats.reshape(count, per_owner * fields),
            carry[owner_head][:, None],
            jnp.zeros((count, pad), jnp.float32),
        ],
        axis=1,
    ).reshape(count, 8, head_dim)
    got = lax.all_to_all(jnp.concatenate([slices, extra], axis=1), axis, 0, 0)
    got, passenger = lax.optimization_barrier((got, passenger))
    got_extra = got[:, rows:, :].reshape(count, 8 * head_dim)
    factors = got_extra[:, per_owner * fields]
    part = got_extra[:, : per_owner * fields].reshape(count, per_owner, fields)
    part_top = part[:, :, :head_count]
    top = jnp.max(part_top, axis=0)
    mass = jnp.sum(part[:, :, head_count:2 * head_count] * jnp.exp(part_top - top[None]), axis=0)
    tally = jnp.sum(part[:, :, 2 * head_count:], axis=0)
    combined = jnp.concatenate([top, mass, tally], axis=1).reshape(1, per_owner * fields)
    block = jnp.arange(count)
    inside = (block[None, None, :] > block[None, :, None]) & (block[None, None, :] < block[:, None, None])
    spans = jnp.prod(jnp.where(inside, factors[None, None, :], 1.0), axis=2)
    mix = jnp.where(block[None, :] < block[:, None], spans, 0.0)
    scanned = jnp.dot(
        mix, got[:, :rows, :].reshape(count, rows * head_dim), precision=lax.Precision.HIGHEST
    )
    back_extra = jnp.broadcast_to(
        jnp.concatenate([combined, jnp.zeros((1, pad + 1), jnp.float32)], axis=1),
        (count, 8 * head_dim),
    ).reshape(count, 8, head_dim)
    sent_back = jnp.concatenate([scanned.reshape(count, rows, head_dim), back_extra], axis=1)
    back = lax.all_to_all(sent_back, axis, 0, 0)
    state = back[:, :rows, :].reshape(head_count, head_dim, head_dim)
    totals = back[:, rows:, :].reshape(count, 8 * head_dim)[:, : per_owner * fields]
    return state, totals.reshape(pair_count, fields), passenger


def local(
    tokens,
    log_decay,
    lengths,
    label_ids,
    w_query,
    w_key,
    w_value,
    norm_gain,
    label_query,
    label_weight,
):
    tok_rows = tokens.shape[1]
    model_width = tokens.shape[2]
    head_count = log_decay.shape[1]
    head_dim = model_width // head_count
    qk_scale = head_dim ** (-0.5)
    record_count = lengths.shape[1]
    label_count = label_query.shape[0]
    shard_start = lax.axis_index("ctx") * tok_rows
    local_pos = jnp.arange(tok_rows, dtype=jnp.int32)
    record = record_ids(lengths[0], shard_start + local_pos)
    before_rec = record_ids(lengths[0], jnp.reshape(shard_start - 1, (1,)))[0]
    features = tokens[0]
    queries = jnp.dot(features, w_query, preferred_element_type=jnp.float32).astype(jnp.bfloat16)
    key_rows = jnp.dot(features, w_key, preferred_element_type=jnp.float32).astype(jnp.bfloat16)
    value_rows = jnp.dot(features, w_value, preferred_element_type=jnp.float32).astype(jnp.bfloat16)
    q3 = queries.reshape(tok_rows, head_count, head_dim)
    k3 = key_rows.reshape(tok_rows, head_count, head_dim)
    v3 = value_rows.reshape(tok_rows, head_count, head_dim)
    decay_cum = jnp.cumsum(log_decay[0], axis=1)
    pair_mask = (local_pos[:, None] >= local_pos[None, :]) & (record[:, None] == record[None, :])
    linked = record == before_rec
    tail_rec = record == record[tok_rows - 1]

    last_cum = decay_cum[:, tok_rows - 1]
    k_factor = jnp.where(tail_rec[None, :], jnp.exp(last_cum[:, None] - decay_cum), 0.0)
    k_decayed = (k3.astype(jnp.float32) * k_factor.T[:, :, None]).astype(jnp.bfloat16)
    local_state = jnp.einsum("thd,the->hde", k_decayed, v3, preferred_element_type=jnp.float32)
    carry = jnp.where(linked[tok_rows - 1], jnp.exp(last_cum), 0.0)

    scores = jnp.einsum("thd,shd->hts", q3, k3, preferred_element_type=jnp.float32) * qk_scale
    decay_pair = jnp.exp(jnp.minimum(decay_cum[:, :, None] - decay_cum[:, None, :], 0.0))
    weights = jnp.where(pair_mask[None], scores * decay_pair, 0.0).astype(jnp.bfloat16)
    intra = jnp.einsum("hts,shd->thd", weights, v3, preferred_element_type=jnp.float32)

    member = record[None, :] == jnp.arange(record_count, dtype=jnp.int32)[:, None]
    kf3 = features.reshape(tok_rows, head_count, head_dim)
    lq3 = label_query.reshape(label_count, head_count, head_dim)
    lw3 = label_weight.reshape(label_count, head_count, head_dim)
    pscore = jnp.einsum("lhd,thd->hlt", lq3, kf3, preferred_element_type=jnp.float32) * qk_scale
    maxima = jnp.max(
        jnp.where(member[None, :, None, :], pscore[:, None, :, :], NEG_FILL), axis=3
    )
    maxima_tok = jnp.sum(
        jnp.where(member[None, :, None, :], maxima[:, :, :, None], 0.0), axis=1
    )
    pool_weight = jnp.exp(pscore - maxima_tok)
    mass = jnp.sum(jnp.where(member[None, :, None, :], pool_weight[:, None], 0.0), axis=3)
    label_hot = (label_ids[0][:, None] == jnp.arange(label_count, dtype=jnp.int32)[None, :]).astype(
        jnp.bfloat16
    )
    counts = jnp.dot(member.astype(jnp.bfloat16), label_hot, preferred_element_type=jnp.float32)

    stats = jnp.concatenate(
        [
            jnp.transpose(maxima, (1, 2, 0)),
            jnp.transpose(mass, (1, 2, 0)),
            counts[:, :, None],
        ],
        axis=2,
    ).reshape(record_count * label_count, 2 * head_count + 1)
    incoming, totals, intra = exclusive_state_scan(local_state, carry, stats, intra, "ctx")
    totals = totals.reshape(record_count, label_count, 2 * head_count + 1)
    top = jnp.transpose(totals[:, :, :head_count], (2, 0, 1))
    total_mass = jnp.transpose(totals[:, :, head_count:2 * head_count], (2, 0, 1))
    total_counts = totals[:, :, 2 * head_count]
    rescale = jnp.exp(maxima - top) / total_mass

    q_decayed = q3.astype(jnp.float32) * jnp.where(linked[None, :], jnp.exp(decay_cum), 0.0).T[:, :, None]
    inter = jnp.einsum(
        "thd,hde->the", q_decayed, incoming, precision=lax.Precision.HIGH,
        preferred_element_type=jnp.float32,
    )
    total_out = intra + inter * qk_scale
    centred = total_out - jnp.mean(total_out, axis=2, keepdims=True)
    variance = jnp.mean(centred * centred, axis=2, keepdims=True)
    gain3 = norm_gain.reshape(head_count, head_dim)
    normed = centred * lax.rsqrt(variance + 1e-05) * gain3[None]
    out_rows = normed.reshape(tok_rows, model_width).astype(jnp.bfloat16)

    y3 = out_rows.reshape(tok_rows, head_count, head_dim)
    label_value = jnp.einsum("lhd,thd->hlt", lw3, y3, preferred_element_type=jnp.float32)
    weighted = jnp.sum(
        jnp.where(member[None, :, None, :], (pool_weight * label_value)[:, None], 0.0), axis=3
    )
    part = jnp.sum(weighted * rescale, axis=0)
    count = lax.axis_size("ctx")
    inner = min(count, 8)
    assert count % inner == 0 and inner & (inner - 1) == 0
    part = group_sum(part, "ctx", 1, inner)
    if count > inner:
        part = group_sum(part, "ctx", inner, count // inner)
    logits = part
    target = (total_counts + 0.5) / (lengths[0].astype(jnp.float32)[:, None] + 1.0)
    rec_loss = jnp.mean(jax.nn.softplus(logits) - target * logits, axis=1)
    loss_sum = jnp.sum(rec_loss)
    for bit in butterfly_bits("dp"):
        loss_sum = loss_sum + swapped(loss_sum, "dp", bit)
    mean_loss = loss_sum / (lax.axis_size("dp") * record_count)
    return (out_rows[None], logits[None], rec_loss[None], mean_loss)


def solution(mesh):
    return jax.shard_map(
        local,
        mesh=mesh,
        in_specs=(
            P("dp", "ctx", None),
            P("dp", None, "ctx"),
            P("dp", None),
            P("dp", "ctx"),
            P(),
            P(),
            P(),
            P(),
            P(),
            P(),
        ),
        out_specs=(P("dp", "ctx", None), P("dp", None, None), P("dp", None), P()),
        check_vma=False,
    )
```

```python
import jax
import jax.numpy as jnp
from jax import lax
from jax.sharding import PartitionSpec as P

NEG_FILL = -1e30


def shifted(x, axis, by):
    count = lax.axis_size(axis)
    pairs = [(i, i + by) for i in range(count) if 0 <= i + by < count]
    return lax.ppermute(x, axis, pairs)


def swapped(x, axis, bit):
    count = lax.axis_size(axis)
    return lax.ppermute(x, axis, [(i, i ^ bit) for i in range(count)])


def group_sum(x, axis, stride, size):
    values = [x] + [swapped(x, axis, stride * d) for d in range(1, size)]
    while len(values) > 1:
        values = [values[i] + values[i + 1] for i in range(0, len(values), 2)]
    return values[0]


def butterfly_bits(axis):
    count = lax.axis_size(axis)
    assert count & (count - 1) == 0
    bits = []
    bit = 1
    while bit < count:
        bits.append(bit)
        bit *= 2
    return bits


def record_ids(length_row, positions):
    starts = jnp.cumsum(length_row) - length_row
    return jnp.sum((starts[:, None] <= positions[None, :]).astype(jnp.int32), axis=0) - 1


def exclusive_state_scan(local_state, carry, stats, passenger, axis):
    head_count, head_dim, _ = local_state.shape
    count = lax.axis_size(axis)
    rows = head_count * head_dim // count
    assert rows * count == head_count * head_dim and head_dim % rows == 0
    pair_count, fields = stats.shape
    per_owner = pair_count // count
    assert per_owner * count == pair_count and per_owner * fields < 8 * head_dim
    pad = 8 * head_dim - per_owner * fields - 1
    owner_head = (jnp.arange(count) * rows) // head_dim
    slices = local_state.reshape(count, rows, head_dim)
    extra = jnp.concatenate(
        [
            stats.reshape(count, per_owner * fields),
            carry[owner_head][:, None],
            jnp.zeros((count, pad), jnp.float32),
        ],
        axis=1,
    ).reshape(count, 8, head_dim)
    got = lax.all_to_all(jnp.concatenate([slices, extra], axis=1), axis, 0, 0)
    got, passenger = lax.optimization_barrier((got, passenger))
    got_extra = got[:, rows:, :].reshape(count, 8 * head_dim)
    factors = got_extra[:, per_owner * fields]
    part = got_extra[:, : per_owner * fields].reshape(count, per_owner, fields)
    part_top = part[:, :, :head_count]
    top = jnp.max(part_top, axis=0)
    mass = jnp.sum(part[:, :, head_count:2 * head_count] * jnp.exp(part_top - top[None]), axis=0)
    tally = jnp.sum(part[:, :, 2 * head_count:], axis=0)
    combined = jnp.concatenate([top, mass, tally], axis=1).reshape(1, per_owner * fields)
    block = jnp.arange(count)
    inside = (block[None, None, :] > block[None, :, None]) & (block[None, None, :] < block[:, None, None])
    spans = jnp.prod(jnp.where(inside, factors[None, None, :], 1.0), axis=2)
    mix = jnp.where(block[None, :] < block[:, None], spans, 0.0)
    scanned = jnp.dot(
        mix, got[:, :rows, :].reshape(count, rows * head_dim), precision=lax.Precision.HIGHEST
    )
    back_extra = jnp.broadcast_to(
        jnp.concatenate([combined, jnp.zeros((1, pad + 1), jnp.float32)], axis=1),
        (count, 8 * head_dim),
    ).reshape(count, 8, head_dim)
    sent_back = jnp.concatenate([scanned.reshape(count, rows, head_dim), back_extra], axis=1)
    back = lax.all_to_all(sent_back, axis, 0, 0)
    state = back[:, :rows, :].reshape(head_count, head_dim, head_dim)
    totals = back[:, rows:, :].reshape(count, 8 * head_dim)[:, : per_owner * fields]
    return state, totals.reshape(pair_count, fields), passenger


def local(
    tokens,
    log_decay,
    lengths,
    label_ids,
    w_query,
    w_key,
    w_value,
    norm_gain,
    label_query,
    label_weight,
):
    tok_rows = tokens.shape[1]
    model_width = tokens.shape[2]
    head_count = log_decay.shape[1]
    head_dim = model_width // head_count
    qk_scale = head_dim ** (-0.5)
    record_count = lengths.shape[1]
    label_count = label_query.shape[0]
    shard_start = lax.axis_index("ctx") * tok_rows
    local_pos = jnp.arange(tok_rows, dtype=jnp.int32)
    record = record_ids(lengths[0], shard_start + local_pos)
    before_rec = record_ids(lengths[0], jnp.reshape(shard_start - 1, (1,)))[0]
    features = tokens[0]
    queries = jnp.dot(features, w_query, preferred_element_type=jnp.float32).astype(jnp.bfloat16)
    key_rows = jnp.dot(features, w_key, preferred_element_type=jnp.float32).astype(jnp.bfloat16)
    value_rows = jnp.dot(features, w_value, preferred_element_type=jnp.float32).astype(jnp.bfloat16)
    q3 = queries.reshape(tok_rows, head_count, head_dim)
    k3 = key_rows.reshape(tok_rows, head_count, head_dim)
    v3 = value_rows.reshape(tok_rows, head_count, head_dim)
    decay_cum = jnp.cumsum(log_decay[0], axis=1)
    pair_mask = (local_pos[:, None] >= local_pos[None, :]) & (record[:, None] == record[None, :])
    linked = record == before_rec
    tail_rec = record == record[tok_rows - 1]

    last_cum = decay_cum[:, tok_rows - 1]
    k_factor = jnp.where(tail_rec[None, :], jnp.exp(last_cum[:, None] - decay_cum), 0.0)
    k_decayed = (k3.astype(jnp.float32) * k_factor.T[:, :, None]).astype(jnp.bfloat16)
    local_state = jnp.einsum("thd,the->hde", k_decayed, v3, preferred_element_type=jnp.float32)
    carry = jnp.where(linked[tok_rows - 1], jnp.exp(last_cum), 0.0)

    scores = jnp.einsum("thd,shd->hts", q3, k3, preferred_element_type=jnp.float32) * qk_scale
    decay_pair = jnp.exp(jnp.minimum(decay_cum[:, :, None] - decay_cum[:, None, :], 0.0))
    weights = jnp.where(pair_mask[None], scores * decay_pair, 0.0).astype(jnp.bfloat16)
    intra = jnp.einsum("hts,shd->thd", weights, v3, preferred_element_type=jnp.float32)

    member = record[None, :] == jnp.arange(record_count, dtype=jnp.int32)[:, None]
    kf3 = features.reshape(tok_rows, head_count, head_dim)
    lq3 = label_query.reshape(label_count, head_count, head_dim)
    lw3 = label_weight.reshape(label_count, head_count, head_dim)
    pscore = jnp.einsum("lhd,thd->hlt", lq3, kf3, preferred_element_type=jnp.float32) * qk_scale
    maxima = jnp.max(
        jnp.where(member[None, :, None, :], pscore[:, None, :, :], NEG_FILL), axis=3
    )
    maxima_tok = jnp.sum(
        jnp.where(member[None, :, None, :], maxima[:, :, :, None], 0.0), axis=1
    )
    pool_weight = jnp.exp(pscore - maxima_tok)
    mass = jnp.sum(jnp.where(member[None, :, None, :], pool_weight[:, None], 0.0), axis=3)
    label_hot = (label_ids[0][:, None] == jnp.arange(label_count, dtype=jnp.int32)[None, :]).astype(
        jnp.bfloat16
    )
    counts = jnp.dot(member.astype(jnp.bfloat16), label_hot, preferred_element_type=jnp.float32)

    stats = jnp.concatenate(
        [
            jnp.transpose(maxima, (1, 2, 0)),
            jnp.transpose(mass, (1, 2, 0)),
            counts[:, :, None],
        ],
        axis=2,
    ).reshape(record_count * label_count, 2 * head_count + 1)
    incoming, totals, intra = exclusive_state_scan(local_state, carry, stats, intra, "ctx")
    totals = totals.reshape(record_count, label_count, 2 * head_count + 1)
    top = jnp.transpose(totals[:, :, :head_count], (2, 0, 1))
    total_mass = jnp.transpose(totals[:, :, head_count:2 * head_count], (2, 0, 1))
    total_counts = totals[:, :, 2 * head_count]
    rescale = jnp.exp(maxima - top) / total_mass

    q_decayed = q3.astype(jnp.float32) * jnp.where(linked[None, :], jnp.exp(decay_cum), 0.0).T[:, :, None]
    inter = jnp.einsum(
        "thd,hde->the", q_decayed, incoming, precision=lax.Precision.HIGH,
        preferred_element_type=jnp.float32,
    )
    total_out = intra + inter * qk_scale
    centred = total_out - jnp.mean(total_out, axis=2, keepdims=True)
    variance = jnp.mean(centred * centred, axis=2, keepdims=True)
    gain3 = norm_gain.reshape(head_count, head_dim)
    normed = centred * lax.rsqrt(variance + 1e-05) * gain3[None]
    out_rows = normed.reshape(tok_rows, model_width).astype(jnp.bfloat16)

    y3 = out_rows.reshape(tok_rows, head_count, head_dim)
    label_value = jnp.einsum("lhd,thd->hlt", lw3, y3, preferred_element_type=jnp.float32)
    weighted = jnp.sum(
        jnp.where(member[None, :, None, :], (pool_weight * label_value)[:, None], 0.0), axis=3
    )
    part = jnp.sum(weighted * rescale, axis=0)
    logits = jnp.sum(lax.all_gather(part, "ctx"), axis=0)
    target = (total_counts + 0.5) / (lengths[0].astype(jnp.float32)[:, None] + 1.0)
    rec_loss = jnp.mean(jax.nn.softplus(logits) - target * logits, axis=1)
    loss_sum = jnp.sum(lax.all_gather(jnp.sum(rec_loss), "dp"))
    mean_loss = loss_sum / (lax.axis_size("dp") * record_count)
    return (out_rows[None], logits[None], rec_loss[None], mean_loss)


def solution(mesh):
    return jax.shard_map(
        local,
        mesh=mesh,
        in_specs=(
            P("dp", "ctx", None),
            P("dp", None, "ctx"),
            P("dp", None),
            P("dp", "ctx"),
            P(),
            P(),
            P(),
            P(),
            P(),
            P(),
        ),
        out_specs=(P("dp", "ctx", None), P("dp", None, None), P("dp", None), P()),
        check_vma=False,
    )
```

```python
import jax
import jax.numpy as jnp
from jax import lax
from jax.sharding import PartitionSpec as P

NEG_FILL = -1e30


def shifted(x, axis, by):
    count = lax.axis_size(axis)
    pairs = [(i, i + by) for i in range(count) if 0 <= i + by < count]
    return lax.ppermute(x, axis, pairs)


def swapped(x, axis, bit):
    count = lax.axis_size(axis)
    return lax.ppermute(x, axis, [(i, i ^ bit) for i in range(count)])


def group_sum(x, axis, stride, size):
    values = [x] + [swapped(x, axis, stride * d) for d in range(1, size)]
    while len(values) > 1:
        values = [values[i] + values[i + 1] for i in range(0, len(values), 2)]
    return values[0]


def butterfly_bits(axis):
    count = lax.axis_size(axis)
    assert count & (count - 1) == 0
    bits = []
    bit = 1
    while bit < count:
        bits.append(bit)
        bit *= 2
    return bits


def record_ids(length_row, positions):
    order = jnp.arange(length_row.shape[0])
    starts = jnp.sum(jnp.where(order[None, :] < order[:, None], length_row[None, :], 0), axis=1)
    return jnp.sum((starts[:, None] <= positions[None, :]).astype(jnp.int32), axis=0) - 1


def exclusive_state_scan(local_state, carry, stats, passenger, axis):
    head_count, head_dim, _ = local_state.shape
    count = lax.axis_size(axis)
    rows = head_count * head_dim // count
    assert rows * count == head_count * head_dim and head_dim % rows == 0
    pair_count, fields = stats.shape
    per_owner = pair_count // count
    assert per_owner * count == pair_count and per_owner * fields < 8 * head_dim
    pad = 8 * head_dim - per_owner * fields - 1
    slices = local_state.reshape(count, rows, head_dim)
    extra = jnp.concatenate(
        [
            stats.reshape(count, per_owner * fields),
            jnp.repeat(carry, count // head_count)[:, None],
            jnp.zeros((count, pad), jnp.float32),
        ],
        axis=1,
    ).reshape(count, 8, head_dim)
    got = lax.all_to_all(jnp.concatenate([slices, extra], axis=1), axis, 0, 0)
    got, passenger = lax.optimization_barrier((got, passenger))
    got_extra = got[:, rows:, :].reshape(count, 8 * head_dim)
    factors = got_extra[:, per_owner * fields]
    part = got_extra[:, : per_owner * fields].reshape(count, per_owner, fields)
    part_top = part[:, :, :head_count]
    top = jnp.max(part_top, axis=0)
    mass = jnp.sum(part[:, :, head_count:2 * head_count] * jnp.exp(part_top - top[None]), axis=0)
    tally = jnp.sum(part[:, :, 2 * head_count:], axis=0)
    combined = jnp.concatenate([top, mass, tally], axis=1).reshape(1, per_owner * fields)
    block = jnp.arange(count)
    inside = (block[None, None, :] > block[None, :, None]) & (block[None, None, :] < block[:, None, None])
    spans = jnp.prod(jnp.where(inside, factors[None, None, :], 1.0), axis=2)
    mix = jnp.where(block[None, :] < block[:, None], spans, 0.0)
    scanned = jnp.dot(
        mix, got[:, :rows, :].reshape(count, rows * head_dim), precision=lax.Precision.HIGHEST
    )
    back_extra = jnp.broadcast_to(
        jnp.concatenate([combined, jnp.zeros((1, pad + 1), jnp.float32)], axis=1),
        (count, 8 * head_dim),
    ).reshape(count, 8, head_dim)
    sent_back = jnp.concatenate([scanned.reshape(count, rows, head_dim), back_extra], axis=1)
    back = lax.all_to_all(sent_back, axis, 0, 0)
    state = back[:, :rows, :].reshape(head_count, head_dim, head_dim)
    totals = back[:, rows:, :].reshape(count, 8 * head_dim)[:, : per_owner * fields]
    return state, totals.reshape(pair_count, fields), passenger


def local(
    tokens,
    log_decay,
    lengths,
    label_ids,
    w_query,
    w_key,
    w_value,
    norm_gain,
    label_query,
    label_weight,
):
    tok_rows = tokens.shape[1]
    model_width = tokens.shape[2]
    head_count = log_decay.shape[1]
    head_dim = model_width // head_count
    qk_scale = head_dim ** (-0.5)
    record_count = lengths.shape[1]
    label_count = label_query.shape[0]
    shard_start = lax.axis_index("ctx") * tok_rows
    local_pos = jnp.arange(tok_rows, dtype=jnp.int32)
    record = record_ids(lengths[0], shard_start + local_pos)
    before_rec = record_ids(lengths[0], jnp.reshape(shard_start - 1, (1,)))[0]
    features = tokens[0]
    queries = jnp.dot(features, w_query, preferred_element_type=jnp.float32).astype(jnp.bfloat16)
    key_rows = jnp.dot(features, w_key, preferred_element_type=jnp.float32).astype(jnp.bfloat16)
    value_rows = jnp.dot(features, w_value, preferred_element_type=jnp.float32).astype(jnp.bfloat16)
    q3 = queries.reshape(tok_rows, head_count, head_dim)
    k3 = key_rows.reshape(tok_rows, head_count, head_dim)
    v3 = value_rows.reshape(tok_rows, head_count, head_dim)
    decay_cum = jnp.cumsum(log_decay[0], axis=1)
    pair_mask = (local_pos[:, None] >= local_pos[None, :]) & (record[:, None] == record[None, :])
    linked = record == before_rec
    tail_rec = record == record[tok_rows - 1]

    last_cum = decay_cum[:, tok_rows - 1]
    k_factor = jnp.where(tail_rec[None, :], jnp.exp(last_cum[:, None] - decay_cum), 0.0)
    k_decayed = (k3.astype(jnp.float32) * k_factor.T[:, :, None]).astype(jnp.bfloat16)
    local_state = jnp.einsum("thd,the->hde", k_decayed, v3, preferred_element_type=jnp.float32)
    carry = jnp.where(linked[tok_rows - 1], jnp.exp(last_cum), 0.0)

    scores = jnp.einsum("thd,shd->hts", q3, k3, preferred_element_type=jnp.float32) * qk_scale
    decay_pair = jnp.exp(jnp.minimum(decay_cum[:, :, None] - decay_cum[:, None, :], 0.0))
    weights = jnp.where(pair_mask[None], scores * decay_pair, 0.0).astype(jnp.bfloat16)
    intra = jnp.einsum("hts,shd->thd", weights, v3, preferred_element_type=jnp.float32)

    member = record[None, :] == jnp.arange(record_count, dtype=jnp.int32)[:, None]
    kf3 = features.reshape(tok_rows, head_count, head_dim)
    lq3 = label_query.reshape(label_count, head_count, head_dim)
    lw3 = label_weight.reshape(label_count, head_count, head_dim)
    pscore = jnp.einsum("lhd,thd->hlt", lq3, kf3, preferred_element_type=jnp.float32) * qk_scale
    maxima = jnp.max(
        jnp.where(member[None, :, None, :], pscore[:, None, :, :], NEG_FILL), axis=3
    )
    maxima_tok = maxima[:, record_count - 1, :, None]
    for r in range(record_count - 2, -1, -1):
        maxima_tok = jnp.where(record[None, None, :] == r, maxima[:, r, :, None], maxima_tok)
    pool_weight = jnp.exp(pscore - maxima_tok)
    mass = jnp.sum(jnp.where(member[None, :, None, :], pool_weight[:, None], 0.0), axis=3)
    label_hot = (label_ids[0][:, None] == jnp.arange(label_count, dtype=jnp.int32)[None, :]).astype(
        jnp.bfloat16
    )
    counts = jnp.dot(member.astype(jnp.bfloat16), label_hot, preferred_element_type=jnp.float32)

    stats = jnp.concatenate(
        [
            jnp.transpose(maxima, (1, 2, 0)),
            jnp.transpose(mass, (1, 2, 0)),
            counts[:, :, None],
        ],
        axis=2,
    ).reshape(record_count * label_count, 2 * head_count + 1)
    incoming, totals, intra = exclusive_state_scan(local_state, carry, stats, intra, "ctx")
    totals = totals.reshape(record_count, label_count, 2 * head_count + 1)
    top = jnp.transpose(totals[:, :, :head_count], (2, 0, 1))
    total_mass = jnp.transpose(totals[:, :, head_count:2 * head_count], (2, 0, 1))
    total_counts = totals[:, :, 2 * head_count]
    rescale = jnp.exp(maxima - top) / total_mass

    q_decayed = q3.astype(jnp.float32) * jnp.where(linked[None, :], jnp.exp(decay_cum), 0.0).T[:, :, None]
    inter = jnp.einsum(
        "thd,hde->the", q_decayed, incoming, precision=lax.Precision.HIGH,
        preferred_element_type=jnp.float32,
    )
    total_out = intra + inter * qk_scale
    centred = total_out - jnp.mean(total_out, axis=2, keepdims=True)
    variance = jnp.mean(centred * centred, axis=2, keepdims=True)
    gain3 = norm_gain.reshape(head_count, head_dim)
    normed = centred * lax.rsqrt(variance + 1e-05) * gain3[None]
    out_rows = normed.reshape(tok_rows, model_width).astype(jnp.bfloat16)

    y3 = out_rows.reshape(tok_rows, head_count, head_dim)
    label_value = jnp.einsum("lhd,thd->hlt", lw3, y3, preferred_element_type=jnp.float32)
    weighted = jnp.sum(
        jnp.where(member[None, :, None, :], (pool_weight * label_value)[:, None], 0.0), axis=3
    )
    part = jnp.sum(weighted * rescale, axis=0)
    count = lax.axis_size("ctx")
    inner = min(count, 8)
    assert count % inner == 0 and inner & (inner - 1) == 0
    part = group_sum(part, "ctx", 1, inner)
    if count > inner:
        part = group_sum(part, "ctx", inner, count // inner)
    logits = part
    target = (total_counts + 0.5) / (lengths[0].astype(jnp.float32)[:, None] + 1.0)
    rec_loss = jnp.mean(jax.nn.softplus(logits) - target * logits, axis=1)
    loss_sum = jnp.sum(rec_loss)
    for bit in butterfly_bits("dp"):
        loss_sum = loss_sum + swapped(loss_sum, "dp", bit)
    mean_loss = loss_sum / (lax.axis_size("dp") * record_count)
    return (out_rows[None], logits[None], rec_loss[None], mean_loss)


def solution(mesh):
    return jax.shard_map(
        local,
        mesh=mesh,
        in_specs=(
            P("dp", "ctx", None),
            P("dp", None, "ctx"),
            P("dp", None),
            P("dp", "ctx"),
            P(),
            P(),
            P(),
            P(),
            P(),
            P(),
        ),
        out_specs=(P("dp", "ctx", None), P("dp", None, None), P("dp", None), P()),
        check_vma=False,
    )
```

```python
import jax
import jax.numpy as jnp
from jax import lax
from jax.sharding import PartitionSpec as P

NEG_FILL = -1e30


def shifted(x, axis, by):
    count = lax.axis_size(axis)
    pairs = [(i, i + by) for i in range(count) if 0 <= i + by < count]
    return lax.ppermute(x, axis, pairs)


def swapped(x, axis, bit):
    count = lax.axis_size(axis)
    return lax.ppermute(x, axis, [(i, i ^ bit) for i in range(count)])


def group_sum(x, axis, stride, size):
    values = [x] + [swapped(x, axis, stride * d) for d in range(1, size)]
    while len(values) > 1:
        values = [values[i] + values[i + 1] for i in range(0, len(values), 2)]
    return values[0]


def butterfly_bits(axis):
    count = lax.axis_size(axis)
    assert count & (count - 1) == 0
    bits = []
    bit = 1
    while bit < count:
        bits.append(bit)
        bit *= 2
    return bits


def record_ids(length_row, positions):
    starts = jnp.cumsum(length_row) - length_row
    return jnp.sum((starts[:, None] <= positions[None, :]).astype(jnp.int32), axis=0) - 1


def exclusive_state_scan(local_state, carry, stats, passenger, axis):
    head_count, head_dim, _ = local_state.shape
    count = lax.axis_size(axis)
    rows = head_count * head_dim // count
    assert rows * count == head_count * head_dim and head_dim % rows == 0
    pair_count, fields = stats.shape
    per_owner = pair_count // count
    assert per_owner * count == pair_count and per_owner * fields < 8 * head_dim
    pad = 8 * head_dim - per_owner * fields - 1
    owner_head = (jnp.arange(count) * rows) // head_dim
    slices = local_state.reshape(count, rows, head_dim)
    extra = jnp.concatenate(
        [
            stats.reshape(count, per_owner * fields),
            carry[owner_head][:, None],
            jnp.zeros((count, pad), jnp.float32),
        ],
        axis=1,
    ).reshape(count, 8, head_dim)
    got = lax.all_to_all(jnp.concatenate([slices, extra], axis=1), axis, 0, 0)
    got, passenger = lax.optimization_barrier((got, passenger))
    got_extra = got[:, rows:, :].reshape(count, 8 * head_dim)
    factors = got_extra[:, per_owner * fields]
    part = got_extra[:, : per_owner * fields].reshape(count, per_owner, fields)
    part_top = part[:, :, :head_count]
    top = jnp.max(part_top, axis=0)
    mass = jnp.sum(part[:, :, head_count:2 * head_count] * jnp.exp(part_top - top[None]), axis=0)
    tally = jnp.sum(part[:, :, 2 * head_count:], axis=0)
    combined = jnp.concatenate([top, mass, tally], axis=1).reshape(1, per_owner * fields)
    block = jnp.arange(count)
    inside = (block[None, None, :] > block[None, :, None]) & (block[None, None, :] < block[:, None, None])
    spans = jnp.prod(jnp.where(inside, factors[None, None, :], 1.0), axis=2)
    mix = jnp.where(block[None, :] < block[:, None], spans, 0.0)
    scanned = jnp.dot(
        mix, got[:, :rows, :].reshape(count, rows * head_dim), precision=lax.Precision.HIGHEST
    )
    back_extra = jnp.broadcast_to(
        jnp.concatenate([combined, jnp.zeros((1, pad + 1), jnp.float32)], axis=1),
        (count, 8 * head_dim),
    ).reshape(count, 8, head_dim)
    sent_back = jnp.concatenate([scanned.reshape(count, rows, head_dim), back_extra], axis=1)
    back = lax.all_to_all(sent_back, axis, 0, 0)
    state = back[:, :rows, :].reshape(head_count, head_dim, head_dim)
    totals = back[:, rows:, :].reshape(count, 8 * head_dim)[:, : per_owner * fields]
    return state, totals.reshape(pair_count, fields), passenger


def local(
    tokens,
    log_decay,
    lengths,
    label_ids,
    w_query,
    w_key,
    w_value,
    norm_gain,
    label_query,
    label_weight,
):
    tok_rows = tokens.shape[1]
    model_width = tokens.shape[2]
    head_count = log_decay.shape[1]
    head_dim = model_width // head_count
    qk_scale = head_dim ** (-0.5)
    record_count = lengths.shape[1]
    label_count = label_query.shape[0]
    shard_start = lax.axis_index("ctx") * tok_rows
    local_pos = jnp.arange(tok_rows, dtype=jnp.int32)
    record = record_ids(lengths[0], shard_start + local_pos)
    before_rec = record_ids(lengths[0], jnp.reshape(shard_start - 1, (1,)))[0]
    features = tokens[0]
    queries = jnp.dot(features, w_query, preferred_element_type=jnp.float32).astype(jnp.bfloat16)
    key_rows = jnp.dot(features, w_key, preferred_element_type=jnp.float32).astype(jnp.bfloat16)
    value_rows = jnp.dot(features, w_value, preferred_element_type=jnp.float32).astype(jnp.bfloat16)
    q3 = queries.reshape(tok_rows, head_count, head_dim)
    k3 = key_rows.reshape(tok_rows, head_count, head_dim)
    v3 = value_rows.reshape(tok_rows, head_count, head_dim)
    decay_cum = jnp.cumsum(log_decay[0], axis=1)
    pair_mask = (local_pos[:, None] >= local_pos[None, :]) & (record[:, None] == record[None, :])
    linked = record == before_rec
    tail_rec = record == record[tok_rows - 1]

    last_cum = decay_cum[:, tok_rows - 1]
    k_factor = jnp.where(tail_rec[None, :], jnp.exp(last_cum[:, None] - decay_cum), 0.0)
    k_decayed = (
        key_rows.astype(jnp.float32) * jnp.repeat(k_factor.T, head_dim, axis=1)
    ).astype(jnp.bfloat16)
    full_state = lax.dot_general(
        k_decayed, value_rows, (((0,), (0,)), ((), ())), preferred_element_type=jnp.float32
    )
    local_state = jnp.stack(
        [
            full_state[h * head_dim:(h + 1) * head_dim, h * head_dim:(h + 1) * head_dim]
            for h in range(head_count)
        ]
    )
    carry = jnp.where(linked[tok_rows - 1], jnp.exp(last_cum), 0.0)

    scores = jnp.einsum("thd,shd->hts", q3, k3, preferred_element_type=jnp.float32) * qk_scale
    decay_pair = jnp.exp(jnp.minimum(decay_cum[:, :, None] - decay_cum[:, None, :], 0.0))
    weights = jnp.where(pair_mask[None], scores * decay_pair, 0.0).astype(jnp.bfloat16)
    intra = jnp.einsum("hts,shd->thd", weights, v3, preferred_element_type=jnp.float32)

    member = record[None, :] == jnp.arange(record_count, dtype=jnp.int32)[:, None]
    kf3 = features.reshape(tok_rows, head_count, head_dim)
    lq3 = label_query.reshape(label_count, head_count, head_dim)
    lw3 = label_weight.reshape(label_count, head_count, head_dim)
    pscore = jnp.einsum("lhd,thd->hlt", lq3, kf3, preferred_element_type=jnp.float32) * qk_scale
    maxima = jnp.max(
        jnp.where(member[None, :, None, :], pscore[:, None, :, :], NEG_FILL), axis=3
    )
    maxima_tok = jnp.sum(
        jnp.where(member[None, :, None, :], maxima[:, :, :, None], 0.0), axis=1
    )
    pool_weight = jnp.exp(pscore - maxima_tok)
    mass = jnp.sum(jnp.where(member[None, :, None, :], pool_weight[:, None], 0.0), axis=3)
    label_hot = (label_ids[0][:, None] == jnp.arange(label_count, dtype=jnp.int32)[None, :]).astype(
        jnp.bfloat16
    )
    counts = jnp.dot(member.astype(jnp.bfloat16), label_hot, preferred_element_type=jnp.float32)

    stats = jnp.concatenate(
        [
            jnp.transpose(maxima, (1, 2, 0)),
            jnp.transpose(mass, (1, 2, 0)),
            counts[:, :, None],
        ],
        axis=2,
    ).reshape(record_count * label_count, 2 * head_count + 1)
    incoming, totals, intra = exclusive_state_scan(local_state, carry, stats, intra, "ctx")
    totals = totals.reshape(record_count, label_count, 2 * head_count + 1)
    top = jnp.transpose(totals[:, :, :head_count], (2, 0, 1))
    total_mass = jnp.transpose(totals[:, :, head_count:2 * head_count], (2, 0, 1))
    total_counts = totals[:, :, 2 * head_count]
    rescale = jnp.exp(maxima - top) / total_mass

    q_decayed = q3.astype(jnp.float32) * jnp.where(linked[None, :], jnp.exp(decay_cum), 0.0).T[:, :, None]
    inter = jnp.einsum(
        "thd,hde->the", q_decayed, incoming, precision=lax.Precision.HIGH,
        preferred_element_type=jnp.float32,
    )
    total_out = intra + inter * qk_scale
    centred = total_out - jnp.mean(total_out, axis=2, keepdims=True)
    variance = jnp.mean(centred * centred, axis=2, keepdims=True)
    gain3 = norm_gain.reshape(head_count, head_dim)
    normed = centred * lax.rsqrt(variance + 1e-05) * gain3[None]
    out_rows = normed.reshape(tok_rows, model_width).astype(jnp.bfloat16)

    y3 = out_rows.reshape(tok_rows, head_count, head_dim)
    label_value = jnp.einsum("lhd,thd->hlt", lw3, y3, preferred_element_type=jnp.float32)
    weighted = jnp.sum(
        jnp.where(member[None, :, None, :], (pool_weight * label_value)[:, None], 0.0), axis=3
    )
    part = jnp.sum(weighted * rescale, axis=0)
    count = lax.axis_size("ctx")
    inner = min(count, 8)
    assert count % inner == 0 and inner & (inner - 1) == 0
    part = group_sum(part, "ctx", 1, inner)
    if count > inner:
        part = group_sum(part, "ctx", inner, count // inner)
    logits = part
    target = (total_counts + 0.5) / (lengths[0].astype(jnp.float32)[:, None] + 1.0)
    rec_loss = jnp.mean(jax.nn.softplus(logits) - target * logits, axis=1)
    loss_sum = jnp.sum(rec_loss)
    for bit in butterfly_bits("dp"):
        loss_sum = loss_sum + swapped(loss_sum, "dp", bit)
    mean_loss = loss_sum / (lax.axis_size("dp") * record_count)
    return (out_rows[None], logits[None], rec_loss[None], mean_loss)


def solution(mesh):
    return jax.shard_map(
        local,
        mesh=mesh,
        in_specs=(
            P("dp", "ctx", None),
            P("dp", None, "ctx"),
            P("dp", None),
            P("dp", "ctx"),
            P(),
            P(),
            P(),
            P(),
            P(),
            P(),
        ),
        out_specs=(P("dp", "ctx", None), P("dp", None, None), P("dp", None), P()),
        check_vma=False,
    )
```

```python
import jax
import jax.numpy as jnp
from jax import lax
from jax.sharding import PartitionSpec as P

NEG_FILL = -1e30


def shifted(x, axis, by):
    count = lax.axis_size(axis)
    pairs = [(i, i + by) for i in range(count) if 0 <= i + by < count]
    return lax.ppermute(x, axis, pairs)


def swapped(x, axis, bit):
    count = lax.axis_size(axis)
    return lax.ppermute(x, axis, [(i, i ^ bit) for i in range(count)])


def group_sum(x, axis, stride, size):
    values = [x] + [swapped(x, axis, stride * d) for d in range(1, size)]
    while len(values) > 1:
        values = [values[i] + values[i + 1] for i in range(0, len(values), 2)]
    return values[0]


def butterfly_bits(axis):
    count = lax.axis_size(axis)
    assert count & (count - 1) == 0
    bits = []
    bit = 1
    while bit < count:
        bits.append(bit)
        bit *= 2
    return bits


def record_ids(length_row, positions):
    order = jnp.arange(length_row.shape[0])
    starts = jnp.sum(jnp.where(order[None, :] < order[:, None], length_row[None, :], 0), axis=1)
    return jnp.sum((starts[:, None] <= positions[None, :]).astype(jnp.int32), axis=0) - 1


def exclusive_state_scan(local_state, carry, stats, passenger, axis):
    head_count, head_dim, _ = local_state.shape
    count = lax.axis_size(axis)
    rows = head_count * head_dim // count
    assert rows * count == head_count * head_dim and head_dim % rows == 0
    pair_count, fields = stats.shape
    per_owner = pair_count // count
    assert per_owner * count == pair_count and per_owner * fields < 8 * head_dim
    pad = 8 * head_dim - per_owner * fields - 1
    slices = local_state.reshape(count, rows, head_dim)
    extra = jnp.concatenate(
        [
            stats.reshape(count, per_owner * fields),
            jnp.repeat(carry, count // head_count)[:, None],
            jnp.zeros((count, pad), jnp.float32),
        ],
        axis=1,
    ).reshape(count, 8, head_dim)
    got = lax.all_to_all(jnp.concatenate([slices, extra], axis=1), axis, 0, 0)
    got, passenger = lax.optimization_barrier((got, passenger))
    got_extra = got[:, rows:, :].reshape(count, 8 * head_dim)
    factors = got_extra[:, per_owner * fields]
    part = got_extra[:, : per_owner * fields].reshape(count, per_owner, fields)
    part_top = part[:, :, :head_count]
    top = jnp.max(part_top, axis=0)
    mass = jnp.sum(part[:, :, head_count:2 * head_count] * jnp.exp(part_top - top[None]), axis=0)
    tally = jnp.sum(part[:, :, 2 * head_count:], axis=0)
    combined = jnp.concatenate([top, mass, tally], axis=1).reshape(1, per_owner * fields)
    block = jnp.arange(count)
    inside = (block[None, None, :] > block[None, :, None]) & (block[None, None, :] < block[:, None, None])
    spans = jnp.prod(jnp.where(inside, factors[None, None, :], 1.0), axis=2)
    mix = jnp.where(block[None, :] < block[:, None], spans, 0.0)
    scanned = jnp.dot(
        mix, got[:, :rows, :].reshape(count, rows * head_dim), precision=lax.Precision.HIGHEST
    )
    back_extra = jnp.broadcast_to(
        jnp.concatenate([combined, jnp.zeros((1, pad + 1), jnp.float32)], axis=1),
        (count, 8 * head_dim),
    ).reshape(count, 8, head_dim)
    sent_back = jnp.concatenate([scanned.reshape(count, rows, head_dim), back_extra], axis=1)
    back = lax.all_to_all(sent_back, axis, 0, 0)
    state = back[:, :rows, :].reshape(head_count, head_dim, head_dim)
    totals = back[:, rows:, :].reshape(count, 8 * head_dim)[:, : per_owner * fields]
    return state, totals.reshape(pair_count, fields), passenger


def local(
    tokens,
    log_decay,
    lengths,
    label_ids,
    w_query,
    w_key,
    w_value,
    norm_gain,
    label_query,
    label_weight,
):
    tok_rows = tokens.shape[1]
    model_width = tokens.shape[2]
    head_count = log_decay.shape[1]
    head_dim = model_width // head_count
    qk_scale = head_dim ** (-0.5)
    record_count = lengths.shape[1]
    label_count = label_query.shape[0]
    shard_start = lax.axis_index("ctx") * tok_rows
    local_pos = jnp.arange(tok_rows, dtype=jnp.int32)
    record = record_ids(lengths[0], shard_start + local_pos)
    before_rec = record_ids(lengths[0], jnp.reshape(shard_start - 1, (1,)))[0]
    features = tokens[0]
    queries = jnp.dot(features, w_query, preferred_element_type=jnp.float32).astype(jnp.bfloat16)
    key_rows = jnp.dot(features, w_key, preferred_element_type=jnp.float32).astype(jnp.bfloat16)
    value_rows = jnp.dot(features, w_value, preferred_element_type=jnp.float32).astype(jnp.bfloat16)
    q3 = queries.reshape(tok_rows, head_count, head_dim)
    k3 = key_rows.reshape(tok_rows, head_count, head_dim)
    v3 = value_rows.reshape(tok_rows, head_count, head_dim)
    upper = (local_pos[:, None] <= local_pos[None, :]).astype(jnp.float32)
    decay_cum = jnp.dot(log_decay[0], upper, precision=lax.Precision.HIGHEST)
    pair_mask = (local_pos[:, None] >= local_pos[None, :]) & (record[:, None] == record[None, :])
    linked = record == before_rec
    tail_rec = record == record[tok_rows - 1]

    last_cum = decay_cum[:, tok_rows - 1]
    k_factor = jnp.where(tail_rec[None, :], jnp.exp(last_cum[:, None] - decay_cum), 0.0)
    k_decayed = (
        key_rows.astype(jnp.float32) * jnp.repeat(k_factor.T, head_dim, axis=1)
    ).astype(jnp.bfloat16)
    full_state = lax.dot_general(
        k_decayed, value_rows, (((0,), (0,)), ((), ())), preferred_element_type=jnp.float32
    )
    local_state = jnp.stack(
        [
            full_state[h * head_dim:(h + 1) * head_dim, h * head_dim:(h + 1) * head_dim]
            for h in range(head_count)
        ]
    )
    carry = jnp.where(linked[tok_rows - 1], jnp.exp(last_cum), 0.0)

    scores = jnp.einsum("thd,shd->hts", q3, k3, preferred_element_type=jnp.float32) * qk_scale
    decay_pair = jnp.exp(jnp.minimum(decay_cum[:, :, None] - decay_cum[:, None, :], 0.0))
    weights = jnp.where(pair_mask[None], scores * decay_pair, 0.0).astype(jnp.bfloat16)
    intra = jnp.einsum("hts,shd->thd", weights, v3, preferred_element_type=jnp.float32)

    member = record[None, :] == jnp.arange(record_count, dtype=jnp.int32)[:, None]
    kf3 = features.reshape(tok_rows, head_count, head_dim)
    lq3 = label_query.reshape(label_count, head_count, head_dim)
    lw3 = label_weight.reshape(label_count, head_count, head_dim)
    pscore = jnp.einsum("lhd,thd->hlt", lq3, kf3, preferred_element_type=jnp.float32) * qk_scale
    maxima = jnp.max(
        jnp.where(member[None, :, None, :], pscore[:, None, :, :], NEG_FILL), axis=3
    )
    maxima_tok = jnp.sum(
        jnp.where(member[None, :, None, :], maxima[:, :, :, None], 0.0), axis=1
    )
    pool_weight = jnp.exp(pscore - maxima_tok)
    mass = jnp.sum(jnp.where(member[None, :, None, :], pool_weight[:, None], 0.0), axis=3)
    label_hot = (label_ids[0][:, None] == jnp.arange(label_count, dtype=jnp.int32)[None, :]).astype(
        jnp.bfloat16
    )
    counts = jnp.dot(member.astype(jnp.bfloat16), label_hot, preferred_element_type=jnp.float32)

    stats = jnp.concatenate(
        [
            jnp.transpose(maxima, (1, 2, 0)),
            jnp.transpose(mass, (1, 2, 0)),
            counts[:, :, None],
        ],
        axis=2,
    ).reshape(record_count * label_count, 2 * head_count + 1)
    incoming, totals, intra = exclusive_state_scan(local_state, carry, stats, intra, "ctx")
    totals = totals.reshape(record_count, label_count, 2 * head_count + 1)
    top = jnp.transpose(totals[:, :, :head_count], (2, 0, 1))
    total_mass = jnp.transpose(totals[:, :, head_count:2 * head_count], (2, 0, 1))
    total_counts = totals[:, :, 2 * head_count]
    rescale = jnp.exp(maxima - top) / total_mass

    q_decayed = q3.astype(jnp.float32) * jnp.where(linked[None, :], jnp.exp(decay_cum), 0.0).T[:, :, None]
    inter = jnp.einsum(
        "thd,hde->the", q_decayed, incoming, precision=lax.Precision.HIGH,
        preferred_element_type=jnp.float32,
    )
    total_out = intra + inter * qk_scale
    centred = total_out - jnp.mean(total_out, axis=2, keepdims=True)
    variance = jnp.mean(centred * centred, axis=2, keepdims=True)
    gain3 = norm_gain.reshape(head_count, head_dim)
    normed = centred * lax.rsqrt(variance + 1e-05) * gain3[None]
    out_rows = normed.reshape(tok_rows, model_width).astype(jnp.bfloat16)

    y3 = out_rows.reshape(tok_rows, head_count, head_dim)
    label_value = jnp.einsum("lhd,thd->hlt", lw3, y3, preferred_element_type=jnp.float32)
    weighted = jnp.sum(
        jnp.where(member[None, :, None, :], (pool_weight * label_value)[:, None], 0.0), axis=3
    )
    part = jnp.sum(weighted * rescale, axis=0)
    count = lax.axis_size("ctx")
    inner = min(count, 8)
    assert count % inner == 0 and inner & (inner - 1) == 0
    part = group_sum(part, "ctx", 1, inner)
    if count > inner:
        part = group_sum(part, "ctx", inner, count // inner)
    logits = part
    target = (total_counts + 0.5) / (lengths[0].astype(jnp.float32)[:, None] + 1.0)
    rec_loss = jnp.mean(jax.nn.softplus(logits) - target * logits, axis=1)
    loss_sum = jnp.sum(rec_loss)
    for bit in butterfly_bits("dp"):
        loss_sum = loss_sum + swapped(loss_sum, "dp", bit)
    mean_loss = loss_sum / (lax.axis_size("dp") * record_count)
    return (out_rows[None], logits[None], rec_loss[None], mean_loss)


def solution(mesh):
    return jax.shard_map(
        local,
        mesh=mesh,
        in_specs=(
            P("dp", "ctx", None),
            P("dp", None, "ctx"),
            P("dp", None),
            P("dp", "ctx"),
            P(),
            P(),
            P(),
            P(),
            P(),
            P(),
        ),
        out_specs=(P("dp", "ctx", None), P("dp", None, None), P("dp", None), P()),
        check_vma=False,
    )
```

```python
import jax
import jax.numpy as jnp
from jax import lax
from jax.sharding import PartitionSpec as P

NEG_FILL = -1e30


def shifted(x, axis, by):
    count = lax.axis_size(axis)
    pairs = [(i, i + by) for i in range(count) if 0 <= i + by < count]
    return lax.ppermute(x, axis, pairs)


def swapped(x, axis, bit):
    count = lax.axis_size(axis)
    return lax.ppermute(x, axis, [(i, i ^ bit) for i in range(count)])


def group_sum(x, axis, stride, size):
    values = [x] + [swapped(x, axis, stride * d) for d in range(1, size)]
    while len(values) > 1:
        values = [values[i] + values[i + 1] for i in range(0, len(values), 2)]
    return values[0]


def butterfly_bits(axis):
    count = lax.axis_size(axis)
    assert count & (count - 1) == 0
    bits = []
    bit = 1
    while bit < count:
        bits.append(bit)
        bit *= 2
    return bits


def record_ids(length_row, positions):
    order = jnp.arange(length_row.shape[0])
    starts = jnp.sum(jnp.where(order[None, :] < order[:, None], length_row[None, :], 0), axis=1)
    return jnp.sum((starts[:, None] <= positions[None, :]).astype(jnp.int32), axis=0) - 1


def exclusive_state_scan(local_state, carry, stats, passenger, axis):
    head_count, head_dim, _ = local_state.shape
    count = lax.axis_size(axis)
    rows = head_count * head_dim // count
    assert rows * count == head_count * head_dim and head_dim % rows == 0
    pair_count, fields = stats.shape
    per_owner = pair_count // count
    assert per_owner * count == pair_count and per_owner * fields < 8 * head_dim
    pad = 8 * head_dim - per_owner * fields - 1
    slices = local_state.reshape(count, rows, head_dim)
    extra = jnp.concatenate(
        [
            stats.reshape(count, per_owner * fields),
            jnp.repeat(carry, count // head_count)[:, None],
            jnp.zeros((count, pad), jnp.float32),
        ],
        axis=1,
    ).reshape(count, 8, head_dim)
    got = lax.all_to_all(jnp.concatenate([slices, extra], axis=1), axis, 0, 0)
    got, passenger = lax.optimization_barrier((got, passenger))
    got_extra = got[:, rows:, :].reshape(count, 8 * head_dim)
    factors = got_extra[:, per_owner * fields]
    part = got_extra[:, : per_owner * fields].reshape(count, per_owner, fields)
    part_top = part[:, :, :head_count]
    top = jnp.max(part_top, axis=0)
    mass = jnp.sum(part[:, :, head_count:2 * head_count] * jnp.exp(part_top - top[None]), axis=0)
    tally = jnp.sum(part[:, :, 2 * head_count:], axis=0)
    combined = jnp.concatenate([top, mass, tally], axis=1).reshape(1, per_owner * fields)
    block = jnp.arange(count)
    inside = (block[None, None, :] > block[None, :, None]) & (block[None, None, :] < block[:, None, None])
    spans = jnp.prod(jnp.where(inside, factors[None, None, :], 1.0), axis=2)
    mix = jnp.where(block[None, :] < block[:, None], spans, 0.0)
    scanned = jnp.dot(
        mix, got[:, :rows, :].reshape(count, rows * head_dim), precision=lax.Precision.HIGHEST
    )
    back_extra = jnp.broadcast_to(
        jnp.concatenate([combined, jnp.zeros((1, pad + 1), jnp.float32)], axis=1),
        (count, 8 * head_dim),
    ).reshape(count, 8, head_dim)
    sent_back = jnp.concatenate([scanned.reshape(count, rows, head_dim), back_extra], axis=1)
    back = lax.all_to_all(sent_back, axis, 0, 0)
    state = back[:, :rows, :].reshape(head_count, head_dim, head_dim)
    totals = back[:, rows:, :].reshape(count, 8 * head_dim)[:, : per_owner * fields]
    return state, totals.reshape(pair_count, fields), passenger


def local(
    tokens,
    log_decay,
    lengths,
    label_ids,
    w_query,
    w_key,
    w_value,
    norm_gain,
    label_query,
    label_weight,
):
    tok_rows = tokens.shape[1]
    model_width = tokens.shape[2]
    head_count = log_decay.shape[1]
    head_dim = model_width // head_count
    qk_scale = head_dim ** (-0.5)
    record_count = lengths.shape[1]
    label_count = label_query.shape[0]
    shard_start = lax.axis_index("ctx") * tok_rows
    local_pos = jnp.arange(tok_rows, dtype=jnp.int32)
    record = record_ids(lengths[0], shard_start + local_pos)
    before_rec = record_ids(lengths[0], jnp.reshape(shard_start - 1, (1,)))[0]
    features = tokens[0]
    queries = jnp.dot(features, w_query, preferred_element_type=jnp.float32).astype(jnp.bfloat16)
    key_rows = jnp.dot(features, w_key, preferred_element_type=jnp.float32).astype(jnp.bfloat16)
    value_rows = jnp.dot(features, w_value, preferred_element_type=jnp.float32).astype(jnp.bfloat16)
    q3 = queries.reshape(tok_rows, head_count, head_dim)
    k3 = key_rows.reshape(tok_rows, head_count, head_dim)
    v3 = value_rows.reshape(tok_rows, head_count, head_dim)
    upper = (local_pos[:, None] <= local_pos[None, :]).astype(jnp.float32)
    decay_cum = jnp.dot(log_decay[0], upper, precision=lax.Precision.HIGHEST)
    pair_mask = (local_pos[:, None] >= local_pos[None, :]) & (record[:, None] == record[None, :])
    linked = record == before_rec
    tail_rec = record == record[tok_rows - 1]

    last_cum = decay_cum[:, tok_rows - 1]
    k_factor = jnp.where(tail_rec[None, :], jnp.exp(last_cum[:, None] - decay_cum), 0.0)
    k_decayed = (
        key_rows.astype(jnp.float32) * jnp.repeat(k_factor.T, head_dim, axis=1)
    ).astype(jnp.bfloat16)
    full_state = lax.dot_general(
        k_decayed, value_rows, (((0,), (0,)), ((), ())), preferred_element_type=jnp.float32
    )
    local_state = jnp.stack(
        [
            full_state[h * head_dim:(h + 1) * head_dim, h * head_dim:(h + 1) * head_dim]
            for h in range(head_count)
        ]
    )
    carry = jnp.where(linked[tok_rows - 1], jnp.exp(last_cum), 0.0)

    scores = jnp.einsum("thd,shd->hts", q3, k3, preferred_element_type=jnp.float32) * qk_scale
    decay_pair = jnp.exp(jnp.minimum(decay_cum[:, :, None] - decay_cum[:, None, :], 0.0))
    weights = jnp.where(pair_mask[None], scores * decay_pair, 0.0).astype(jnp.bfloat16)
    intra = jnp.einsum("hts,shd->thd", weights, v3, preferred_element_type=jnp.float32)

    member = record[None, :] == jnp.arange(record_count, dtype=jnp.int32)[:, None]
    kf3 = features.reshape(tok_rows, head_count, head_dim)
    lq3 = label_query.reshape(label_count, head_count, head_dim)
    lw3 = label_weight.reshape(label_count, head_count, head_dim)
    pscore = jnp.einsum("lhd,thd->hlt", lq3, kf3, preferred_element_type=jnp.float32) * qk_scale
    maxima = jnp.max(
        jnp.where(member[None, :, None, :], pscore[:, None, :, :], NEG_FILL), axis=3
    )
    maxima_tok = jnp.sum(
        jnp.where(member[None, :, None, :], maxima[:, :, :, None], 0.0), axis=1
    )
    pool_weight = jnp.exp(pscore - maxima_tok)
    mass = jnp.sum(jnp.where(member[None, :, None, :], pool_weight[:, None], 0.0), axis=3)
    label_hot = (label_ids[0][:, None] == jnp.arange(label_count, dtype=jnp.int32)[None, :]).astype(
        jnp.bfloat16
    )
    counts = jnp.dot(member.astype(jnp.bfloat16), label_hot, preferred_element_type=jnp.float32)

    stats = jnp.concatenate(
        [
            jnp.transpose(maxima, (1, 2, 0)),
            jnp.transpose(mass, (1, 2, 0)),
            counts[:, :, None],
        ],
        axis=2,
    ).reshape(record_count * label_count, 2 * head_count + 1)
    incoming, totals, intra = exclusive_state_scan(local_state, carry, stats, intra, "ctx")
    totals = totals.reshape(record_count, label_count, 2 * head_count + 1)
    top = jnp.transpose(totals[:, :, :head_count], (2, 0, 1))
    total_mass = jnp.transpose(totals[:, :, head_count:2 * head_count], (2, 0, 1))
    total_counts = totals[:, :, 2 * head_count]
    rescale = jnp.exp(maxima - top) / total_mass

    q_decayed = q3.astype(jnp.float32) * jnp.where(linked[None, :], jnp.exp(decay_cum), 0.0).T[:, :, None]
    inter = jnp.einsum(
        "thd,hde->the", q_decayed, incoming, precision=lax.Precision.HIGH,
        preferred_element_type=jnp.float32,
    )
    total_out = intra + inter * qk_scale
    centred = total_out - jnp.mean(total_out, axis=2, keepdims=True)
    variance = jnp.mean(centred * centred, axis=2, keepdims=True)
    gain3 = norm_gain.reshape(head_count, head_dim)
    normed = centred * lax.rsqrt(variance + 1e-05) * gain3[None]
    out_rows = normed.reshape(tok_rows, model_width).astype(jnp.bfloat16)

    y3 = out_rows.reshape(tok_rows, head_count, head_dim)
    label_value = jnp.einsum("lhd,thd->hlt", lw3, y3, preferred_element_type=jnp.float32)
    late_tok = maxima[:, record_count - 1, :, None]
    for r in range(record_count - 2, -1, -1):
        late_tok = jnp.where(record[None, None, :] == r, maxima[:, r, :, None], late_tok)
    late_weight = jnp.exp(pscore - late_tok)
    weighted = jnp.sum(
        jnp.where(member[None, :, None, :], (late_weight * label_value)[:, None], 0.0), axis=3
    )
    part = jnp.sum(weighted * rescale, axis=0)
    count = lax.axis_size("ctx")
    inner = min(count, 8)
    assert count % inner == 0 and inner & (inner - 1) == 0
    part = group_sum(part, "ctx", 1, inner)
    if count > inner:
        part = group_sum(part, "ctx", inner, count // inner)
    logits = part
    target = (total_counts + 0.5) / (lengths[0].astype(jnp.float32)[:, None] + 1.0)
    rec_loss = jnp.mean(jax.nn.softplus(logits) - target * logits, axis=1)
    loss_sum = jnp.sum(rec_loss)
    for bit in butterfly_bits("dp"):
        loss_sum = loss_sum + swapped(loss_sum, "dp", bit)
    mean_loss = loss_sum / (lax.axis_size("dp") * record_count)
    return (out_rows[None], logits[None], rec_loss[None], mean_loss)


def solution(mesh):
    return jax.shard_map(
        local,
        mesh=mesh,
        in_specs=(
            P("dp", "ctx", None),
            P("dp", None, "ctx"),
            P("dp", None),
            P("dp", "ctx"),
            P(),
            P(),
            P(),
            P(),
            P(),
            P(),
        ),
        out_specs=(P("dp", "ctx", None), P("dp", None, None), P("dp", None), P()),
        check_vma=False,
    )
```

```python
import jax
import jax.numpy as jnp
from jax import lax
from jax.sharding import PartitionSpec as P

NEG_FILL = -1e30


def shifted(x, axis, by):
    count = lax.axis_size(axis)
    pairs = [(i, i + by) for i in range(count) if 0 <= i + by < count]
    return lax.ppermute(x, axis, pairs)


def swapped(x, axis, bit):
    count = lax.axis_size(axis)
    return lax.ppermute(x, axis, [(i, i ^ bit) for i in range(count)])


def group_sum(x, axis, stride, size):
    values = [x] + [swapped(x, axis, stride * d) for d in range(1, size)]
    while len(values) > 1:
        values = [values[i] + values[i + 1] for i in range(0, len(values), 2)]
    return values[0]


def butterfly_bits(axis):
    count = lax.axis_size(axis)
    assert count & (count - 1) == 0
    bits = []
    bit = 1
    while bit < count:
        bits.append(bit)
        bit *= 2
    return bits


def record_ids(length_row, positions):
    order = jnp.arange(length_row.shape[0])
    starts = jnp.sum(jnp.where(order[None, :] < order[:, None], length_row[None, :], 0), axis=1)
    return jnp.sum((starts[:, None] <= positions[None, :]).astype(jnp.int32), axis=0) - 1


def exclusive_state_scan(local_state, carry, stats, passenger, axis):
    head_count, head_dim, _ = local_state.shape
    count = lax.axis_size(axis)
    rows = head_count * head_dim // count
    assert rows * count == head_count * head_dim and head_dim % rows == 0
    pair_count, fields = stats.shape
    per_owner = pair_count // count
    assert per_owner * count == pair_count and per_owner * fields < 8 * head_dim
    pad = 8 * head_dim - per_owner * fields - 1
    slices = local_state.reshape(count, rows, head_dim)
    extra = jnp.concatenate(
        [
            stats.reshape(count, per_owner * fields),
            jnp.repeat(carry, count // head_count)[:, None],
            jnp.zeros((count, pad), jnp.float32),
        ],
        axis=1,
    ).reshape(count, 8, head_dim)
    got = lax.all_to_all(jnp.concatenate([slices, extra], axis=1), axis, 0, 0)
    got, passenger = lax.optimization_barrier((got, passenger))
    got_extra = got[:, rows:, :].reshape(count, 8 * head_dim)
    factors = got_extra[:, per_owner * fields]
    part = got_extra[:, : per_owner * fields].reshape(count, per_owner, fields)
    part_top = part[:, :, :head_count]
    top = jnp.max(part_top, axis=0)
    mass = jnp.sum(part[:, :, head_count:2 * head_count] * jnp.exp(part_top - top[None]), axis=0)
    tally = jnp.sum(part[:, :, 2 * head_count:], axis=0)
    combined = jnp.concatenate([top, mass, tally], axis=1).reshape(1, per_owner * fields)
    block = jnp.arange(count)
    inside = (block[None, None, :] > block[None, :, None]) & (block[None, None, :] < block[:, None, None])
    spans = jnp.prod(jnp.where(inside, factors[None, None, :], 1.0), axis=2)
    mix = jnp.where(block[None, :] < block[:, None], spans, 0.0)
    scanned = jnp.dot(
        mix, got[:, :rows, :].reshape(count, rows * head_dim), precision=lax.Precision.HIGHEST
    )
    back_extra = jnp.broadcast_to(
        jnp.concatenate([combined, jnp.zeros((1, pad + 1), jnp.float32)], axis=1),
        (count, 8 * head_dim),
    ).reshape(count, 8, head_dim)
    sent_back = jnp.concatenate([scanned.reshape(count, rows, head_dim), back_extra], axis=1)
    back = lax.all_to_all(sent_back, axis, 0, 0)
    state = back[:, :rows, :].reshape(head_count, head_dim, head_dim)
    totals = back[:, rows:, :].reshape(count, 8 * head_dim)[:, : per_owner * fields]
    return state, totals.reshape(pair_count, fields), passenger


def local(
    tokens,
    log_decay,
    lengths,
    label_ids,
    w_query,
    w_key,
    w_value,
    norm_gain,
    label_query,
    label_weight,
):
    tok_rows = tokens.shape[1]
    model_width = tokens.shape[2]
    head_count = log_decay.shape[1]
    head_dim = model_width // head_count
    qk_scale = head_dim ** (-0.5)
    record_count = lengths.shape[1]
    label_count = label_query.shape[0]
    shard_start = lax.axis_index("ctx") * tok_rows
    local_pos = jnp.arange(tok_rows, dtype=jnp.int32)
    record = record_ids(lengths[0], shard_start + local_pos)
    before_rec = record_ids(lengths[0], jnp.reshape(shard_start - 1, (1,)))[0]
    features = tokens[0]
    queries = jnp.dot(features, w_query, preferred_element_type=jnp.float32).astype(jnp.bfloat16)
    key_rows = jnp.dot(features, w_key, preferred_element_type=jnp.float32).astype(jnp.bfloat16)
    value_rows = jnp.dot(features, w_value, preferred_element_type=jnp.float32).astype(jnp.bfloat16)
    q3 = queries.reshape(tok_rows, head_count, head_dim)
    k3 = key_rows.reshape(tok_rows, head_count, head_dim)
    v3 = value_rows.reshape(tok_rows, head_count, head_dim)
    upper = (local_pos[:, None] <= local_pos[None, :]).astype(jnp.float32)
    decay_cum = jnp.dot(log_decay[0], upper, precision=lax.Precision.HIGHEST)
    pair_mask = (local_pos[:, None] >= local_pos[None, :]) & (record[:, None] == record[None, :])
    linked = record == before_rec
    tail_rec = record == record[tok_rows - 1]

    last_cum = decay_cum[:, tok_rows - 1]
    k_factor = jnp.where(tail_rec[None, :], jnp.exp(last_cum[:, None] - decay_cum), 0.0)
    k_decayed = (
        key_rows.astype(jnp.float32) * jnp.repeat(k_factor.T, head_dim, axis=1)
    ).astype(jnp.bfloat16)
    full_state = lax.dot_general(
        k_decayed, value_rows, (((0,), (0,)), ((), ())), preferred_element_type=jnp.float32
    )
    local_state = jnp.stack(
        [
            full_state[h * head_dim:(h + 1) * head_dim, h * head_dim:(h + 1) * head_dim]
            for h in range(head_count)
        ]
    )
    carry = jnp.where(linked[tok_rows - 1], jnp.exp(last_cum), 0.0)

    scores = jnp.einsum("thd,shd->hts", q3, k3, preferred_element_type=jnp.float32) * qk_scale
    decay_pair = jnp.exp(jnp.minimum(decay_cum[:, :, None] - decay_cum[:, None, :], 0.0))
    weights = jnp.where(pair_mask[None], scores * decay_pair, 0.0).astype(jnp.bfloat16)
    intra = jnp.einsum("hts,shd->thd", weights, v3, preferred_element_type=jnp.float32)

    member = record[None, :] == jnp.arange(record_count, dtype=jnp.int32)[:, None]
    kf3 = features.reshape(tok_rows, head_count, head_dim)
    lq3 = label_query.reshape(label_count, head_count, head_dim)
    lw3 = label_weight.reshape(label_count, head_count, head_dim)
    pscore = jnp.einsum("lhd,thd->hlt", lq3, kf3, preferred_element_type=jnp.float32) * qk_scale
    maxima = jnp.max(
        jnp.where(member[None, :, None, :], pscore[:, None, :, :], NEG_FILL), axis=3
    )
    maxima_tok = jnp.sum(
        jnp.where(member[None, :, None, :], maxima[:, :, :, None], 0.0), axis=1
    )
    pool_weight = jnp.exp(pscore - maxima_tok)
    mass = jnp.sum(jnp.where(member[None, :, None, :], pool_weight[:, None], 0.0), axis=3)
    label_hot = (label_ids[0][:, None] == jnp.arange(label_count, dtype=jnp.int32)[None, :]).astype(
        jnp.bfloat16
    )
    counts = jnp.dot(member.astype(jnp.bfloat16), label_hot, preferred_element_type=jnp.float32)

    stats = jnp.concatenate(
        [
            jnp.transpose(maxima, (1, 2, 0)),
            jnp.transpose(mass, (1, 2, 0)),
            counts[:, :, None],
        ],
        axis=2,
    ).reshape(record_count * label_count, 2 * head_count + 1)
    incoming, totals, intra = exclusive_state_scan(local_state, carry, stats, intra, "ctx")
    totals = totals.reshape(record_count, label_count, 2 * head_count + 1)
    top = jnp.transpose(totals[:, :, :head_count], (2, 0, 1))
    total_mass = jnp.transpose(totals[:, :, head_count:2 * head_count], (2, 0, 1))
    total_counts = totals[:, :, 2 * head_count]
    rescale = jnp.exp(maxima - top) / total_mass

    q_decayed = q3.astype(jnp.float32) * jnp.where(linked[None, :], jnp.exp(decay_cum), 0.0).T[:, :, None]
    inter = jnp.einsum(
        "thd,hde->the", q_decayed, incoming, precision=lax.Precision.HIGH,
        preferred_element_type=jnp.float32,
    )
    total_out = intra + inter * qk_scale
    centred = total_out - jnp.mean(total_out, axis=2, keepdims=True)
    variance = jnp.mean(centred * centred, axis=2, keepdims=True)
    gain3 = norm_gain.reshape(head_count, head_dim)
    normed = centred * lax.rsqrt(variance + 1e-05) * gain3[None]
    out_rows = normed.reshape(tok_rows, model_width).astype(jnp.bfloat16)

    y3 = out_rows.reshape(tok_rows, head_count, head_dim)
    label_value = jnp.einsum("lhd,thd->hlt", lw3, y3, preferred_element_type=jnp.float32)
    weighted = jnp.sum(
        jnp.where(member[None, :, None, :], (pool_weight * label_value)[:, None], 0.0), axis=3
    )
    part = jnp.sum(weighted * rescale, axis=0)
    count = lax.axis_size("ctx")
    assert count & (count - 1) == 0
    stride = 1
    for size in (4, 2, 4):
        size = min(size, count // stride)
        if size > 1:
            part = group_sum(part, "ctx", stride, size)
            stride *= size
    assert stride == count
    logits = part
    target = (total_counts + 0.5) / (lengths[0].astype(jnp.float32)[:, None] + 1.0)
    rec_loss = jnp.mean(jax.nn.softplus(logits) - target * logits, axis=1)
    loss_sum = jnp.sum(rec_loss)
    for bit in butterfly_bits("dp"):
        loss_sum = loss_sum + swapped(loss_sum, "dp", bit)
    mean_loss = loss_sum / (lax.axis_size("dp") * record_count)
    return (out_rows[None], logits[None], rec_loss[None], mean_loss)


def solution(mesh):
    return jax.shard_map(
        local,
        mesh=mesh,
        in_specs=(
            P("dp", "ctx", None),
            P("dp", None, "ctx"),
            P("dp", None),
            P("dp", "ctx"),
            P(),
            P(),
            P(),
            P(),
            P(),
            P(),
        ),
        out_specs=(P("dp", "ctx", None), P("dp", None, None), P("dp", None), P()),
        check_vma=False,
    )
```

```python
import jax
import jax.numpy as jnp
from jax import lax
from jax.sharding import PartitionSpec as P

NEG_FILL = -1e30


def shifted(x, axis, by):
    count = lax.axis_size(axis)
    pairs = [(i, i + by) for i in range(count) if 0 <= i + by < count]
    return lax.ppermute(x, axis, pairs)


def swapped(x, axis, bit):
    count = lax.axis_size(axis)
    return lax.ppermute(x, axis, [(i, i ^ bit) for i in range(count)])


def group_sum(x, axis, stride, size):
    values = [x] + [swapped(x, axis, stride * d) for d in range(1, size)]
    while len(values) > 1:
        values = [values[i] + values[i + 1] for i in range(0, len(values), 2)]
    return values[0]


def butterfly_bits(axis):
    count = lax.axis_size(axis)
    assert count & (count - 1) == 0
    bits = []
    bit = 1
    while bit < count:
        bits.append(bit)
        bit *= 2
    return bits


def record_ids(length_row, positions):
    order = jnp.arange(length_row.shape[0])
    starts = jnp.sum(jnp.where(order[None, :] < order[:, None], length_row[None, :], 0), axis=1)
    return jnp.sum((starts[:, None] <= positions[None, :]).astype(jnp.int32), axis=0) - 1


def exclusive_state_scan(local_state, carry, stats, passenger, axis):
    head_count, head_dim, _ = local_state.shape
    count = lax.axis_size(axis)
    rows = head_count * head_dim // count
    assert rows * count == head_count * head_dim and head_dim % rows == 0
    pair_count, fields = stats.shape
    per_owner = pair_count // count
    assert per_owner * count == pair_count and per_owner * fields < 8 * head_dim
    pad = 8 * head_dim - per_owner * fields - 1
    slices = local_state.reshape(count, rows, head_dim)
    extra = jnp.concatenate(
        [
            stats.reshape(count, per_owner * fields),
            jnp.repeat(carry, count // head_count)[:, None],
            jnp.zeros((count, pad), jnp.float32),
        ],
        axis=1,
    ).reshape(count, 8, head_dim)
    got = lax.all_to_all(jnp.concatenate([slices, extra], axis=1), axis, 0, 0)
    got, passenger = lax.optimization_barrier((got, passenger))
    got_extra = got[:, rows:, :].reshape(count, 8 * head_dim)
    factors = got_extra[:, per_owner * fields]
    part = got_extra[:, : per_owner * fields].reshape(count, per_owner, fields)
    part_top = part[:, :, :head_count]
    top = jnp.max(part_top, axis=0)
    mass = jnp.sum(part[:, :, head_count:2 * head_count] * jnp.exp(part_top - top[None]), axis=0)
    tally = jnp.sum(part[:, :, 2 * head_count:], axis=0)
    combined = jnp.concatenate([top, mass, tally], axis=1).reshape(1, per_owner * fields)
    block = jnp.arange(count)
    inside = (block[None, None, :] > block[None, :, None]) & (block[None, None, :] < block[:, None, None])
    spans = jnp.prod(jnp.where(inside, factors[None, None, :], 1.0), axis=2)
    mix = jnp.where(block[None, :] < block[:, None], spans, 0.0)
    scanned = jnp.dot(
        mix, got[:, :rows, :].reshape(count, rows * head_dim), precision=lax.Precision.HIGHEST
    )
    back_extra = jnp.broadcast_to(
        jnp.concatenate([combined, jnp.zeros((1, pad + 1), jnp.float32)], axis=1),
        (count, 8 * head_dim),
    ).reshape(count, 8, head_dim)
    sent_back = jnp.concatenate([scanned.reshape(count, rows, head_dim), back_extra], axis=1)
    back = lax.all_to_all(sent_back, axis, 0, 0)
    state = back[:, :rows, :].reshape(head_count, head_dim, head_dim)
    totals = back[:, rows:, :].reshape(count, 8 * head_dim)[:, : per_owner * fields]
    return state, totals.reshape(pair_count, fields), passenger


def local(
    tokens,
    log_decay,
    lengths,
    label_ids,
    w_query,
    w_key,
    w_value,
    norm_gain,
    label_query,
    label_weight,
):
    tok_rows = tokens.shape[1]
    model_width = tokens.shape[2]
    head_count = log_decay.shape[1]
    head_dim = model_width // head_count
    qk_scale = head_dim ** (-0.5)
    record_count = lengths.shape[1]
    label_count = label_query.shape[0]
    shard_start = lax.axis_index("ctx") * tok_rows
    local_pos = jnp.arange(tok_rows, dtype=jnp.int32)
    record = record_ids(lengths[0], shard_start + local_pos)
    before_rec = record_ids(lengths[0], jnp.reshape(shard_start - 1, (1,)))[0]
    features = tokens[0]
    queries = jnp.dot(features, w_query, preferred_element_type=jnp.float32).astype(jnp.bfloat16)
    key_rows = jnp.dot(features, w_key, preferred_element_type=jnp.float32).astype(jnp.bfloat16)
    value_rows = jnp.dot(features, w_value, preferred_element_type=jnp.float32).astype(jnp.bfloat16)
    q3 = queries.reshape(tok_rows, head_count, head_dim)
    k3 = key_rows.reshape(tok_rows, head_count, head_dim)
    v3 = value_rows.reshape(tok_rows, head_count, head_dim)
    upper = (local_pos[:, None] <= local_pos[None, :]).astype(jnp.float32)
    decay_cum = jnp.dot(log_decay[0], upper, precision=lax.Precision.HIGHEST)
    pair_mask = (local_pos[:, None] >= local_pos[None, :]) & (record[:, None] == record[None, :])
    linked = record == before_rec
    tail_rec = record == record[tok_rows - 1]

    last_cum = decay_cum[:, tok_rows - 1]
    k_factor = jnp.where(tail_rec[None, :], jnp.exp(last_cum[:, None] - decay_cum), 0.0)
    k_decayed = (
        key_rows.astype(jnp.float32) * jnp.repeat(k_factor.T, head_dim, axis=1)
    ).astype(jnp.bfloat16)
    full_state = lax.dot_general(
        k_decayed, value_rows, (((0,), (0,)), ((), ())), preferred_element_type=jnp.float32
    )
    local_state = jnp.stack(
        [
            full_state[h * head_dim:(h + 1) * head_dim, h * head_dim:(h + 1) * head_dim]
            for h in range(head_count)
        ]
    )
    carry = jnp.where(linked[tok_rows - 1], jnp.exp(last_cum), 0.0)

    scores = jnp.einsum("thd,shd->hts", q3, k3, preferred_element_type=jnp.float32) * qk_scale
    decay_pair = jnp.exp(jnp.minimum(decay_cum[:, :, None] - decay_cum[:, None, :], 0.0))
    weights = jnp.where(pair_mask[None], scores * decay_pair, 0.0).astype(jnp.bfloat16)
    intra = jnp.einsum("hts,shd->thd", weights, v3, preferred_element_type=jnp.float32)

    member = record[None, :] == jnp.arange(record_count, dtype=jnp.int32)[:, None]
    kf3 = features.reshape(tok_rows, head_count, head_dim)
    lq3 = label_query.reshape(label_count, head_count, head_dim)
    lw3 = label_weight.reshape(label_count, head_count, head_dim)
    pscore = jnp.einsum("lhd,thd->hlt", lq3, kf3, preferred_element_type=jnp.float32) * qk_scale
    maxima = jnp.max(
        jnp.where(member[None, :, None, :], pscore[:, None, :, :], NEG_FILL), axis=3
    )
    maxima_tok = jnp.sum(
        jnp.where(member[None, :, None, :], maxima[:, :, :, None], 0.0), axis=1
    )
    pool_weight = jnp.exp(pscore - maxima_tok)
    mass = jnp.sum(jnp.where(member[None, :, None, :], pool_weight[:, None], 0.0), axis=3)
    label_hot = (label_ids[0][:, None] == jnp.arange(label_count, dtype=jnp.int32)[None, :]).astype(
        jnp.bfloat16
    )
    counts = jnp.dot(member.astype(jnp.bfloat16), label_hot, preferred_element_type=jnp.float32)

    stats = jnp.concatenate(
        [
            jnp.transpose(maxima, (1, 2, 0)),
            jnp.transpose(mass, (1, 2, 0)),
            counts[:, :, None],
        ],
        axis=2,
    ).reshape(record_count * label_count, 2 * head_count + 1)
    incoming, totals, intra = exclusive_state_scan(local_state, carry, stats, intra, "ctx")
    totals = totals.reshape(record_count, label_count, 2 * head_count + 1)
    top = jnp.transpose(totals[:, :, :head_count], (2, 0, 1))
    total_mass = jnp.transpose(totals[:, :, head_count:2 * head_count], (2, 0, 1))
    total_counts = totals[:, :, 2 * head_count]
    rescale = jnp.exp(maxima - top) / total_mass

    q_decayed = q3.astype(jnp.float32) * jnp.where(linked[None, :], jnp.exp(decay_cum), 0.0).T[:, :, None]
    inter = jnp.einsum(
        "thd,hde->the", q_decayed, incoming, precision=lax.Precision.HIGH,
        preferred_element_type=jnp.float32,
    )
    total_out = intra + inter * qk_scale
    centred = total_out - jnp.mean(total_out, axis=2, keepdims=True)
    variance = jnp.mean(centred * centred, axis=2, keepdims=True)
    gain3 = norm_gain.reshape(head_count, head_dim)
    normed = centred * lax.rsqrt(variance + 1e-05) * gain3[None]
    out_rows = normed.reshape(tok_rows, model_width).astype(jnp.bfloat16)

    y3 = out_rows.reshape(tok_rows, head_count, head_dim)
    label_value = jnp.einsum("lhd,thd->hlt", lw3, y3, preferred_element_type=jnp.float32)
    weighted = jnp.sum(
        jnp.where(member[None, :, None, :], (pool_weight * label_value)[:, None], 0.0), axis=3
    )
    part = jnp.sum(weighted * rescale, axis=0)
    count = lax.axis_size("ctx")
    assert count & (count - 1) == 0
    stride = 1
    for size in (4, 2, 2, 2):
        size = min(size, count // stride)
        if size > 1:
            part = group_sum(part, "ctx", stride, size)
            stride *= size
    assert stride == count
    logits = part
    target = (total_counts + 0.5) / (lengths[0].astype(jnp.float32)[:, None] + 1.0)
    rec_loss = jnp.mean(jax.nn.softplus(logits) - target * logits, axis=1)
    loss_sum = jnp.sum(rec_loss)
    for bit in butterfly_bits("dp"):
        loss_sum = loss_sum + swapped(loss_sum, "dp", bit)
    mean_loss = loss_sum / (lax.axis_size("dp") * record_count)
    return (out_rows[None], logits[None], rec_loss[None], mean_loss)


def solution(mesh):
    return jax.shard_map(
        local,
        mesh=mesh,
        in_specs=(
            P("dp", "ctx", None),
            P("dp", None, "ctx"),
            P("dp", None),
            P("dp", "ctx"),
            P(),
            P(),
            P(),
            P(),
            P(),
            P(),
        ),
        out_specs=(P("dp", "ctx", None), P("dp", None, None), P("dp", None), P()),
        check_vma=False,
    )
```

```python
import jax
import jax.numpy as jnp
from jax import lax
from jax.sharding import PartitionSpec as P

NEG_FILL = -1e30


def shifted(x, axis, by):
    count = lax.axis_size(axis)
    pairs = [(i, i + by) for i in range(count) if 0 <= i + by < count]
    return lax.ppermute(x, axis, pairs)


def swapped(x, axis, bit):
    count = lax.axis_size(axis)
    return lax.ppermute(x, axis, [(i, i ^ bit) for i in range(count)])


def group_sum(x, axis, stride, size):
    values = [x] + [swapped(x, axis, stride * d) for d in range(1, size)]
    while len(values) > 1:
        values = [values[i] + values[i + 1] for i in range(0, len(values), 2)]
    return values[0]


def butterfly_bits(axis):
    count = lax.axis_size(axis)
    assert count & (count - 1) == 0
    bits = []
    bit = 1
    while bit < count:
        bits.append(bit)
        bit *= 2
    return bits


def record_ids(length_row, positions):
    order = jnp.arange(length_row.shape[0])
    starts = jnp.sum(jnp.where(order[None, :] < order[:, None], length_row[None, :], 0), axis=1)
    return jnp.sum((starts[:, None] <= positions[None, :]).astype(jnp.int32), axis=0) - 1


def exclusive_state_scan(local_state, carry, stats, passenger, axis):
    head_count, head_dim, _ = local_state.shape
    count = lax.axis_size(axis)
    rows = head_count * head_dim // count
    assert rows * count == head_count * head_dim and head_dim % rows == 0
    pair_count, fields = stats.shape
    per_owner = pair_count // count
    assert per_owner * count == pair_count and per_owner * fields < 8 * head_dim
    pad = 8 * head_dim - per_owner * fields - 1
    slices = local_state.reshape(count, rows, head_dim)
    extra = jnp.concatenate(
        [
            stats.reshape(count, per_owner * fields),
            jnp.repeat(carry, count // head_count)[:, None],
            jnp.zeros((count, pad), jnp.float32),
        ],
        axis=1,
    ).reshape(count, 8, head_dim)
    got = lax.all_to_all(jnp.concatenate([slices, extra], axis=1), axis, 0, 0)
    got, passenger = lax.optimization_barrier((got, passenger))
    got_extra = got[:, rows:, :].reshape(count, 8 * head_dim)
    factors = got_extra[:, per_owner * fields]
    part = got_extra[:, : per_owner * fields].reshape(count, per_owner, fields)
    part_top = part[:, :, :head_count]
    top = jnp.max(part_top, axis=0)
    mass = jnp.sum(part[:, :, head_count:2 * head_count] * jnp.exp(part_top - top[None]), axis=0)
    tally = jnp.sum(part[:, :, 2 * head_count:], axis=0)
    combined = jnp.concatenate([top, mass, tally], axis=1).reshape(1, per_owner * fields)
    block = jnp.arange(count)
    inside = (block[None, None, :] > block[None, :, None]) & (block[None, None, :] < block[:, None, None])
    spans = jnp.prod(jnp.where(inside, factors[None, None, :], 1.0), axis=2)
    mix = jnp.where(block[None, :] < block[:, None], spans, 0.0)
    scanned = jnp.dot(
        mix, got[:, :rows, :].reshape(count, rows * head_dim), precision=lax.Precision.HIGHEST
    )
    back_extra = jnp.broadcast_to(
        jnp.concatenate([combined, jnp.zeros((1, pad + 1), jnp.float32)], axis=1),
        (count, 8 * head_dim),
    ).reshape(count, 8, head_dim)
    sent_back = jnp.concatenate([scanned.reshape(count, rows, head_dim), back_extra], axis=1)
    back = lax.all_to_all(sent_back, axis, 0, 0)
    state = back[:, :rows, :].reshape(head_count, head_dim, head_dim)
    totals = back[:, rows:, :].reshape(count, 8 * head_dim)[:, : per_owner * fields]
    return state, totals.reshape(pair_count, fields), passenger


def local(
    tokens,
    log_decay,
    lengths,
    label_ids,
    w_query,
    w_key,
    w_value,
    norm_gain,
    label_query,
    label_weight,
):
    tok_rows = tokens.shape[1]
    model_width = tokens.shape[2]
    head_count = log_decay.shape[1]
    head_dim = model_width // head_count
    qk_scale = head_dim ** (-0.5)
    record_count = lengths.shape[1]
    label_count = label_query.shape[0]
    shard_start = lax.axis_index("ctx") * tok_rows
    local_pos = jnp.arange(tok_rows, dtype=jnp.int32)
    record = record_ids(lengths[0], shard_start + local_pos)
    before_rec = record_ids(lengths[0], jnp.reshape(shard_start - 1, (1,)))[0]
    features = tokens[0]
    queries = jnp.dot(features, w_query, preferred_element_type=jnp.float32).astype(jnp.bfloat16)
    key_rows = jnp.dot(features, w_key, preferred_element_type=jnp.float32).astype(jnp.bfloat16)
    value_rows = jnp.dot(features, w_value, preferred_element_type=jnp.float32).astype(jnp.bfloat16)
    q3 = queries.reshape(tok_rows, head_count, head_dim)
    k3 = key_rows.reshape(tok_rows, head_count, head_dim)
    v3 = value_rows.reshape(tok_rows, head_count, head_dim)
    upper = (local_pos[:, None] <= local_pos[None, :]).astype(jnp.float32)
    decay_cum = jnp.dot(log_decay[0], upper, precision=lax.Precision.HIGHEST)
    pair_mask = (local_pos[:, None] >= local_pos[None, :]) & (record[:, None] == record[None, :])
    linked = record == before_rec
    tail_rec = record == record[tok_rows - 1]

    last_cum = decay_cum[:, tok_rows - 1]
    k_factor = jnp.where(tail_rec[None, :], jnp.exp(last_cum[:, None] - decay_cum), 0.0)
    k_decayed = (
        key_rows.astype(jnp.float32) * jnp.repeat(k_factor.T, head_dim, axis=1)
    ).astype(jnp.bfloat16)
    full_state = lax.dot_general(
        k_decayed, value_rows, (((0,), (0,)), ((), ())), preferred_element_type=jnp.float32
    )
    local_state = jnp.stack(
        [
            full_state[h * head_dim:(h + 1) * head_dim, h * head_dim:(h + 1) * head_dim]
            for h in range(head_count)
        ]
    )
    carry = jnp.where(linked[tok_rows - 1], jnp.exp(last_cum), 0.0)

    scores = jnp.einsum("thd,shd->hts", q3, k3, preferred_element_type=jnp.float32) * qk_scale
    decay_pair = jnp.exp(jnp.minimum(decay_cum[:, :, None] - decay_cum[:, None, :], 0.0))
    weights = jnp.where(pair_mask[None], scores * decay_pair, 0.0).astype(jnp.bfloat16)
    intra = jnp.einsum("hts,shd->thd", weights, v3, preferred_element_type=jnp.float32)

    member = record[None, :] == jnp.arange(record_count, dtype=jnp.int32)[:, None]
    kf3 = features.reshape(tok_rows, head_count, head_dim)
    lq3 = label_query.reshape(label_count, head_count, head_dim)
    lw3 = label_weight.reshape(label_count, head_count, head_dim)
    pscore = jnp.einsum("lhd,thd->hlt", lq3, kf3, preferred_element_type=jnp.float32) * qk_scale
    maxima = jnp.max(
        jnp.where(member[None, :, None, :], pscore[:, None, :, :], NEG_FILL), axis=3
    )
    maxima_tok = jnp.sum(
        jnp.where(member[None, :, None, :], maxima[:, :, :, None], 0.0), axis=1
    )
    pool_weight = jnp.exp(pscore - maxima_tok)
    mass = jnp.sum(jnp.where(member[None, :, None, :], pool_weight[:, None], 0.0), axis=3)
    label_hot = (label_ids[0][:, None] == jnp.arange(label_count, dtype=jnp.int32)[None, :]).astype(
        jnp.bfloat16
    )
    counts = jnp.dot(member.astype(jnp.bfloat16), label_hot, preferred_element_type=jnp.float32)

    stats = jnp.concatenate(
        [
            jnp.transpose(maxima, (1, 2, 0)),
            jnp.transpose(mass, (1, 2, 0)),
        ],
        axis=2,
    ).reshape(record_count * label_count, 2 * head_count)
    incoming, totals, intra = exclusive_state_scan(local_state, carry, stats, intra, "ctx")
    totals = totals.reshape(record_count, label_count, 2 * head_count)
    top = jnp.transpose(totals[:, :, :head_count], (2, 0, 1))
    total_mass = jnp.transpose(totals[:, :, head_count:2 * head_count], (2, 0, 1))
    rescale = jnp.exp(maxima - top) / total_mass

    q_decayed = q3.astype(jnp.float32) * jnp.where(linked[None, :], jnp.exp(decay_cum), 0.0).T[:, :, None]
    inter = jnp.einsum(
        "thd,hde->the", q_decayed, incoming, precision=lax.Precision.HIGH,
        preferred_element_type=jnp.float32,
    )
    total_out = intra + inter * qk_scale
    centred = total_out - jnp.mean(total_out, axis=2, keepdims=True)
    variance = jnp.mean(centred * centred, axis=2, keepdims=True)
    gain3 = norm_gain.reshape(head_count, head_dim)
    normed = centred * lax.rsqrt(variance + 1e-05) * gain3[None]
    out_rows = normed.reshape(tok_rows, model_width).astype(jnp.bfloat16)

    y3 = out_rows.reshape(tok_rows, head_count, head_dim)
    label_value = jnp.einsum("lhd,thd->hlt", lw3, y3, preferred_element_type=jnp.float32)
    weighted = jnp.sum(
        jnp.where(member[None, :, None, :], (pool_weight * label_value)[:, None], 0.0), axis=3
    )
    part = jnp.stack([jnp.sum(weighted * rescale, axis=0), counts])
    count = lax.axis_size("ctx")
    assert count & (count - 1) == 0
    stride = 1
    for size in (4, 2, 4):
        size = min(size, count // stride)
        if size > 1:
            part = group_sum(part, "ctx", stride, size)
            stride *= size
    assert stride == count
    logits = part[0]
    total_counts = part[1]
    target = (total_counts + 0.5) / (lengths[0].astype(jnp.float32)[:, None] + 1.0)
    rec_loss = jnp.mean(jax.nn.softplus(logits) - target * logits, axis=1)
    loss_sum = jnp.sum(rec_loss)
    for bit in butterfly_bits("dp"):
        loss_sum = loss_sum + swapped(loss_sum, "dp", bit)
    mean_loss = loss_sum / (lax.axis_size("dp") * record_count)
    return (out_rows[None], logits[None], rec_loss[None], mean_loss)


def solution(mesh):
    return jax.shard_map(
        local,
        mesh=mesh,
        in_specs=(
            P("dp", "ctx", None),
            P("dp", None, "ctx"),
            P("dp", None),
            P("dp", "ctx"),
            P(),
            P(),
            P(),
            P(),
            P(),
            P(),
        ),
        out_specs=(P("dp", "ctx", None), P("dp", None, None), P("dp", None), P()),
        check_vma=False,
    )
```

```python
import jax
import jax.numpy as jnp
from jax import lax
from jax.sharding import PartitionSpec as P

NEG_FILL = -1e30


def shifted(x, axis, by):
    count = lax.axis_size(axis)
    pairs = [(i, i + by) for i in range(count) if 0 <= i + by < count]
    return lax.ppermute(x, axis, pairs)


def swapped(x, axis, bit):
    count = lax.axis_size(axis)
    return lax.ppermute(x, axis, [(i, i ^ bit) for i in range(count)])


def group_sum(x, axis, stride, size):
    values = [x] + [swapped(x, axis, stride * d) for d in range(1, size)]
    while len(values) > 1:
        values = [values[i] + values[i + 1] for i in range(0, len(values), 2)]
    return values[0]


def butterfly_bits(axis):
    count = lax.axis_size(axis)
    assert count & (count - 1) == 0
    bits = []
    bit = 1
    while bit < count:
        bits.append(bit)
        bit *= 2
    return bits


def record_ids(length_row, positions):
    order = jnp.arange(length_row.shape[0])
    starts = jnp.sum(jnp.where(order[None, :] < order[:, None], length_row[None, :], 0), axis=1)
    return jnp.sum((starts[:, None] <= positions[None, :]).astype(jnp.int32), axis=0) - 1


def exclusive_state_scan(local_state, carry, stats, passenger, axis):
    head_count, head_dim, _ = local_state.shape
    count = lax.axis_size(axis)
    rows = head_count * head_dim // count
    assert rows * count == head_count * head_dim and head_dim % rows == 0
    pair_count, fields = stats.shape
    per_owner = pair_count // count
    assert per_owner * count == pair_count and per_owner * fields < 8 * head_dim
    pad = 8 * head_dim - per_owner * fields - 1
    slices = local_state.reshape(count, rows, head_dim)
    extra = jnp.concatenate(
        [
            stats.reshape(count, per_owner * fields),
            jnp.repeat(carry, count // head_count)[:, None],
            jnp.zeros((count, pad), jnp.float32),
        ],
        axis=1,
    ).reshape(count, 8, head_dim)
    got = lax.all_to_all(jnp.concatenate([slices, extra], axis=1), axis, 0, 0)
    got, passenger = lax.optimization_barrier((got, passenger))
    got_extra = got[:, rows:, :].reshape(count, 8 * head_dim)
    factors = got_extra[:, per_owner * fields]
    part = got_extra[:, : per_owner * fields].reshape(count, per_owner, fields)
    part_top = part[:, :, :head_count]
    top = jnp.max(part_top, axis=0)
    mass = jnp.sum(part[:, :, head_count:2 * head_count] * jnp.exp(part_top - top[None]), axis=0)
    tally = jnp.sum(part[:, :, 2 * head_count:], axis=0)
    combined = jnp.concatenate([top, mass, tally], axis=1).reshape(1, per_owner * fields)
    block = jnp.arange(count)
    inside = (block[None, None, :] > block[None, :, None]) & (block[None, None, :] < block[:, None, None])
    spans = jnp.prod(jnp.where(inside, factors[None, None, :], 1.0), axis=2)
    mix = jnp.where(block[None, :] < block[:, None], spans, 0.0)
    scanned = jnp.dot(
        mix, got[:, :rows, :].reshape(count, rows * head_dim), precision=lax.Precision.HIGH
    )
    back_extra = jnp.broadcast_to(
        jnp.concatenate([combined, jnp.zeros((1, pad + 1), jnp.float32)], axis=1),
        (count, 8 * head_dim),
    ).reshape(count, 8, head_dim)
    sent_back = jnp.concatenate([scanned.reshape(count, rows, head_dim), back_extra], axis=1)
    back = lax.all_to_all(sent_back, axis, 0, 0)
    state = back[:, :rows, :].reshape(head_count, head_dim, head_dim)
    totals = back[:, rows:, :].reshape(count, 8 * head_dim)[:, : per_owner * fields]
    return state, totals.reshape(pair_count, fields), passenger


def local(
    tokens,
    log_decay,
    lengths,
    label_ids,
    w_query,
    w_key,
    w_value,
    norm_gain,
    label_query,
    label_weight,
):
    tok_rows = tokens.shape[1]
    model_width = tokens.shape[2]
    head_count = log_decay.shape[1]
    head_dim = model_width // head_count
    qk_scale = head_dim ** (-0.5)
    record_count = lengths.shape[1]
    label_count = label_query.shape[0]
    shard_start = lax.axis_index("ctx") * tok_rows
    local_pos = jnp.arange(tok_rows, dtype=jnp.int32)
    record = record_ids(lengths[0], shard_start + local_pos)
    before_rec = record_ids(lengths[0], jnp.reshape(shard_start - 1, (1,)))[0]
    features = tokens[0]
    queries = jnp.dot(features, w_query, preferred_element_type=jnp.float32).astype(jnp.bfloat16)
    key_rows = jnp.dot(features, w_key, preferred_element_type=jnp.float32).astype(jnp.bfloat16)
    value_rows = jnp.dot(features, w_value, preferred_element_type=jnp.float32).astype(jnp.bfloat16)
    q3 = queries.reshape(tok_rows, head_count, head_dim)
    k3 = key_rows.reshape(tok_rows, head_count, head_dim)
    v3 = value_rows.reshape(tok_rows, head_count, head_dim)
    upper = (local_pos[:, None] <= local_pos[None, :]).astype(jnp.float32)
    decay_cum = jnp.dot(log_decay[0], upper, precision=lax.Precision.HIGHEST)
    pair_mask = (local_pos[:, None] >= local_pos[None, :]) & (record[:, None] == record[None, :])
    linked = record == before_rec
    tail_rec = record == record[tok_rows - 1]

    last_cum = decay_cum[:, tok_rows - 1]
    k_factor = jnp.where(tail_rec[None, :], jnp.exp(last_cum[:, None] - decay_cum), 0.0)
    k_decayed = (
        key_rows.astype(jnp.float32) * jnp.repeat(k_factor.T, head_dim, axis=1)
    ).astype(jnp.bfloat16)
    full_state = lax.dot_general(
        k_decayed, value_rows, (((0,), (0,)), ((), ())), preferred_element_type=jnp.float32
    )
    local_state = jnp.stack(
        [
            full_state[h * head_dim:(h + 1) * head_dim, h * head_dim:(h + 1) * head_dim]
            for h in range(head_count)
        ]
    )
    carry = jnp.where(linked[tok_rows - 1], jnp.exp(last_cum), 0.0)

    scores = jnp.einsum("thd,shd->hts", q3, k3, preferred_element_type=jnp.float32) * qk_scale
    decay_pair = jnp.exp(jnp.minimum(decay_cum[:, :, None] - decay_cum[:, None, :], 0.0))
    weights = jnp.where(pair_mask[None], scores * decay_pair, 0.0).astype(jnp.bfloat16)
    intra = jnp.einsum("hts,shd->thd", weights, v3, preferred_element_type=jnp.float32)

    member = record[None, :] == jnp.arange(record_count, dtype=jnp.int32)[:, None]
    kf3 = features.reshape(tok_rows, head_count, head_dim)
    lq3 = label_query.reshape(label_count, head_count, head_dim)
    lw3 = label_weight.reshape(label_count, head_count, head_dim)
    pscore = jnp.einsum("lhd,thd->hlt", lq3, kf3, preferred_element_type=jnp.float32) * qk_scale
    maxima = jnp.max(
        jnp.where(member[None, :, None, :], pscore[:, None, :, :], NEG_FILL), axis=3
    )
    maxima_tok = jnp.sum(
        jnp.where(member[None, :, None, :], maxima[:, :, :, None], 0.0), axis=1
    )
    pool_weight = jnp.exp(pscore - maxima_tok)
    mass = jnp.sum(jnp.where(member[None, :, None, :], pool_weight[:, None], 0.0), axis=3)
    label_hot = (label_ids[0][:, None] == jnp.arange(label_count, dtype=jnp.int32)[None, :]).astype(
        jnp.bfloat16
    )
    counts = jnp.dot(member.astype(jnp.bfloat16), label_hot, preferred_element_type=jnp.float32)

    stats = jnp.concatenate(
        [
            jnp.transpose(maxima, (1, 2, 0)),
            jnp.transpose(mass, (1, 2, 0)),
            counts[:, :, None],
        ],
        axis=2,
    ).reshape(record_count * label_count, 2 * head_count + 1)
    incoming, totals, intra = exclusive_state_scan(local_state, carry, stats, intra, "ctx")
    totals = totals.reshape(record_count, label_count, 2 * head_count + 1)
    top = jnp.transpose(totals[:, :, :head_count], (2, 0, 1))
    total_mass = jnp.transpose(totals[:, :, head_count:2 * head_count], (2, 0, 1))
    total_counts = totals[:, :, 2 * head_count]
    rescale = jnp.exp(maxima - top) / total_mass

    q_decayed = q3.astype(jnp.float32) * jnp.where(linked[None, :], jnp.exp(decay_cum), 0.0).T[:, :, None]
    inter = jnp.einsum(
        "thd,hde->the", q_decayed, incoming, precision=lax.Precision.HIGH,
        preferred_element_type=jnp.float32,
    )
    total_out = intra + inter * qk_scale
    centred = total_out - jnp.mean(total_out, axis=2, keepdims=True)
    variance = jnp.mean(centred * centred, axis=2, keepdims=True)
    gain3 = norm_gain.reshape(head_count, head_dim)
    normed = centred * lax.rsqrt(variance + 1e-05) * gain3[None]
    out_rows = normed.reshape(tok_rows, model_width).astype(jnp.bfloat16)

    y3 = out_rows.reshape(tok_rows, head_count, head_dim)
    label_value = jnp.einsum("lhd,thd->hlt", lw3, y3, preferred_element_type=jnp.float32)
    weighted = jnp.sum(
        jnp.where(member[None, :, None, :], (pool_weight * label_value)[:, None], 0.0), axis=3
    )
    part = jnp.sum(weighted * rescale, axis=0)
    count = lax.axis_size("ctx")
    assert count & (count - 1) == 0
    stride = 1
    for size in (4, 2, 4):
        size = min(size, count // stride)
        if size > 1:
            part = group_sum(part, "ctx", stride, size)
            stride *= size
    assert stride == count
    logits = part
    target = (total_counts + 0.5) / (lengths[0].astype(jnp.float32)[:, None] + 1.0)
    rec_loss = jnp.mean(jax.nn.softplus(logits) - target * logits, axis=1)
    loss_sum = jnp.sum(rec_loss)
    for bit in butterfly_bits("dp"):
        loss_sum = loss_sum + swapped(loss_sum, "dp", bit)
    mean_loss = loss_sum / (lax.axis_size("dp") * record_count)
    return (out_rows[None], logits[None], rec_loss[None], mean_loss)


def solution(mesh):
    return jax.shard_map(
        local,
        mesh=mesh,
        in_specs=(
            P("dp", "ctx", None),
            P("dp", None, "ctx"),
            P("dp", None),
            P("dp", "ctx"),
            P(),
            P(),
            P(),
            P(),
            P(),
            P(),
        ),
        out_specs=(P("dp", "ctx", None), P("dp", None, None), P("dp", None), P()),
        check_vma=False,
    )
```

```python
import jax
import jax.numpy as jnp
from jax import lax
from jax.sharding import PartitionSpec as P

NEG_FILL = -1e30


def shifted(x, axis, by):
    count = lax.axis_size(axis)
    pairs = [(i, i + by) for i in range(count) if 0 <= i + by < count]
    return lax.ppermute(x, axis, pairs)


def swapped(x, axis, bit):
    count = lax.axis_size(axis)
    return lax.ppermute(x, axis, [(i, i ^ bit) for i in range(count)])


def group_sum(x, axis, stride, size):
    values = [x] + [swapped(x, axis, stride * d) for d in range(1, size)]
    while len(values) > 1:
        values = [values[i] + values[i + 1] for i in range(0, len(values), 2)]
    return values[0]


def butterfly_bits(axis):
    count = lax.axis_size(axis)
    assert count & (count - 1) == 0
    bits = []
    bit = 1
    while bit < count:
        bits.append(bit)
        bit *= 2
    return bits


def record_ids(length_row, positions):
    order = jnp.arange(length_row.shape[0])
    starts = jnp.sum(jnp.where(order[None, :] < order[:, None], length_row[None, :], 0), axis=1)
    return jnp.sum((starts[:, None] <= positions[None, :]).astype(jnp.int32), axis=0) - 1


def exclusive_state_scan(local_state, carry, stats, passenger, axis):
    head_count, head_dim, _ = local_state.shape
    count = lax.axis_size(axis)
    rows = head_count * head_dim // count
    assert rows * count == head_count * head_dim and head_dim % rows == 0
    pair_count, fields = stats.shape
    per_owner = pair_count // count
    assert per_owner * count == pair_count and per_owner * fields < 8 * head_dim
    pad = 8 * head_dim - per_owner * fields - 1
    slices = local_state.reshape(count, rows, head_dim)
    extra = jnp.concatenate(
        [
            stats.reshape(count, per_owner * fields),
            jnp.repeat(carry, count // head_count)[:, None],
            jnp.zeros((count, pad), jnp.float32),
        ],
        axis=1,
    ).reshape(count, 8, head_dim)
    got = lax.all_to_all(jnp.concatenate([slices, extra], axis=1), axis, 0, 0)
    got, passenger = lax.optimization_barrier((got, passenger))
    got_extra = got[:, rows:, :].reshape(count, 8 * head_dim)
    factors = got_extra[:, per_owner * fields]
    part = got_extra[:, : per_owner * fields].reshape(count, per_owner, fields)
    part_top = part[:, :, :head_count]
    top = jnp.max(part_top, axis=0)
    mass = jnp.sum(part[:, :, head_count:2 * head_count] * jnp.exp(part_top - top[None]), axis=0)
    tally = jnp.sum(part[:, :, 2 * head_count:], axis=0)
    combined = jnp.concatenate([top, mass, tally], axis=1).reshape(1, per_owner * fields)
    block = jnp.arange(count)
    inside = (block[None, None, :] > block[None, :, None]) & (block[None, None, :] < block[:, None, None])
    spans = jnp.prod(jnp.where(inside, factors[None, None, :], 1.0), axis=2)
    mix = jnp.where(block[None, :] < block[:, None], spans, 0.0)
    scanned = jnp.dot(
        mix, got[:, :rows, :].reshape(count, rows * head_dim), precision=lax.Precision.HIGH
    )
    back_extra = jnp.broadcast_to(
        jnp.concatenate([combined, jnp.zeros((1, pad + 1), jnp.float32)], axis=1),
        (count, 8 * head_dim),
    ).reshape(count, 8, head_dim)
    sent_back = jnp.concatenate([scanned.reshape(count, rows, head_dim), back_extra], axis=1)
    back = lax.all_to_all(sent_back, axis, 0, 0)
    state = back[:, :rows, :].reshape(head_count, head_dim, head_dim)
    totals = back[:, rows:, :].reshape(count, 8 * head_dim)[:, : per_owner * fields]
    return state, totals.reshape(pair_count, fields), passenger


def local(
    tokens,
    log_decay,
    lengths,
    label_ids,
    w_query,
    w_key,
    w_value,
    norm_gain,
    label_query,
    label_weight,
):
    tok_rows = tokens.shape[1]
    model_width = tokens.shape[2]
    head_count = log_decay.shape[1]
    head_dim = model_width // head_count
    qk_scale = head_dim ** (-0.5)
    record_count = lengths.shape[1]
    label_count = label_query.shape[0]
    shard_start = lax.axis_index("ctx") * tok_rows
    local_pos = jnp.arange(tok_rows, dtype=jnp.int32)
    record = record_ids(lengths[0], shard_start + local_pos)
    before_rec = record_ids(lengths[0], jnp.reshape(shard_start - 1, (1,)))[0]
    features = tokens[0]
    queries = jnp.dot(features, w_query, preferred_element_type=jnp.float32).astype(jnp.bfloat16)
    key_rows = jnp.dot(features, w_key, preferred_element_type=jnp.float32).astype(jnp.bfloat16)
    value_rows = jnp.dot(features, w_value, preferred_element_type=jnp.float32).astype(jnp.bfloat16)
    q3 = queries.reshape(tok_rows, head_count, head_dim)
    k3 = key_rows.reshape(tok_rows, head_count, head_dim)
    v3 = value_rows.reshape(tok_rows, head_count, head_dim)
    upper = (local_pos[:, None] <= local_pos[None, :]).astype(jnp.float32)
    decay_cum = jnp.dot(log_decay[0], upper, precision=lax.Precision.HIGHEST)
    pair_mask = (local_pos[:, None] >= local_pos[None, :]) & (record[:, None] == record[None, :])
    linked = record == before_rec
    tail_rec = record == record[tok_rows - 1]

    last_cum = decay_cum[:, tok_rows - 1]
    k_factor = jnp.where(tail_rec[None, :], jnp.exp(last_cum[:, None] - decay_cum), 0.0)
    k_decayed = (
        key_rows.astype(jnp.float32) * jnp.repeat(k_factor.T, head_dim, axis=1)
    ).astype(jnp.bfloat16)
    full_state = lax.dot_general(
        k_decayed, value_rows, (((0,), (0,)), ((), ())), preferred_element_type=jnp.float32
    )
    local_state = jnp.stack(
        [
            full_state[h * head_dim:(h + 1) * head_dim, h * head_dim:(h + 1) * head_dim]
            for h in range(head_count)
        ]
    )
    carry = jnp.where(linked[tok_rows - 1], jnp.exp(last_cum), 0.0)

    scores = jnp.einsum("thd,shd->hts", q3, k3, preferred_element_type=jnp.float32) * qk_scale
    decay_pair = jnp.exp(jnp.minimum(decay_cum[:, :, None] - decay_cum[:, None, :], 0.0))
    weights = jnp.where(pair_mask[None], scores * decay_pair, 0.0).astype(jnp.bfloat16)
    intra = jnp.einsum("hts,shd->thd", weights, v3, preferred_element_type=jnp.float32)

    member = record[None, :] == jnp.arange(record_count, dtype=jnp.int32)[:, None]
    kf3 = features.reshape(tok_rows, head_count, head_dim)
    lq3 = label_query.reshape(label_count, head_count, head_dim)
    lw3 = label_weight.reshape(label_count, head_count, head_dim)
    pscore = jnp.einsum("lhd,thd->hlt", lq3, kf3, preferred_element_type=jnp.float32) * qk_scale
    maxima = jnp.max(
        jnp.where(member[None, :, None, :], pscore[:, None, :, :], NEG_FILL), axis=3
    )
    maxima_tok = maxima[:, record_count - 1, :, None]
    for r in range(record_count - 2, -1, -1):
        maxima_tok = jnp.where(record[None, None, :] == r, maxima[:, r, :, None], maxima_tok)
    pool_weight = jnp.exp(pscore - maxima_tok)
    mass = jnp.sum(jnp.where(member[None, :, None, :], pool_weight[:, None], 0.0), axis=3)
    label_hot = (label_ids[0][:, None] == jnp.arange(label_count, dtype=jnp.int32)[None, :]).astype(
        jnp.bfloat16
    )
    counts = jnp.dot(member.astype(jnp.bfloat16), label_hot, preferred_element_type=jnp.float32)

    stats = jnp.concatenate(
        [
            jnp.transpose(maxima, (1, 2, 0)),
            jnp.transpose(mass, (1, 2, 0)),
            counts[:, :, None],
        ],
        axis=2,
    ).reshape(record_count * label_count, 2 * head_count + 1)
    incoming, totals, intra = exclusive_state_scan(local_state, carry, stats, intra, "ctx")
    totals = totals.reshape(record_count, label_count, 2 * head_count + 1)
    top = jnp.transpose(totals[:, :, :head_count], (2, 0, 1))
    total_mass = jnp.transpose(totals[:, :, head_count:2 * head_count], (2, 0, 1))
    total_counts = totals[:, :, 2 * head_count]
    rescale = jnp.exp(maxima - top) / total_mass

    q_decayed = q3.astype(jnp.float32) * jnp.where(linked[None, :], jnp.exp(decay_cum), 0.0).T[:, :, None]
    inter = jnp.einsum(
        "thd,hde->the", q_decayed, incoming, precision=lax.Precision.HIGH,
        preferred_element_type=jnp.float32,
    )
    total_out = intra + inter * qk_scale
    centred = total_out - jnp.mean(total_out, axis=2, keepdims=True)
    variance = jnp.mean(centred * centred, axis=2, keepdims=True)
    gain3 = norm_gain.reshape(head_count, head_dim)
    normed = centred * lax.rsqrt(variance + 1e-05) * gain3[None]
    out_rows = normed.reshape(tok_rows, model_width).astype(jnp.bfloat16)

    y3 = out_rows.reshape(tok_rows, head_count, head_dim)
    label_value = jnp.einsum("lhd,thd->hlt", lw3, y3, preferred_element_type=jnp.float32)
    weighted = jnp.sum(
        jnp.where(member[None, :, None, :], (pool_weight * label_value)[:, None], 0.0), axis=3
    )
    part = jnp.sum(weighted * rescale, axis=0)
    count = lax.axis_size("ctx")
    assert count & (count - 1) == 0
    stride = 1
    for size in (4, 2, 4):
        size = min(size, count // stride)
        if size > 1:
            part = group_sum(part, "ctx", stride, size)
            stride *= size
    assert stride == count
    logits = part
    target = (total_counts + 0.5) / (lengths[0].astype(jnp.float32)[:, None] + 1.0)
    rec_loss = jnp.mean(jax.nn.softplus(logits) - target * logits, axis=1)
    loss_sum = jnp.sum(rec_loss)
    for bit in butterfly_bits("dp"):
        loss_sum = loss_sum + swapped(loss_sum, "dp", bit)
    mean_loss = loss_sum / (lax.axis_size("dp") * record_count)
    return (out_rows[None], logits[None], rec_loss[None], mean_loss)


def solution(mesh):
    return jax.shard_map(
        local,
        mesh=mesh,
        in_specs=(
            P("dp", "ctx", None),
            P("dp", None, "ctx"),
            P("dp", None),
            P("dp", "ctx"),
            P(),
            P(),
            P(),
            P(),
            P(),
            P(),
        ),
        out_specs=(P("dp", "ctx", None), P("dp", None, None), P("dp", None), P()),
        check_vma=False,
    )
```
